32 devices in a mesh: gx: 4 (over z), gy: 8 (over y, x, core).
Axes of the slice: x: 2, y: 2, z: 4, core: 2. Of those that a mesh axis runs over, the one named last changes fastest.
Arguments:
- adjoint: float32 [3, 66, 131072], P(None, None, ('gx', 'gy')), may hold values from -6 to 6
- deriv_r: float32 [66, 66], replicated, may hold values from -0.75 to 0.75
- deriv_s: float32 [66, 66], replicated, may hold values from -0.75 to 0.75
- lift: float32 [66, 33], replicated, may hold values from -0.75 to 0.75
- metric: float32 [4, 131072], P(None, ('gx', 'gy')), may hold values from -1.5 to 1.5
- face_scale: float32 [3, 131072], P(None, ('gx', 'gy')), may hold values from 0.5 to 4
- face_angle: float32 [3, 131072], P(None, ('gx', 'gy')), may hold values from -3.140625 to 3.140625
- neighbours: int32 [3, 131072], P(None, ('gx', 'gy')), may hold values from 0 to 131071, as said below
- neighbour_face: int32 [3, 131072], P(None, ('gx', 'gy')), may hold values from 0 to 2, as said below
- remap_table: float32 [16, 66, 66], replicated, may hold values from -0.75 to 0.75
- intersection_elem: int32 [262144], P(('gx', 'gy')), may hold values from 0 to 4095
- intersection_old: int32 [262144], P(('gx', 'gy')), may hold values from -1 to 2047, as said below
- intersection_weight: float32 [262144], P(('gx', 'gy')), may hold values from 0.05 to 1
- block_type: int32 [2048], P(('gx', 'gy')), may hold values from 0 to 15
Outputs:
- adj_new: float32 [3, 66, 131072], P(None, None, ('gx', 'gy'))
- adj_old: float32 [3, 66, 65536], P(None, None, ('gx', 'gy'))
The draws below stay inside these ranges and needn't reach their ends.
Inputs may be any that keep to these rules, and one draw needn't show every extreme that they name: `neighbours`: the face relation is symmetric: the element across face g of e has e across face neighbour_face[g, e]; the element across lies fewer than 32 positions from e in the slab's element order, counted cyclically. `neighbour_face`: faces are numbered 0, 1, 2. `intersection_old`: -1 marks a padded row; in every draw some devices have all their rows live, and some owner receives full groups from every device within 4 of it. `intersection_elem`: index of the new element on the device that holds the row.
All inputs are finite; a program needn't handle non-finite values.
Results may differ from the reference program's by a relative error of at most 0.00007.
Values sent between devices are 32-bit elements; how exact they have to be, the bound alone decides.
No kernel may reach another device: no remote copies, remote signals or barrier semaphores. Data moves between devices by JAX's collectives and lax.ppermute only.
A program may use at most 192 MiB of HBM per device.

```python
import math
import jax
import jax.numpy as jnp
import numpy as np
from jax import lax

ORDER = 10
NP = 66
NFP = 11
E_DEV = 4096
ELEMENTS = 131072
E_OLD_DEV = 2048
OLD_ELEMENTS = 65536
Q_DEV = 8192
Q_TOTAL = 262144
REACH = 4
BLOCK = 128
BLK_TOTAL = 2048
NTYPE = 16
RIM = 32
N_GX = 4
N_GY = 8


def shuffle_block(block_key):
    return jax.random.permutation(block_key, RIM)


def neighbour_pairs(key):
    orders = jnp.array([[0, 1, 2], [0, 2, 1], [1, 0, 2], [1, 2, 0], [2, 0, 1], [2, 1, 0]], jnp.int32)
    elem_ids = jnp.arange(ELEMENTS, dtype=jnp.int32)
    picks = jax.random.randint(jax.random.fold_in(key, 0), (ELEMENTS,), 0, 6)
    labels = orders[picks]
    across = jnp.zeros((3, ELEMENTS), jnp.int32)
    facing = jnp.zeros((3, ELEMENTS), jnp.int32)
    block_count = ELEMENTS // RIM
    block_ids = jnp.arange(block_count, dtype=jnp.int32)[:, None]
    within = jnp.arange(RIM, dtype=jnp.int32)[None, :]
    for round_id in range(3):
        shift_by = (round_id + 1) * RIM // 4
        block_keys = jax.random.split(jax.random.fold_in(key, round_id + 1), block_count)
        mixed = jax.vmap(shuffle_block)(block_keys).astype(jnp.int32)
        first_half = mixed[:, 0::2]
        second_half = mixed[:, 1::2]
        partner_local = jnp.zeros((block_count, RIM), jnp.int32)
        partner_local = partner_local.at[block_ids, first_half].set(second_half)
        partner_local = partner_local.at[block_ids, second_half].set(first_half)
        positions = (block_ids * RIM + within + shift_by) % ELEMENTS
        partner_pos = (block_ids * RIM + partner_local + shift_by) % ELEMENTS
        partner = jnp.zeros((ELEMENTS,), jnp.int32).at[positions.reshape(-1)].set(partner_pos.reshape(-1))
        used_face = labels[:, round_id]
        across = across.at[used_face, elem_ids].set(partner)
        facing = facing.at[used_face, elem_ids].set(labels[partner, round_id])
    return (across, facing)


def draw_neighbours(key, part):
    return neighbour_pairs(jax.random.fold_in(key, 7))[0]


def draw_neighbour_face(key, part):
    return neighbour_pairs(jax.random.fold_in(key, 7))[1]


def draw_intersection_old(key, part):
    owners = N_GX * N_GY
    row_ids = jnp.arange(Q_TOTAL, dtype=jnp.int32)
    sender = row_ids // Q_DEV
    levels = jnp.array([2, 4, 7, 10], jnp.int32)
    sender_heat = levels[jax.random.randint(jax.random.fold_in(key, 1), (owners,), 0, 4)]
    hot_start = jax.random.randint(jax.random.fold_in(key, 2), (), 0, owners)
    device_ids = jnp.arange(owners, dtype=jnp.int32)
    in_hot = (device_ids - hot_start + owners) % owners < 2 * REACH + 1
    sender_heat = jnp.where(in_hot, 10, sender_heat)
    is_live = jax.random.randint(jax.random.fold_in(key, 3), (Q_TOTAL,), 0, 10) < sender_heat[sender]
    old_index = jax.random.randint(jax.random.fold_in(key, 4), (Q_TOTAL,), 0, E_OLD_DEV)
    return jnp.where(is_live, old_index, -1).astype(jnp.int32)


def plant(drawn, rng, smallest, top_value):
    longest = drawn.shape.index(max(drawn.shape))
    spots = []
    for shift in (0, 1):
        where = [jax.random.randint(jax.random.fold_in(rng, axis), (), 0, length) for axis, length in enumerate(drawn.shape)]
        where[longest] = (where[longest] + shift) % drawn.shape[longest]
        spots.append(tuple(where))
    return drawn.at[spots[0]].set(smallest).at[spots[1]].set(top_value)


def shard_levels(key, extent, pieces, low, largest):
    def one(axis_at, parts):
        draws = jax.random.uniform(jax.random.fold_in(jax.random.fold_in(key, 6), axis_at), (parts,), jnp.float32, low / len(pieces), largest / len(pieces))
        return jnp.repeat(jnp.exp(draws), extent[axis_at] // parts).reshape((-1,) + (1,) * (len(extent) - axis_at - 1))

    factor_of = one(*pieces[0])
    for cut in pieces[1:]:
        factor_of = factor_of * one(*cut)
    return factor_of


def scatter_about(own_key, extent, scale, limit, cuts=(), kind=jnp.bfloat16):
    entries = scale * jax.random.normal(own_key, extent, jnp.float32)
    if cuts:
        entries = entries * shard_levels(own_key, extent, cuts, -0.22, 0.18)
    return jnp.clip(entries, -limit, limit).astype(kind)


def setup_inputs(seed: int = 0) -> dict:
    streams_of = jax.random.split(jax.random.key(seed), 15)
    return {
        "adjoint": scatter_about(streams_of[0], (3, NP, ELEMENTS), 1.0, 6.0, ((2, 32),), jnp.float32),
        "deriv_r": scatter_about(streams_of[1], (NP, NP), NP ** -0.5, 0.75, (), jnp.float32),
        "deriv_s": scatter_about(streams_of[2], (NP, NP), NP ** -0.5, 0.75, (), jnp.float32),
        "lift": scatter_about(streams_of[3], (NP, 3 * NFP), NP ** -0.5, 0.75, (), jnp.float32),
        "metric": jnp.clip(jax.random.uniform(streams_of[4], (4, ELEMENTS), jnp.float32, -1.5, 1.5) * shard_levels(streams_of[4], (4, ELEMENTS), ((1, 32),), -0.4, 0.0), -1.5, 1.5),
        "face_scale": jnp.clip(jnp.exp(math.log(4.0) - 2.0794415 * jax.random.uniform(streams_of[5], (3, ELEMENTS), jnp.float32) ** shard_levels(streams_of[5], (3, ELEMENTS), ((1, 32),), -0.2, 0.2)), 0.5, 4.0),
        "face_angle": jnp.clip(jax.random.uniform(streams_of[6], (3, ELEMENTS), jnp.float32, -3.140625, 3.140625), -3.140625, 3.140625),
        "neighbours": draw_neighbours(jax.random.fold_in(streams_of[14], 71), 0),
        "neighbour_face": draw_neighbour_face(jax.random.fold_in(streams_of[14], 71), 0),
        "remap_table": scatter_about(streams_of[9], (NTYPE, NP, NP), NP ** -0.5, 0.75, (), jnp.float32),
        "intersection_elem": plant(jax.random.randint(streams_of[10], (Q_TOTAL,), 0, E_DEV), jax.random.fold_in(streams_of[10], 1), 0, E_DEV - 1).astype(jnp.int32),
        "intersection_old": draw_intersection_old(jax.random.fold_in(streams_of[14], 71), 0),
        "intersection_weight": jnp.clip(jnp.exp(math.log(1.0) - 2.9957323 * jax.random.uniform(streams_of[12], (Q_TOTAL,), jnp.float32) ** shard_levels(streams_of[12], (Q_TOTAL,), ((0, 32),), -0.2, 0.2)), 0.05, 1.0),
        "block_type": plant(jax.random.randint(streams_of[13], (BLK_TOTAL,), 0, NTYPE), jax.random.fold_in(streams_of[13], 1), 0, NTYPE - 1).astype(jnp.int32),
    }


gravity = 2.0
depth = 0.5
wave_speed = 1.0
time_step = 0.04
highest = lax.Precision.HIGHEST


def face_table(degree):
    basis_count = (degree + 1) * (degree + 2) // 2

    def node_place(column, level):
        return level * (degree + 1) - level * (level - 1) // 2 + column

    ones_table = np.zeros((3, degree + 1, basis_count), np.float32)
    for level in range(degree + 1):
        ones_table[0, level, node_place(level, 0)] = 1.0
        ones_table[1, level, node_place(degree - level, level)] = 1.0
        ones_table[2, level, node_place(0, degree - level)] = 1.0
    return jnp.asarray(ones_table)


def offset_table(q_rows, reach):
    cap_far = q_rows // 32
    cap_near = q_rows // 8
    cap_home = q_rows - 2 * cap_near - 2 * (reach - 1) * cap_far
    offsets_list = []
    for offset in range(-reach, reach + 1):
        if offset == 0:
            group_size = cap_home
        elif abs(offset) == 1:
            group_size = cap_near
        else:
            group_size = cap_far
        offsets_list.extend([offset] * group_size)
    return np.array(offsets_list, np.int32)


def volume_terms(current, deriv_r, deriv_s, metric):
    along_r = jnp.einsum("pq,fpe->fqe", deriv_r, current, precision=highest)
    along_s = jnp.einsum("pq,fpe->fqe", deriv_s, current, precision=highest)
    to_height = -gravity * (metric[0] * along_r[1] + metric[1] * along_s[1] + metric[2] * along_r[2] + metric[3] * along_s[2])
    to_along_x = -depth * (metric[0] * along_r[0] + metric[1] * along_s[0])
    to_along_y = -depth * (metric[2] * along_r[0] + metric[3] * along_s[0])
    return jnp.stack([to_height, to_along_x, to_along_y])


def face_terms(current, lift, face_scale, face_angle):
    lift_faces = lift.reshape(lift.shape[0], 3, -1)
    lifted = jnp.einsum("pgn,fpe->fnge", lift_faces, current, precision=highest)
    normal_x = jnp.cos(face_angle)[None]
    normal_y = jnp.sin(face_angle)[None]
    half_scale = 0.5 * face_scale[None]
    height, along_x, along_y = lifted[0], lifted[1], lifted[2]
    face_height = half_scale * (gravity * (normal_x * along_x + normal_y * along_y) - wave_speed * height)
    face_along_x = half_scale * (depth * normal_x * height - wave_speed * along_x)
    face_along_y = half_scale * (depth * normal_y * height - wave_speed * along_y)
    return jnp.stack([face_height, face_along_x, face_along_y])


def reference(adjoint, deriv_r, deriv_s, lift, metric, face_scale, face_angle, neighbours, neighbour_face, remap_table, intersection_elem, intersection_old, intersection_weight, block_type):
    face_ones = face_table(ORDER)
    elem_total = adjoint.shape[2]
    flat_index = neighbour_face * elem_total + neighbours

    def advance(current):
        volume = volume_terms(current, deriv_r, deriv_s, metric)
        traces = face_terms(current, lift, face_scale, face_angle)
        flattened = traces.reshape(3, traces.shape[1], 3 * elem_total)
        outside = jnp.take(flattened, flat_index, axis=2)
        jump_terms = traces - outside[:, ::-1]
        surface = jnp.einsum("gnp,fnge->fpe", face_ones, jump_terms, precision=highest)
        return current + time_step * (volume + surface)

    section_two = (2.0 / 3.0) * advance(adjoint)
    section_one = 0.25 * advance(section_two)
    adj_new = adjoint / 3.0 + 0.75 * section_two + advance(section_one)

    owner_count = N_GX * N_GY
    row_ids = jnp.arange(Q_TOTAL, dtype=jnp.int32)
    source = row_ids // Q_DEV
    gathered = jnp.take(adj_new, source * E_DEV + intersection_elem, axis=2)
    blocks = gathered.reshape(3, NP, BLK_TOTAL, BLOCK)
    chosen = jnp.take(remap_table, block_type, axis=0)
    mapped = jnp.einsum("bij,fibr->fjbr", chosen, blocks, precision=highest)
    mapped = (mapped * intersection_weight.reshape(1, 1, BLK_TOTAL, BLOCK)).reshape(3, NP, Q_TOTAL)
    row_offset = jnp.asarray(offset_table(Q_DEV, REACH))[row_ids % Q_DEV]
    row_owner = ((source + row_offset + owner_count) % owner_count).astype(jnp.int32)
    target = jnp.where(intersection_old < 0, OLD_ELEMENTS, row_owner * E_OLD_DEV + intersection_old).astype(jnp.int32)
    old_sums = jnp.zeros((3, NP, OLD_ELEMENTS + 1), jnp.float32).at[:, :, target].add(mapped)
    return adj_new, old_sums[:, :, :OLD_ELEMENTS]
```

```python
import jax
import jax.numpy as jnp
import numpy as np
from jax import lax
from jax.sharding import PartitionSpec as P

ORDER = 10
REACH = 4
BLOCK = 128
RIM = 32
HALO = 128
E_OLD_DEV = 2048

gravity = 2.0
depth = 0.5
wave_speed = 1.0
time_step = 0.04
highest = lax.Precision.HIGHEST
AXES = ("gx", "gy")


def extended(cells, width):
    count = lax.axis_size(AXES)
    head = cells[:width]
    tail = cells[cells.shape[0] - width :]
    return jnp.concatenate(
        [
            lax.ppermute(tail, AXES, [(i, (i + 1) % count) for i in range(count)]),
            cells,
            lax.ppermute(head, AXES, [((i + 1) % count, i) for i in range(count)]),
        ],
        axis=0,
    )


def shifted(shard, by):
    length = lax.axis_size(AXES)
    return lax.ppermute(shard, AXES, [(i, (i + by) % length) for i in range(length)])


def face_table(degree):
    basis_count = (degree + 1) * (degree + 2) // 2

    def node_place(column, level):
        return level * (degree + 1) - level * (level - 1) // 2 + column

    ones_table = np.zeros((3, degree + 1, basis_count), np.float32)
    for level in range(degree + 1):
        ones_table[0, level, node_place(level, 0)] = 1.0
        ones_table[1, level, node_place(degree - level, level)] = 1.0
        ones_table[2, level, node_place(0, degree - level)] = 1.0
    return ones_table


def surface_matrix(degree):
    ones_table = face_table(degree)
    faces, nodes, basis_count = ones_table.shape
    own = ones_table.reshape(faces * nodes, basis_count)
    other = -ones_table[:, ::-1, :].reshape(faces * nodes, basis_count)
    return jnp.asarray(np.concatenate([own, other], axis=0))


def group_bounds(q_rows, reach):
    cap_far = q_rows // 32
    cap_near = q_rows // 8
    cap_home = q_rows - 2 * cap_near - 2 * (reach - 1) * cap_far
    bounds = []
    start = 0
    for offset in range(-reach, reach + 1):
        if offset == 0:
            group_size = cap_home
        elif abs(offset) == 1:
            group_size = cap_near
        else:
            group_size = cap_far
        bounds.append((offset, start, group_size))
        start = start + group_size
    return bounds


def split_dot(onehot, values):
    return jnp.dot(onehot.astype(jnp.float32), values, precision=lax.Precision.HIGH)


def body(
    adjoint,
    deriv_r,
    deriv_s,
    lift,
    metric,
    face_scale,
    face_angle,
    neighbours,
    neighbour_face,
    remap_table,
    intersection_elem,
    intersection_old,
    intersection_weight,
    block_type,
):
    fields, basis_count, elem_count = adjoint.shape
    nodes = ORDER + 1
    devices = lax.axis_size(AXES)
    elem_total = elem_count * devices
    first_elem = lax.axis_index(AXES) * elem_count
    width = elem_count + 2 * HALO

    state = adjoint.reshape(fields * basis_count, elem_count).T
    params = jnp.concatenate([metric, face_scale, face_angle], axis=0).T
    links = jnp.concatenate([neighbours, neighbour_face], axis=0).T
    both = extended(jnp.concatenate([state, params], axis=1), HALO)
    links = extended(links, HALO)
    start = both[:, : fields * basis_count]
    params = both[:, fields * basis_count :]
    m0, m1, m2, m3 = (params[:, k : k + 1] for k in range(4))
    half_scale = 0.5 * params[:, 4:7][:, :, None]
    angle = params[:, 7:10][:, :, None]
    normal_x = jnp.cos(angle)
    normal_y = jnp.sin(angle)
    local_index = (links[:, 0:3] - first_elem + HALO + elem_total) % elem_total
    local_index = jnp.clip(local_index, 0, width - 1)
    across_face = links[:, 3:6][:, :, None, None]

    mats = jnp.concatenate([deriv_r, deriv_s, lift], axis=1)
    surf = surface_matrix(ORDER)

    def advance(current):
        cur = current.reshape(width, fields, basis_count)
        prod = jnp.einsum("wcp,pk->wck", cur, mats, precision=highest)
        along_r = prod[:, :, :basis_count]
        along_s = prod[:, :, basis_count : 2 * basis_count]
        lifted = prod[:, :, 2 * basis_count :].reshape(width, fields, 3, nodes)
        to_height = -gravity * (
            m0 * along_r[:, 1] + m1 * along_s[:, 1] + m2 * along_r[:, 2] + m3 * along_s[:, 2]
        )
        to_along_x = -depth * (m0 * along_r[:, 0] + m1 * along_s[:, 0])
        to_along_y = -depth * (m2 * along_r[:, 0] + m3 * along_s[:, 0])
        height, along_x, along_y = (lifted[:, 0], lifted[:, 1], lifted[:, 2])
        face_height = half_scale * (
            gravity * (normal_x * along_x + normal_y * along_y) - wave_speed * height
        )
        face_along_x = half_scale * (depth * normal_x * height - wave_speed * along_x)
        face_along_y = half_scale * (depth * normal_y * height - wave_speed * along_y)
        traces = jnp.stack([face_height, face_along_x, face_along_y], axis=1)
        rows = traces.reshape(width, fields * 3 * nodes)
        picked = jnp.take(rows, local_index, axis=0).reshape(width, 3, fields, 3, nodes)
        outside = jnp.where(
            across_face == 0,
            picked[:, :, :, 0],
            jnp.where(across_face == 1, picked[:, :, :, 1], picked[:, :, :, 2]),
        )
        outside = jnp.swapaxes(outside, 1, 2).reshape(width, fields, 3 * nodes)
        jumps = jnp.concatenate([traces.reshape(width, fields, 3 * nodes), outside], axis=2)
        surface = jnp.einsum("wcn,np->wcp", jumps, surf, precision=highest)
        volume = jnp.stack([to_height, to_along_x, to_along_y], axis=1)
        return current + time_step * (volume + surface).reshape(width, fields * basis_count)

    section_two = 2.0 / 3.0 * advance(start)
    section_one = 0.25 * advance(section_two)
    adj_rows = start / 3.0 + 0.75 * section_two + advance(section_one)
    adj_rows = adj_rows[HALO : HALO + elem_count]
    adj_new = adj_rows.T.reshape(fields, basis_count, elem_count)

    rows_here = intersection_elem.shape[0]
    block_here = rows_here // BLOCK
    field_rows = fields * basis_count
    picked = jnp.take(adj_rows, intersection_elem, axis=0)
    picked = picked.reshape(block_here, BLOCK, fields, basis_count)
    chosen = jnp.take(remap_table, block_type, axis=0)
    mapped = jnp.einsum("brci,bij->brcj", picked, chosen, precision=highest)
    mapped = mapped * intersection_weight.reshape(block_here, BLOCK, 1, 1)
    mapped = mapped.reshape(rows_here, field_rows)
    labelled = jnp.concatenate(
        [mapped, intersection_old.astype(jnp.float32)[:, None]], axis=1
    )
    bounds = group_bounds(rows_here, REACH)
    kept = []
    for offset, start_row, group_size in bounds:
        piece = labelled[start_row : start_row + group_size]
        kept.append(piece if offset == 0 else shifted(piece, offset))
    received = jnp.concatenate(kept, axis=0)
    labels = received[:, field_rows].astype(jnp.int32)
    old_count = E_OLD_DEV
    selector = (jnp.arange(old_count, dtype=jnp.int32)[:, None] == labels[None, :])
    old_sums = split_dot(selector, received[:, :field_rows])
    return (adj_new, old_sums.T.reshape(fields, basis_count, old_count))


def solution(mesh):
    in_specs = (
        P(None, None, AXES),
        P(),
        P(),
        P(),
        P(None, AXES),
        P(None, AXES),
        P(None, AXES),
        P(None, AXES),
        P(None, AXES),
        P(),
        P(AXES),
        P(AXES),
        P(AXES),
        P(AXES),
    )
    out_specs = (P(None, None, AXES), P(None, None, AXES))
    return jax.shard_map(body, mesh=mesh, in_specs=in_specs, out_specs=out_specs, check_vma=False)
```

```python
import jax
import jax.numpy as jnp
import numpy as np
from jax import lax
from jax.experimental import pallas as pl
from jax.experimental.pallas import tpu as pltpu
from jax.sharding import PartitionSpec as P

ORDER = 10
REACH = 4
BLOCK = 128
RIM = 32
HALO = 128
E_OLD_DEV = 2048

gravity = 2.0
depth = 0.5
wave_speed = 1.0
time_step = 0.04
highest = lax.Precision.HIGHEST
AXES = ("gx", "gy")


def extended(cells, width, axis=0):
    count = lax.axis_size(AXES)
    size = cells.shape[axis]
    head = lax.slice_in_dim(cells, 0, width, axis=axis)
    tail = lax.slice_in_dim(cells, size - width, size, axis=axis)
    return jnp.concatenate(
        [
            lax.ppermute(tail, AXES, [(i, (i + 1) % count) for i in range(count)]),
            cells,
            lax.ppermute(head, AXES, [((i + 1) % count, i) for i in range(count)]),
        ],
        axis=axis,
    )


def shifted(shard, by):
    length = lax.axis_size(AXES)
    return lax.ppermute(shard, AXES, [(i, (i + by) % length) for i in range(length)])


def face_table(degree):
    basis_count = (degree + 1) * (degree + 2) // 2

    def node_place(column, level):
        return level * (degree + 1) - level * (level - 1) // 2 + column

    ones_table = np.zeros((3, degree + 1, basis_count), np.float32)
    for level in range(degree + 1):
        ones_table[0, level, node_place(level, 0)] = 1.0
        ones_table[1, level, node_place(degree - level, level)] = 1.0
        ones_table[2, level, node_place(0, degree - level)] = 1.0
    return ones_table


def surface_matrix(degree):
    ones_table = face_table(degree)
    faces, nodes, basis_count = ones_table.shape
    own = ones_table.reshape(faces * nodes, basis_count)
    other = -ones_table[:, ::-1, :].reshape(faces * nodes, basis_count)
    return jnp.asarray(np.concatenate([own, other], axis=0))


def group_bounds(q_rows, reach):
    cap_far = q_rows // 32
    cap_near = q_rows // 8
    cap_home = q_rows - 2 * cap_near - 2 * (reach - 1) * cap_far
    bounds = []
    start = 0
    for offset in range(-reach, reach + 1):
        if offset == 0:
            group_size = cap_home
        elif abs(offset) == 1:
            group_size = cap_near
        else:
            group_size = cap_far
        bounds.append((offset, start, group_size))
        start = start + group_size
    return bounds


def split_dot(onehot, values):
    return jnp.dot(onehot.astype(jnp.float32), values, precision=lax.Precision.HIGH)


LANES = 128
ROWS = 40


def stage_tables(deriv_r, deriv_s, lift, degree):
    basis_count = deriv_r.shape[0]
    nodes = degree + 1
    lift_t = jnp.zeros((ROWS, basis_count), jnp.float32).at[: 3 * nodes].set(lift.T)
    deriv_t = jnp.zeros((144, basis_count), jnp.float32)
    deriv_t = deriv_t.at[:basis_count].set(deriv_r.T).at[72 : 72 + basis_count].set(deriv_s.T)
    ones_table = face_table(degree)
    faces = ones_table.shape[0]
    own = np.zeros((basis_count, ROWS), np.float32)
    own[:, : faces * nodes] = ones_table.reshape(faces * nodes, basis_count).T
    parts = [own]
    for g in range(faces):
        other = np.zeros((basis_count, ROWS), np.float32)
        for f in range(faces):
            other[:, f * nodes : (f + 1) * nodes] = -ones_table[g, ::-1, :].T
        parts.append(other)
    surf = jnp.asarray(np.concatenate(parts, axis=1))
    return lift_t, deriv_t, surf


def stage_kernel(x_ref, met_ref, geo_ref, li_ref, nf_ref, lt_ref, dt_ref, sm_ref, out_ref, s2_ref, s1_ref, z_ref):
    fields, basis_count, width = x_ref.shape
    blocks = width // LANES
    z_ref[:, 0:LANES] = jnp.zeros((fields * ROWS, LANES), jnp.float32)
    z_ref[:, width + LANES : width + 2 * LANES] = jnp.zeros((fields * ROWS, LANES), jnp.float32)
    rowface = lax.broadcasted_iota(jnp.int32, (ROWS, LANES), 0) // (ORDER + 1)
    window = lax.broadcasted_iota(jnp.int32, (3 * LANES, LANES), 0)

    def dot(a, b):
        return jnp.dot(a, b, precision=highest, preferred_element_type=jnp.float32)

    def run(src_ref, kind):
        def traces(b, carry):
            off = pl.multiple_of(b * LANES, LANES)
            lifted = [dot(lt_ref[...], src_ref[c, :, pl.ds(off, LANES)]) for c in range(fields)]
            half_scale = geo_ref[0, :, pl.ds(off, LANES)]
            normal_x = geo_ref[1, :, pl.ds(off, LANES)]
            normal_y = geo_ref[2, :, pl.ds(off, LANES)]
            height, along_x, along_y = lifted
            face_height = half_scale * (
                gravity * (normal_x * along_x + normal_y * along_y) - wave_speed * height
            )
            face_along_x = half_scale * (depth * normal_x * height - wave_speed * along_x)
            face_along_y = half_scale * (depth * normal_y * height - wave_speed * along_y)
            dst = pl.multiple_of(off + LANES, LANES)
            z_ref[0:ROWS, pl.ds(dst, LANES)] = face_height
            z_ref[ROWS : 2 * ROWS, pl.ds(dst, LANES)] = face_along_x
            z_ref[2 * ROWS : 3 * ROWS, pl.ds(dst, LANES)] = face_along_y
            return carry

        lax.fori_loop(0, blocks, traces, 0)

        def update(b, carry):
            off = pl.multiple_of(b * LANES, LANES)
            near = z_ref[:, pl.ds(off, 3 * LANES)]
            gathered = []
            for g in range(3):
                spot = li_ref[g : g + 1, pl.ds(off, LANES)] - (off - LANES)
                onehot = (window == spot).astype(jnp.float32)
                across = nf_ref[g : g + 1, pl.ds(off, LANES)]
                picked = dot(near, onehot)
                gathered.append((picked, rowface == across))
            m = met_ref[:, pl.ds(off, LANES)]
            m0, m1, m2, m3 = (m[k : k + 1] for k in range(4))
            cur = [src_ref[c, :, pl.ds(off, LANES)] for c in range(fields)]
            rs = [dot(dt_ref[...], cur[c]) for c in range(fields)]
            along_r = [v[0:basis_count] for v in rs]
            along_s = [v[72 : 72 + basis_count] for v in rs]
            volume = [
                -gravity * (m0 * along_r[1] + m1 * along_s[1] + m2 * along_r[2] + m3 * along_s[2]),
                -depth * (m0 * along_r[0] + m1 * along_s[0]),
                -depth * (m2 * along_r[0] + m3 * along_s[0]),
            ]
            for c in range(fields):
                own = z_ref[c * ROWS : (c + 1) * ROWS, pl.ds(pl.multiple_of(off + LANES, LANES), LANES)]
                pieces = [own] + [
                    jnp.where(mask, picked[c * ROWS : (c + 1) * ROWS], 0.0) for picked, mask in gathered
                ]
                surface = dot(sm_ref[...], jnp.concatenate(pieces, axis=0))
                new = cur[c] + time_step * (volume[c] + surface)
                if kind == 0:
                    s2_ref[c, :, pl.ds(off, LANES)] = 2.0 / 3.0 * new
                elif kind == 1:
                    s1_ref[c, :, pl.ds(off, LANES)] = 0.25 * new
                else:
                    dst = pl.multiple_of(off - LANES, LANES)
                    out_ref[c, :, pl.ds(dst, LANES)] = (
                        x_ref[c, :, pl.ds(off, LANES)] / 3.0 + 0.75 * s2_ref[c, :, pl.ds(off, LANES)] + new
                    )
            return carry

        if kind == 2:
            lax.fori_loop(1, blocks - 1, update, 0)
        else:
            lax.fori_loop(0, blocks, update, 0)

    run(x_ref, 0)
    run(s2_ref, 1)
    run(s1_ref, 2)


def body(
    adjoint,
    deriv_r,
    deriv_s,
    lift,
    metric,
    face_scale,
    face_angle,
    neighbours,
    neighbour_face,
    remap_table,
    intersection_elem,
    intersection_old,
    intersection_weight,
    block_type,
):
    fields, basis_count, elem_count = adjoint.shape
    nodes = ORDER + 1
    devices = lax.axis_size(AXES)
    elem_total = elem_count * devices
    first_elem = lax.axis_index(AXES) * elem_count
    width = elem_count + 2 * HALO

    state = adjoint.reshape(fields * basis_count, elem_count)
    params = jnp.concatenate([state, metric, face_scale, face_angle], axis=0)
    params = extended(params, HALO, axis=1)
    links = extended(jnp.concatenate([neighbours, neighbour_face], axis=0), HALO, axis=1)
    start = params[: fields * basis_count].reshape(fields, basis_count, width)
    params = params[fields * basis_count :]
    met = params[0:4]
    half_scale = 0.5 * params[4:7]
    angle = params[7:10]

    def spread(v):
        rows = jnp.repeat(v, nodes, axis=0)
        return jnp.concatenate([rows, jnp.zeros((ROWS - 3 * nodes, width), jnp.float32)], axis=0)

    geo = jnp.stack([spread(half_scale), spread(jnp.cos(angle)), spread(jnp.sin(angle))])
    local_index = (links[0:3] - first_elem + HALO + elem_total) % elem_total
    local_index = jnp.clip(local_index, 0, width - 1)
    across_face = links[3:6]
    lift_t, deriv_t, surf = stage_tables(deriv_r, deriv_s, lift, ORDER)
    adj_new = pl.pallas_call(
        stage_kernel,
        out_shape=jax.ShapeDtypeStruct((fields, basis_count, elem_count), jnp.float32),
        scratch_shapes=[
            pltpu.VMEM((fields, basis_count, width), jnp.float32),
            pltpu.VMEM((fields, basis_count, width), jnp.float32),
            pltpu.VMEM((fields * ROWS, width + 2 * LANES), jnp.float32),
        ],
        compiler_params=pltpu.CompilerParams(vmem_limit_bytes=48 * 1024 * 1024),
    )(start, met, geo, local_index, across_face, lift_t, deriv_t, surf)
    adj_rows = adj_new.reshape(fields * basis_count, elem_count).T

    rows_here = intersection_elem.shape[0]
    block_here = rows_here // BLOCK
    field_rows = fields * basis_count
    picked = jnp.take(adj_rows, intersection_elem, axis=0)
    picked = picked.reshape(block_here, BLOCK, fields, basis_count)
    chosen = jnp.take(remap_table, block_type, axis=0)
    mapped = jnp.einsum("brci,bij->brcj", picked, chosen, precision=highest)
    mapped = mapped * intersection_weight.reshape(block_here, BLOCK, 1, 1)
    mapped = mapped.reshape(rows_here, field_rows)
    labelled = jnp.concatenate(
        [mapped, intersection_old.astype(jnp.float32)[:, None]], axis=1
    )
    bounds = group_bounds(rows_here, REACH)
    kept = []
    for offset, start_row, group_size in bounds:
        piece = labelled[start_row : start_row + group_size]
        kept.append(piece if offset == 0 else shifted(piece, offset))
    received = jnp.concatenate(kept, axis=0)
    labels = received[:, field_rows].astype(jnp.int32)
    old_count = E_OLD_DEV
    selector = (jnp.arange(old_count, dtype=jnp.int32)[:, None] == labels[None, :])
    old_sums = split_dot(selector, received[:, :field_rows])
    return (adj_new, old_sums.T.reshape(fields, basis_count, old_count))


def solution(mesh):
    in_specs = (
        P(None, None, AXES),
        P(),
        P(),
        P(),
        P(None, AXES),
        P(None, AXES),
        P(None, AXES),
        P(None, AXES),
        P(None, AXES),
        P(),
        P(AXES),
        P(AXES),
        P(AXES),
        P(AXES),
    )
    out_specs = (P(None, None, AXES), P(None, None, AXES))
    return jax.shard_map(body, mesh=mesh, in_specs=in_specs, out_specs=out_specs, check_vma=False)
```

```python
import jax
import jax.numpy as jnp
import numpy as np
from jax import lax
from jax.experimental import pallas as pl
from jax.experimental.pallas import tpu as pltpu
from jax.sharding import PartitionSpec as P

ORDER = 10
REACH = 4
BLOCK = 128
RIM = 32
HALO = 128
E_OLD_DEV = 2048

gravity = 2.0
depth = 0.5
wave_speed = 1.0
time_step = 0.04
highest = lax.Precision.HIGHEST
AXES = ("gx", "gy")


def extended(cells, width, axis=0):
    count = lax.axis_size(AXES)
    size = cells.shape[axis]
    head = lax.slice_in_dim(cells, 0, width, axis=axis)
    tail = lax.slice_in_dim(cells, size - width, size, axis=axis)
    return jnp.concatenate(
        [
            lax.ppermute(tail, AXES, [(i, (i + 1) % count) for i in range(count)]),
            cells,
            lax.ppermute(head, AXES, [((i + 1) % count, i) for i in range(count)]),
        ],
        axis=axis,
    )


def shifted(shard, by):
    length = lax.axis_size(AXES)
    return lax.ppermute(shard, AXES, [(i, (i + by) % length) for i in range(length)])


def face_table(degree):
    basis_count = (degree + 1) * (degree + 2) // 2

    def node_place(column, level):
        return level * (degree + 1) - level * (level - 1) // 2 + column

    ones_table = np.zeros((3, degree + 1, basis_count), np.float32)
    for level in range(degree + 1):
        ones_table[0, level, node_place(level, 0)] = 1.0
        ones_table[1, level, node_place(degree - level, level)] = 1.0
        ones_table[2, level, node_place(0, degree - level)] = 1.0
    return ones_table


def surface_matrix(degree):
    ones_table = face_table(degree)
    faces, nodes, basis_count = ones_table.shape
    own = ones_table.reshape(faces * nodes, basis_count)
    other = -ones_table[:, ::-1, :].reshape(faces * nodes, basis_count)
    return jnp.asarray(np.concatenate([own, other], axis=0))


def group_bounds(q_rows, reach):
    cap_far = q_rows // 32
    cap_near = q_rows // 8
    cap_home = q_rows - 2 * cap_near - 2 * (reach - 1) * cap_far
    bounds = []
    start = 0
    for offset in range(-reach, reach + 1):
        if offset == 0:
            group_size = cap_home
        elif abs(offset) == 1:
            group_size = cap_near
        else:
            group_size = cap_far
        bounds.append((offset, start, group_size))
        start = start + group_size
    return bounds


def split_dot(onehot, values):
    return jnp.dot(onehot.astype(jnp.float32), values, precision=lax.Precision.HIGH)


LANES = 128
ROWS = 48


def stage_tables(deriv_r, deriv_s, lift, degree):
    basis_count = deriv_r.shape[0]
    nodes = degree + 1
    lift_t = jnp.zeros((ROWS, basis_count), jnp.float32).at[: 3 * nodes].set(lift.T)
    deriv_t = jnp.zeros((144, basis_count), jnp.float32)
    deriv_t = deriv_t.at[:basis_count].set(deriv_r.T).at[72 : 72 + basis_count].set(deriv_s.T)
    ones_table = face_table(degree)
    faces = ones_table.shape[0]
    own = np.zeros((basis_count, ROWS), np.float32)
    own[:, : faces * nodes] = ones_table.reshape(faces * nodes, basis_count).T
    parts = [own, own]
    for g in range(faces):
        other = np.zeros((basis_count, ROWS), np.float32)
        for f in range(faces):
            other[:, f * nodes : (f + 1) * nodes] = -ones_table[g, ::-1, :].T
        parts.extend([other, other])
    surf = jnp.asarray(np.concatenate(parts, axis=1), jnp.bfloat16)
    return lift_t, deriv_t, surf


def stage_kernel(x_ref, met_ref, geo_ref, li_ref, nf_ref, lt_ref, dt_ref, sm_ref, out_ref, s2_ref, s1_ref, z_ref):
    fields, basis_count, width = x_ref.shape
    blocks = width // LANES
    split_rows = 2 * fields * ROWS
    z_ref[:, 0:LANES] = jnp.zeros((split_rows, LANES), jnp.bfloat16)
    z_ref[:, width + LANES : width + 2 * LANES] = jnp.zeros((split_rows, LANES), jnp.bfloat16)
    rowface = lax.broadcasted_iota(jnp.int32, (ROWS, LANES), 0) // (ORDER + 1)
    window = lax.broadcasted_iota(jnp.int32, (3 * LANES, LANES), 0)

    def dot(a, b):
        return jnp.dot(a, b, precision=highest, preferred_element_type=jnp.float32)

    def dot16(a, b):
        return jnp.dot(a, b, preferred_element_type=jnp.float32)

    def run(src_ref, kind):
        def traces(b, carry):
            off = pl.multiple_of(b * LANES, LANES)
            lifted = [dot(lt_ref[...], src_ref[c, :, pl.ds(off, LANES)]) for c in range(fields)]
            half_scale = geo_ref[0, :, pl.ds(off, LANES)]
            normal_x = geo_ref[1, :, pl.ds(off, LANES)]
            normal_y = geo_ref[2, :, pl.ds(off, LANES)]
            height, along_x, along_y = lifted
            face_height = half_scale * (
                gravity * (normal_x * along_x + normal_y * along_y) - wave_speed * height
            )
            face_along_x = half_scale * (depth * normal_x * height - wave_speed * along_x)
            face_along_y = half_scale * (depth * normal_y * height - wave_speed * along_y)
            dst = pl.multiple_of(off + LANES, LANES)
            for c, value in enumerate((face_height, face_along_x, face_along_y)):
                high = value.astype(jnp.bfloat16)
                low = (value - high.astype(jnp.float32)).astype(jnp.bfloat16)
                z_ref[c * ROWS : (c + 1) * ROWS, pl.ds(dst, LANES)] = high
                z_ref[(fields + c) * ROWS : (fields + c + 1) * ROWS, pl.ds(dst, LANES)] = low
            return carry

        lax.fori_loop(0, blocks, traces, 0)

        def update(b, carry):
            off = pl.multiple_of(b * LANES, LANES)
            near = z_ref[:, pl.ds(off, 3 * LANES)]
            gathered = []
            for g in range(3):
                spot = li_ref[g : g + 1, pl.ds(off, LANES)] - (off - LANES)
                onehot = (window == spot).astype(jnp.bfloat16)
                across = nf_ref[g : g + 1, pl.ds(off, LANES)]
                picked = dot16(near, onehot)
                gathered.append((picked, rowface == across))
            m = met_ref[:, pl.ds(off, LANES)]
            m0, m1, m2, m3 = (m[k : k + 1] for k in range(4))
            cur = [src_ref[c, :, pl.ds(off, LANES)] for c in range(fields)]
            rs = [dot(dt_ref[...], cur[c]) for c in range(fields)]
            along_r = [v[0:basis_count] for v in rs]
            along_s = [v[72 : 72 + basis_count] for v in rs]
            volume = [
                -gravity * (m0 * along_r[1] + m1 * along_s[1] + m2 * along_r[2] + m3 * along_s[2]),
                -depth * (m0 * along_r[0] + m1 * along_s[0]),
                -depth * (m2 * along_r[0] + m3 * along_s[0]),
            ]
            here = pl.ds(pl.multiple_of(off + LANES, LANES), LANES)
            for c in range(fields):
                hi_rows = slice(c * ROWS, (c + 1) * ROWS)
                lo_rows = slice((fields + c) * ROWS, (fields + c + 1) * ROWS)
                pieces = [z_ref[hi_rows, here], z_ref[lo_rows, here]]
                for picked, mask in gathered:
                    for rows in (hi_rows, lo_rows):
                        pieces.append(jnp.where(mask, picked[rows], 0.0).astype(jnp.bfloat16))
                surface = dot16(sm_ref[...], jnp.concatenate(pieces, axis=0))
                new = cur[c] + time_step * (volume[c] + surface)
                if kind == 0:
                    s2_ref[c, :, pl.ds(off, LANES)] = 2.0 / 3.0 * new
                elif kind == 1:
                    s1_ref[c, :, pl.ds(off, LANES)] = 0.25 * new
                else:
                    dst = pl.multiple_of(off - LANES, LANES)
                    out_ref[c, :, pl.ds(dst, LANES)] = (
                        x_ref[c, :, pl.ds(off, LANES)] / 3.0 + 0.75 * s2_ref[c, :, pl.ds(off, LANES)] + new
                    )
            return carry

        if kind == 2:
            lax.fori_loop(1, blocks - 1, update, 0)
        else:
            lax.fori_loop(0, blocks, update, 0)

    run(x_ref, 0)
    run(s2_ref, 1)
    run(s1_ref, 2)


def body(
    adjoint,
    deriv_r,
    deriv_s,
    lift,
    metric,
    face_scale,
    face_angle,
    neighbours,
    neighbour_face,
    remap_table,
    intersection_elem,
    intersection_old,
    intersection_weight,
    block_type,
):
    fields, basis_count, elem_count = adjoint.shape
    nodes = ORDER + 1
    devices = lax.axis_size(AXES)
    elem_total = elem_count * devices
    first_elem = lax.axis_index(AXES) * elem_count
    width = elem_count + 2 * HALO

    state = adjoint.reshape(fields * basis_count, elem_count)
    params = jnp.concatenate([state, metric, face_scale, face_angle], axis=0)
    params = extended(params, HALO, axis=1)
    links = extended(jnp.concatenate([neighbours, neighbour_face], axis=0), HALO, axis=1)
    start = params[: fields * basis_count].reshape(fields, basis_count, width)
    params = params[fields * basis_count :]
    met = params[0:4]
    half_scale = 0.5 * params[4:7]
    angle = params[7:10]

    def spread(v):
        rows = jnp.repeat(v, nodes, axis=0)
        return jnp.concatenate([rows, jnp.zeros((ROWS - 3 * nodes, width), jnp.float32)], axis=0)

    geo = jnp.stack([spread(half_scale), spread(jnp.cos(angle)), spread(jnp.sin(angle))])
    local_index = (links[0:3] - first_elem + HALO + elem_total) % elem_total
    local_index = jnp.clip(local_index, 0, width - 1)
    across_face = links[3:6]
    lift_t, deriv_t, surf = stage_tables(deriv_r, deriv_s, lift, ORDER)
    adj_new = pl.pallas_call(
        stage_kernel,
        out_shape=jax.ShapeDtypeStruct((fields, basis_count, elem_count), jnp.float32),
        scratch_shapes=[
            pltpu.VMEM((fields, basis_count, width), jnp.float32),
            pltpu.VMEM((fields, basis_count, width), jnp.float32),
            pltpu.VMEM((2 * fields * ROWS, width + 2 * LANES), jnp.bfloat16),
        ],
        compiler_params=pltpu.CompilerParams(vmem_limit_bytes=48 * 1024 * 1024),
    )(start, met, geo, local_index, across_face, lift_t, deriv_t, surf)
    adj_rows = adj_new.reshape(fields * basis_count, elem_count).T

    rows_here = intersection_elem.shape[0]
    block_here = rows_here // BLOCK
    field_rows = fields * basis_count
    picked = jnp.take(adj_rows, intersection_elem, axis=0)
    picked = picked.reshape(block_here, BLOCK, fields, basis_count)
    chosen = jnp.take(remap_table, block_type, axis=0)
    mapped = jnp.einsum("brci,bij->brcj", picked, chosen, precision=highest)
    mapped = mapped * intersection_weight.reshape(block_here, BLOCK, 1, 1)
    mapped = mapped.reshape(rows_here, field_rows)
    labelled = jnp.concatenate(
        [mapped, intersection_old.astype(jnp.float32)[:, None]], axis=1
    )
    bounds = group_bounds(rows_here, REACH)
    kept = []
    for offset, start_row, group_size in bounds:
        piece = labelled[start_row : start_row + group_size]
        kept.append(piece if offset == 0 else shifted(piece, offset))
    received = jnp.concatenate(kept, axis=0)
    labels = received[:, field_rows].astype(jnp.int32)
    old_count = E_OLD_DEV
    selector = (jnp.arange(old_count, dtype=jnp.int32)[:, None] == labels[None, :])
    old_sums = split_dot(selector, received[:, :field_rows])
    return (adj_new, old_sums.T.reshape(fields, basis_count, old_count))


def solution(mesh):
    in_specs = (
        P(None, None, AXES),
        P(),
        P(),
        P(),
        P(None, AXES),
        P(None, AXES),
        P(None, AXES),
        P(None, AXES),
        P(None, AXES),
        P(),
        P(AXES),
        P(AXES),
        P(AXES),
        P(AXES),
    )
    out_specs = (P(None, None, AXES), P(None, None, AXES))
    return jax.shard_map(body, mesh=mesh, in_specs=in_specs, out_specs=out_specs, check_vma=False)
```

```python
import jax
import jax.numpy as jnp
import numpy as np
from jax import lax
from jax.experimental import pallas as pl
from jax.experimental.pallas import tpu as pltpu
from jax.sharding import PartitionSpec as P

ORDER = 10
REACH = 4
BLOCK = 128
RIM = 32
HALO = 128
E_OLD_DEV = 2048

gravity = 2.0
depth = 0.5
wave_speed = 1.0
time_step = 0.04
highest = lax.Precision.HIGHEST
AXES = ("gx", "gy")


def extended(cells, width, axis=0):
    count = lax.axis_size(AXES)
    size = cells.shape[axis]
    head = lax.slice_in_dim(cells, 0, width, axis=axis)
    tail = lax.slice_in_dim(cells, size - width, size, axis=axis)
    return jnp.concatenate(
        [
            lax.ppermute(tail, AXES, [(i, (i + 1) % count) for i in range(count)]),
            cells,
            lax.ppermute(head, AXES, [((i + 1) % count, i) for i in range(count)]),
        ],
        axis=axis,
    )


def shifted(shard, by):
    length = lax.axis_size(AXES)
    return lax.ppermute(shard, AXES, [(i, (i + by) % length) for i in range(length)])


def face_table(degree):
    basis_count = (degree + 1) * (degree + 2) // 2

    def node_place(column, level):
        return level * (degree + 1) - level * (level - 1) // 2 + column

    ones_table = np.zeros((3, degree + 1, basis_count), np.float32)
    for level in range(degree + 1):
        ones_table[0, level, node_place(level, 0)] = 1.0
        ones_table[1, level, node_place(degree - level, level)] = 1.0
        ones_table[2, level, node_place(0, degree - level)] = 1.0
    return ones_table


def surface_matrix(degree):
    ones_table = face_table(degree)
    faces, nodes, basis_count = ones_table.shape
    own = ones_table.reshape(faces * nodes, basis_count)
    other = -ones_table[:, ::-1, :].reshape(faces * nodes, basis_count)
    return jnp.asarray(np.concatenate([own, other], axis=0))


def group_bounds(q_rows, reach):
    cap_far = q_rows // 32
    cap_near = q_rows // 8
    cap_home = q_rows - 2 * cap_near - 2 * (reach - 1) * cap_far
    bounds = []
    start = 0
    for offset in range(-reach, reach + 1):
        if offset == 0:
            group_size = cap_home
        elif abs(offset) == 1:
            group_size = cap_near
        else:
            group_size = cap_far
        bounds.append((offset, start, group_size))
        start = start + group_size
    return bounds


def split_dot(onehot, values):
    return jnp.dot(onehot.astype(jnp.float32), values, precision=lax.Precision.HIGH)


LANES = 128
ROWS = 48


def stage_tables(deriv_r, deriv_s, lift, degree):
    basis_count = deriv_r.shape[0]
    nodes = degree + 1
    lift_t = jnp.zeros((ROWS, basis_count), jnp.float32).at[: 3 * nodes].set(lift.T)
    deriv_t = jnp.zeros((144, basis_count), jnp.float32)
    deriv_t = deriv_t.at[:basis_count].set(deriv_r.T).at[72 : 72 + basis_count].set(deriv_s.T)
    ones_table = face_table(degree)
    faces = ones_table.shape[0]
    own = np.zeros((basis_count, ROWS), np.float32)
    own[:, : faces * nodes] = ones_table.reshape(faces * nodes, basis_count).T
    parts = [own, own]
    for g in range(faces):
        other = np.zeros((basis_count, ROWS), np.float32)
        for f in range(faces):
            other[:, f * nodes : (f + 1) * nodes] = -ones_table[g, ::-1, :].T
        parts.extend([other, other])
    surf = jnp.asarray(np.concatenate(parts, axis=1), jnp.bfloat16)
    return lift_t, deriv_t, surf


def stage_kernel(
    hbm_ref, left_ref, right_ref, met_ref, geo_ref, li_ref, nf_ref, lt_ref, dt_ref, sm_ref,
    out_ref, x_ref, s2_ref, s1_ref, z_ref, sem,
):
    elem_count = hbm_ref.shape[2]
    copy = pltpu.make_async_copy(hbm_ref, x_ref.at[:, :, HALO : HALO + elem_count], sem)
    copy.start()
    copy.wait()
    x_ref[:, :, 0:HALO] = left_ref[...]
    x_ref[:, :, HALO + elem_count : 2 * HALO + elem_count] = right_ref[...]
    fields, basis_count, width = x_ref.shape
    blocks = width // LANES
    split_rows = 2 * fields * ROWS
    z_ref[:, 0:LANES] = jnp.zeros((split_rows, LANES), jnp.bfloat16)
    z_ref[:, width + LANES : width + 2 * LANES] = jnp.zeros((split_rows, LANES), jnp.bfloat16)
    rowface = lax.broadcasted_iota(jnp.int32, (ROWS, LANES), 0) // (ORDER + 1)
    window = lax.broadcasted_iota(jnp.int32, (3 * LANES, LANES), 0)

    def dot(a, b):
        return jnp.dot(a, b, precision=highest, preferred_element_type=jnp.float32)

    def dot16(a, b):
        return jnp.dot(a, b, preferred_element_type=jnp.float32)

    def run(src_ref, kind):
        def traces(b, carry):
            off = pl.multiple_of(b * LANES, LANES)
            lifted = [dot(lt_ref[...], src_ref[c, :, pl.ds(off, LANES)]) for c in range(fields)]
            half_scale = geo_ref[0, :, pl.ds(off, LANES)]
            normal_x = geo_ref[1, :, pl.ds(off, LANES)]
            normal_y = geo_ref[2, :, pl.ds(off, LANES)]
            height, along_x, along_y = lifted
            face_height = half_scale * (
                gravity * (normal_x * along_x + normal_y * along_y) - wave_speed * height
            )
            face_along_x = half_scale * (depth * normal_x * height - wave_speed * along_x)
            face_along_y = half_scale * (depth * normal_y * height - wave_speed * along_y)
            dst = pl.multiple_of(off + LANES, LANES)
            for c, value in enumerate((face_height, face_along_x, face_along_y)):
                high = value.astype(jnp.bfloat16)
                low = (value - high.astype(jnp.float32)).astype(jnp.bfloat16)
                z_ref[c * ROWS : (c + 1) * ROWS, pl.ds(dst, LANES)] = high
                z_ref[(fields + c) * ROWS : (fields + c + 1) * ROWS, pl.ds(dst, LANES)] = low
            return carry

        lax.fori_loop(0, blocks, traces, 0)

        def update(b, carry):
            off = pl.multiple_of(b * LANES, LANES)
            near = z_ref[:, pl.ds(off, 3 * LANES)]
            gathered = []
            for g in range(3):
                spot = li_ref[g : g + 1, pl.ds(off, LANES)] - (off - LANES)
                onehot = (window == spot).astype(jnp.bfloat16)
                across = nf_ref[g : g + 1, pl.ds(off, LANES)]
                picked = dot16(near, onehot)
                gathered.append((picked, rowface == across))
            m = met_ref[:, pl.ds(off, LANES)]
            m0, m1, m2, m3 = (m[k : k + 1] for k in range(4))
            cur = [src_ref[c, :, pl.ds(off, LANES)] for c in range(fields)]
            rs = [dot(dt_ref[...], cur[c]) for c in range(fields)]
            along_r = [v[0:basis_count] for v in rs]
            along_s = [v[72 : 72 + basis_count] for v in rs]
            volume = [
                -gravity * (m0 * along_r[1] + m1 * along_s[1] + m2 * along_r[2] + m3 * along_s[2]),
                -depth * (m0 * along_r[0] + m1 * along_s[0]),
                -depth * (m2 * along_r[0] + m3 * along_s[0]),
            ]
            here = pl.ds(pl.multiple_of(off + LANES, LANES), LANES)
            for c in range(fields):
                hi_rows = slice(c * ROWS, (c + 1) * ROWS)
                lo_rows = slice((fields + c) * ROWS, (fields + c + 1) * ROWS)
                pieces = [z_ref[hi_rows, here], z_ref[lo_rows, here]]
                for picked, mask in gathered:
                    for rows in (hi_rows, lo_rows):
                        pieces.append(jnp.where(mask, picked[rows], 0.0).astype(jnp.bfloat16))
                surface = dot16(sm_ref[...], jnp.concatenate(pieces, axis=0))
                new = cur[c] + time_step * (volume[c] + surface)
                if kind == 0:
                    s2_ref[c, :, pl.ds(off, LANES)] = 2.0 / 3.0 * new
                elif kind == 1:
                    s1_ref[c, :, pl.ds(off, LANES)] = 0.25 * new
                else:
                    dst = pl.multiple_of(off - LANES, LANES)
                    out_ref[c, :, pl.ds(dst, LANES)] = (
                        x_ref[c, :, pl.ds(off, LANES)] / 3.0 + 0.75 * s2_ref[c, :, pl.ds(off, LANES)] + new
                    )
            return carry

        if kind == 2:
            lax.fori_loop(1, blocks - 1, update, 0)
        else:
            lax.fori_loop(0, blocks, update, 0)

    run(x_ref, 0)
    run(s2_ref, 1)
    run(s1_ref, 2)


def body(
    adjoint,
    deriv_r,
    deriv_s,
    lift,
    metric,
    face_scale,
    face_angle,
    neighbours,
    neighbour_face,
    remap_table,
    intersection_elem,
    intersection_old,
    intersection_weight,
    block_type,
):
    fields, basis_count, elem_count = adjoint.shape
    nodes = ORDER + 1
    devices = lax.axis_size(AXES)
    elem_total = elem_count * devices
    first_elem = lax.axis_index(AXES) * elem_count
    width = elem_count + 2 * HALO

    count = lax.axis_size(AXES)
    left = lax.ppermute(adjoint[:, :, elem_count - HALO :], AXES, [(i, (i + 1) % count) for i in range(count)])
    right = lax.ppermute(adjoint[:, :, :HALO], AXES, [((i + 1) % count, i) for i in range(count)])
    params = extended(jnp.concatenate([metric, face_scale, face_angle], axis=0), HALO, axis=1)
    links = extended(jnp.concatenate([neighbours, neighbour_face], axis=0), HALO, axis=1)
    met = params[0:4]
    half_scale = 0.5 * params[4:7]
    angle = params[7:10]

    def spread(v):
        rows = jnp.repeat(v, nodes, axis=0)
        return jnp.concatenate([rows, jnp.zeros((ROWS - 3 * nodes, width), jnp.float32)], axis=0)

    geo = jnp.stack([spread(half_scale), spread(jnp.cos(angle)), spread(jnp.sin(angle))])
    local_index = (links[0:3] - first_elem + HALO + elem_total) % elem_total
    local_index = jnp.clip(local_index, 0, width - 1)
    across_face = links[3:6]
    lift_t, deriv_t, surf = stage_tables(deriv_r, deriv_s, lift, ORDER)
    vmem = pl.BlockSpec(memory_space=pltpu.VMEM)
    adj_new = pl.pallas_call(
        stage_kernel,
        out_shape=jax.ShapeDtypeStruct((fields, basis_count, elem_count), jnp.float32),
        in_specs=[pl.BlockSpec(memory_space=pl.ANY)] + [vmem] * 9,
        out_specs=vmem,
        scratch_shapes=[
            pltpu.VMEM((fields, basis_count, width), jnp.float32),
            pltpu.VMEM((fields, basis_count, width), jnp.float32),
            pltpu.VMEM((fields, basis_count, width), jnp.float32),
            pltpu.VMEM((2 * fields * ROWS, width + 2 * LANES), jnp.bfloat16),
            pltpu.SemaphoreType.DMA(()),
        ],
        compiler_params=pltpu.CompilerParams(vmem_limit_bytes=56 * 1024 * 1024),
    )(adjoint, left, right, met, geo, local_index, across_face, lift_t, deriv_t, surf)
    adj_rows = adj_new.reshape(fields * basis_count, elem_count).T

    rows_here = intersection_elem.shape[0]
    block_here = rows_here // BLOCK
    field_rows = fields * basis_count
    picked = jnp.take(adj_rows, intersection_elem, axis=0, mode="clip")
    picked = picked.reshape(block_here, BLOCK, fields, basis_count)
    chosen = jnp.take(remap_table, block_type, axis=0)
    mapped = jnp.einsum("brci,bij->brcj", picked, chosen, precision=highest)
    mapped = mapped * intersection_weight.reshape(block_here, BLOCK, 1, 1)
    mapped = mapped.reshape(rows_here, field_rows)
    labelled = jnp.concatenate(
        [mapped, intersection_old.astype(jnp.float32)[:, None]], axis=1
    )
    bounds = group_bounds(rows_here, REACH)
    old_count = E_OLD_DEV
    old_iota = jnp.arange(old_count, dtype=jnp.int32)[:, None]

    def scatter(rows):
        labels = rows[:, field_rows].astype(jnp.int32)
        return split_dot(old_iota == labels[None, :], rows[:, :field_rows])

    moved = []
    for offset, start_row, group_size in bounds:
        piece = labelled[start_row : start_row + group_size]
        if offset == 0:
            home = piece
        else:
            moved.append(shifted(piece, offset))
    old_sums = scatter(home) + scatter(jnp.concatenate(moved, axis=0))
    return (adj_new, old_sums.T.reshape(fields, basis_count, old_count))


def solution(mesh):
    in_specs = (
        P(None, None, AXES),
        P(),
        P(),
        P(),
        P(None, AXES),
        P(None, AXES),
        P(None, AXES),
        P(None, AXES),
        P(None, AXES),
        P(),
        P(AXES),
        P(AXES),
        P(AXES),
        P(AXES),
    )
    out_specs = (P(None, None, AXES), P(None, None, AXES))
    return jax.shard_map(body, mesh=mesh, in_specs=in_specs, out_specs=out_specs, check_vma=False)
```

```python
import jax
import jax.numpy as jnp
import numpy as np
from jax import lax
from jax.experimental import pallas as pl
from jax.experimental.pallas import tpu as pltpu
from jax.sharding import PartitionSpec as P

ORDER = 10
REACH = 4
BLOCK = 128
RIM = 32
HALO = 128
E_OLD_DEV = 2048

gravity = 2.0
depth = 0.5
wave_speed = 1.0
time_step = 0.04
highest = lax.Precision.HIGHEST
AXES = ("gx", "gy")


def extended(cells, width, axis=0):
    count = lax.axis_size(AXES)
    size = cells.shape[axis]
    head = lax.slice_in_dim(cells, 0, width, axis=axis)
    tail = lax.slice_in_dim(cells, size - width, size, axis=axis)
    return jnp.concatenate(
        [
            lax.ppermute(tail, AXES, [(i, (i + 1) % count) for i in range(count)]),
            cells,
            lax.ppermute(head, AXES, [((i + 1) % count, i) for i in range(count)]),
        ],
        axis=axis,
    )


def shifted(shard, by):
    length = lax.axis_size(AXES)
    return lax.ppermute(shard, AXES, [(i, (i + by) % length) for i in range(length)])


def face_table(degree):
    basis_count = (degree + 1) * (degree + 2) // 2

    def node_place(column, level):
        return level * (degree + 1) - level * (level - 1) // 2 + column

    ones_table = np.zeros((3, degree + 1, basis_count), np.float32)
    for level in range(degree + 1):
        ones_table[0, level, node_place(level, 0)] = 1.0
        ones_table[1, level, node_place(degree - level, level)] = 1.0
        ones_table[2, level, node_place(0, degree - level)] = 1.0
    return ones_table


def surface_matrix(degree):
    ones_table = face_table(degree)
    faces, nodes, basis_count = ones_table.shape
    own = ones_table.reshape(faces * nodes, basis_count)
    other = -ones_table[:, ::-1, :].reshape(faces * nodes, basis_count)
    return jnp.asarray(np.concatenate([own, other], axis=0))


def group_bounds(q_rows, reach):
    cap_far = q_rows // 32
    cap_near = q_rows // 8
    cap_home = q_rows - 2 * cap_near - 2 * (reach - 1) * cap_far
    bounds = []
    start = 0
    for offset in range(-reach, reach + 1):
        if offset == 0:
            group_size = cap_home
        elif abs(offset) == 1:
            group_size = cap_near
        else:
            group_size = cap_far
        bounds.append((offset, start, group_size))
        start = start + group_size
    return bounds


def split_dot(onehot, values):
    return jnp.dot(onehot.astype(jnp.float32), values, precision=lax.Precision.HIGH)


LANES = 128
ROWS = 48


def stage_tables(deriv_r, deriv_s, lift, degree):
    basis_count = deriv_r.shape[0]
    nodes = degree + 1
    lift_t = jnp.zeros((ROWS, basis_count), jnp.float32).at[: 3 * nodes].set(lift.T)
    deriv_t = jnp.zeros((144, basis_count), jnp.float32)
    deriv_t = deriv_t.at[:basis_count].set(deriv_r.T).at[72 : 72 + basis_count].set(deriv_s.T)
    ones_table = face_table(degree)
    faces = ones_table.shape[0]
    own = np.zeros((basis_count, ROWS), np.float32)
    own[:, : faces * nodes] = ones_table.reshape(faces * nodes, basis_count).T
    parts = [own, own]
    for g in range(faces):
        other = np.zeros((basis_count, ROWS), np.float32)
        for f in range(faces):
            other[:, f * nodes : (f + 1) * nodes] = -ones_table[g, ::-1, :].T
        parts.extend([other, other])
    surf = jnp.asarray(np.concatenate(parts, axis=1), jnp.bfloat16)
    return lift_t, deriv_t, surf


def stage_kernel(
    hbm_ref, left_ref, right_ref, met_ref, geo_ref, li_ref, nf_ref, lt_ref, dt_ref, sm_ref,
    out_ref, x_ref, s2_ref, s1_ref, z_ref, lth_ref, ltl_ref, dth_ref, dtl_ref, sem,
):
    for full_ref, hi_ref, lo_ref in ((lt_ref, lth_ref, ltl_ref), (dt_ref, dth_ref, dtl_ref)):
        full = full_ref[...]
        high = full.astype(jnp.bfloat16)
        hi_ref[...] = high
        lo_ref[...] = (full - high.astype(jnp.float32)).astype(jnp.bfloat16)
    elem_count = hbm_ref.shape[2]
    copy = pltpu.make_async_copy(hbm_ref, x_ref.at[:, :, HALO : HALO + elem_count], sem)
    copy.start()
    copy.wait()
    x_ref[:, :, 0:HALO] = left_ref[...]
    x_ref[:, :, HALO + elem_count : 2 * HALO + elem_count] = right_ref[...]
    fields, basis_count, width = x_ref.shape
    blocks = width // LANES
    split_rows = 2 * fields * ROWS
    z_ref[:, 0:LANES] = jnp.zeros((split_rows, LANES), jnp.bfloat16)
    z_ref[:, width + LANES : width + 2 * LANES] = jnp.zeros((split_rows, LANES), jnp.bfloat16)
    rowface = lax.broadcasted_iota(jnp.int32, (ROWS, LANES), 0) // (ORDER + 1)
    window = lax.broadcasted_iota(jnp.int32, (3 * LANES, LANES), 0)

    def dot3(hi_ref, lo_ref, b):
        b_high = b.astype(jnp.bfloat16)
        b_low = (b - b_high.astype(jnp.float32)).astype(jnp.bfloat16)
        a_high = hi_ref[...]
        return dot16(a_high, b_high) + dot16(a_high, b_low) + dot16(lo_ref[...], b_high)

    def dot16(a, b):
        return jnp.dot(a, b, preferred_element_type=jnp.float32)

    def run(src_ref, kind):
        def traces(b, carry):
            off = pl.multiple_of(b * LANES, LANES)
            lifted = [dot3(lth_ref, ltl_ref, src_ref[c, :, pl.ds(off, LANES)]) for c in range(fields)]
            half_scale = geo_ref[0, :, pl.ds(off, LANES)]
            normal_x = geo_ref[1, :, pl.ds(off, LANES)]
            normal_y = geo_ref[2, :, pl.ds(off, LANES)]
            height, along_x, along_y = lifted
            face_height = half_scale * (
                gravity * (normal_x * along_x + normal_y * along_y) - wave_speed * height
            )
            face_along_x = half_scale * (depth * normal_x * height - wave_speed * along_x)
            face_along_y = half_scale * (depth * normal_y * height - wave_speed * along_y)
            dst = pl.multiple_of(off + LANES, LANES)
            for c, value in enumerate((face_height, face_along_x, face_along_y)):
                high = value.astype(jnp.bfloat16)
                low = (value - high.astype(jnp.float32)).astype(jnp.bfloat16)
                z_ref[c * ROWS : (c + 1) * ROWS, pl.ds(dst, LANES)] = high
                z_ref[(fields + c) * ROWS : (fields + c + 1) * ROWS, pl.ds(dst, LANES)] = low
            return carry

        lax.fori_loop(0, blocks, traces, 0)

        def update(b, carry):
            off = pl.multiple_of(b * LANES, LANES)
            near = z_ref[:, pl.ds(off, 3 * LANES)]
            gathered = []
            for g in range(3):
                spot = li_ref[g : g + 1, pl.ds(off, LANES)] - (off - LANES)
                onehot = (window == spot).astype(jnp.bfloat16)
                across = nf_ref[g : g + 1, pl.ds(off, LANES)]
                picked = dot16(near, onehot)
                gathered.append((picked, rowface == across))
            m = met_ref[:, pl.ds(off, LANES)]
            m0, m1, m2, m3 = (m[k : k + 1] for k in range(4))
            cur = [src_ref[c, :, pl.ds(off, LANES)] for c in range(fields)]
            rs = [dot3(dth_ref, dtl_ref, cur[c]) for c in range(fields)]
            along_r = [v[0:basis_count] for v in rs]
            along_s = [v[72 : 72 + basis_count] for v in rs]
            volume = [
                -gravity * (m0 * along_r[1] + m1 * along_s[1] + m2 * along_r[2] + m3 * along_s[2]),
                -depth * (m0 * along_r[0] + m1 * along_s[0]),
                -depth * (m2 * along_r[0] + m3 * along_s[0]),
            ]
            here = pl.ds(pl.multiple_of(off + LANES, LANES), LANES)
            for c in range(fields):
                hi_rows = slice(c * ROWS, (c + 1) * ROWS)
                lo_rows = slice((fields + c) * ROWS, (fields + c + 1) * ROWS)
                pieces = [z_ref[hi_rows, here], z_ref[lo_rows, here]]
                for picked, mask in gathered:
                    for rows in (hi_rows, lo_rows):
                        pieces.append(jnp.where(mask, picked[rows], 0.0).astype(jnp.bfloat16))
                surface = dot16(sm_ref[...], jnp.concatenate(pieces, axis=0))
                new = cur[c] + time_step * (volume[c] + surface)
                if kind == 0:
                    s2_ref[c, :, pl.ds(off, LANES)] = 2.0 / 3.0 * new
                elif kind == 1:
                    s1_ref[c, :, pl.ds(off, LANES)] = 0.25 * new
                else:
                    dst = pl.multiple_of(off - LANES, LANES)
                    out_ref[c, :, pl.ds(dst, LANES)] = (
                        x_ref[c, :, pl.ds(off, LANES)] / 3.0 + 0.75 * s2_ref[c, :, pl.ds(off, LANES)] + new
                    )
            return carry

        if kind == 2:
            lax.fori_loop(1, blocks - 1, update, 0)
        else:
            lax.fori_loop(0, blocks, update, 0)

    run(x_ref, 0)
    run(s2_ref, 1)
    run(s1_ref, 2)


def body(
    adjoint,
    deriv_r,
    deriv_s,
    lift,
    metric,
    face_scale,
    face_angle,
    neighbours,
    neighbour_face,
    remap_table,
    intersection_elem,
    intersection_old,
    intersection_weight,
    block_type,
):
    fields, basis_count, elem_count = adjoint.shape
    nodes = ORDER + 1
    devices = lax.axis_size(AXES)
    elem_total = elem_count * devices
    first_elem = lax.axis_index(AXES) * elem_count
    width = elem_count + 2 * HALO

    count = lax.axis_size(AXES)
    left = lax.ppermute(adjoint[:, :, elem_count - HALO :], AXES, [(i, (i + 1) % count) for i in range(count)])
    right = lax.ppermute(adjoint[:, :, :HALO], AXES, [((i + 1) % count, i) for i in range(count)])
    params = extended(jnp.concatenate([metric, face_scale, face_angle], axis=0), HALO, axis=1)
    links = extended(jnp.concatenate([neighbours, neighbour_face], axis=0), HALO, axis=1)
    met = params[0:4]
    half_scale = 0.5 * params[4:7]
    angle = params[7:10]

    def spread(v):
        rows = jnp.repeat(v, nodes, axis=0)
        return jnp.concatenate([rows, jnp.zeros((ROWS - 3 * nodes, width), jnp.float32)], axis=0)

    geo = jnp.stack([spread(half_scale), spread(jnp.cos(angle)), spread(jnp.sin(angle))])
    local_index = (links[0:3] - first_elem + HALO + elem_total) % elem_total
    local_index = jnp.clip(local_index, 0, width - 1)
    across_face = links[3:6]
    lift_t, deriv_t, surf = stage_tables(deriv_r, deriv_s, lift, ORDER)
    vmem = pl.BlockSpec(memory_space=pltpu.VMEM)
    adj_new = pl.pallas_call(
        stage_kernel,
        out_shape=jax.ShapeDtypeStruct((fields, basis_count, elem_count), jnp.float32),
        in_specs=[pl.BlockSpec(memory_space=pl.ANY)] + [vmem] * 9,
        out_specs=vmem,
        scratch_shapes=[
            pltpu.VMEM((fields, basis_count, width), jnp.float32),
            pltpu.VMEM((fields, basis_count, width), jnp.float32),
            pltpu.VMEM((fields, basis_count, width), jnp.float32),
            pltpu.VMEM((2 * fields * ROWS, width + 2 * LANES), jnp.bfloat16),
            pltpu.VMEM((ROWS, basis_count), jnp.bfloat16),
            pltpu.VMEM((ROWS, basis_count), jnp.bfloat16),
            pltpu.VMEM((144, basis_count), jnp.bfloat16),
            pltpu.VMEM((144, basis_count), jnp.bfloat16),
            pltpu.SemaphoreType.DMA(()),
        ],
        compiler_params=pltpu.CompilerParams(vmem_limit_bytes=56 * 1024 * 1024),
    )(adjoint, left, right, met, geo, local_index, across_face, lift_t, deriv_t, surf)
    adj_rows = adj_new.reshape(fields * basis_count, elem_count).T

    rows_here = intersection_elem.shape[0]
    block_here = rows_here // BLOCK
    field_rows = fields * basis_count
    picked = jnp.take(adj_rows, intersection_elem, axis=0, mode="clip")
    picked = picked.reshape(block_here, BLOCK, field_rows)
    chosen = jnp.take(remap_table, block_type, axis=0)
    eye = jnp.eye(fields, dtype=jnp.float32)
    spread_table = (eye[None, :, None, :, None] * chosen[:, None, :, None, :]).reshape(
        block_here, field_rows, field_rows
    )
    mapped = jnp.einsum("brk,bkj->brj", picked, spread_table, precision=highest)
    mapped = mapped * intersection_weight.reshape(block_here, BLOCK, 1)
    mapped = mapped.reshape(rows_here, field_rows)
    labelled = jnp.concatenate(
        [mapped, intersection_old.astype(jnp.float32)[:, None]], axis=1
    )
    bounds = group_bounds(rows_here, REACH)
    old_count = E_OLD_DEV
    old_iota = jnp.arange(old_count, dtype=jnp.int32)[:, None]

    def scatter(rows):
        labels = rows[:, field_rows].astype(jnp.int32)
        return split_dot(old_iota == labels[None, :], rows[:, :field_rows])

    moved = []
    for offset, start_row, group_size in bounds:
        piece = labelled[start_row : start_row + group_size]
        if offset == 0:
            home = piece
        else:
            moved.append(shifted(piece, offset))
    old_sums = scatter(home) + scatter(jnp.concatenate(moved, axis=0))
    return (adj_new, old_sums.T.reshape(fields, basis_count, old_count))


def solution(mesh):
    in_specs = (
        P(None, None, AXES),
        P(),
        P(),
        P(),
        P(None, AXES),
        P(None, AXES),
        P(None, AXES),
        P(None, AXES),
        P(None, AXES),
        P(),
        P(AXES),
        P(AXES),
        P(AXES),
        P(AXES),
    )
    out_specs = (P(None, None, AXES), P(None, None, AXES))
    return jax.shard_map(body, mesh=mesh, in_specs=in_specs, out_specs=out_specs, check_vma=False)
```

```python
import jax
import jax.numpy as jnp
import numpy as np
from jax import lax
from jax.experimental import pallas as pl
from jax.experimental.pallas import tpu as pltpu
from jax.sharding import PartitionSpec as P

ORDER = 10
REACH = 4
BLOCK = 128
RIM = 32
HALO = 128
E_OLD_DEV = 2048

gravity = 2.0
depth = 0.5
wave_speed = 1.0
time_step = 0.04
highest = lax.Precision.HIGHEST
AXES = ("gx", "gy")


def extended(cells, width, axis=0):
    count = lax.axis_size(AXES)
    size = cells.shape[axis]
    head = lax.slice_in_dim(cells, 0, width, axis=axis)
    tail = lax.slice_in_dim(cells, size - width, size, axis=axis)
    return jnp.concatenate(
        [
            lax.ppermute(tail, AXES, [(i, (i + 1) % count) for i in range(count)]),
            cells,
            lax.ppermute(head, AXES, [((i + 1) % count, i) for i in range(count)]),
        ],
        axis=axis,
    )


def shifted(shard, by):
    length = lax.axis_size(AXES)
    return lax.ppermute(shard, AXES, [(i, (i + by) % length) for i in range(length)])


def face_table(degree):
    basis_count = (degree + 1) * (degree + 2) // 2

    def node_place(column, level):
        return level * (degree + 1) - level * (level - 1) // 2 + column

    ones_table = np.zeros((3, degree + 1, basis_count), np.float32)
    for level in range(degree + 1):
        ones_table[0, level, node_place(level, 0)] = 1.0
        ones_table[1, level, node_place(degree - level, level)] = 1.0
        ones_table[2, level, node_place(0, degree - level)] = 1.0
    return ones_table


def surface_matrix(degree):
    ones_table = face_table(degree)
    faces, nodes, basis_count = ones_table.shape
    own = ones_table.reshape(faces * nodes, basis_count)
    other = -ones_table[:, ::-1, :].reshape(faces * nodes, basis_count)
    return jnp.asarray(np.concatenate([own, other], axis=0))


def group_bounds(q_rows, reach):
    cap_far = q_rows // 32
    cap_near = q_rows // 8
    cap_home = q_rows - 2 * cap_near - 2 * (reach - 1) * cap_far
    bounds = []
    start = 0
    for offset in range(-reach, reach + 1):
        if offset == 0:
            group_size = cap_home
        elif abs(offset) == 1:
            group_size = cap_near
        else:
            group_size = cap_far
        bounds.append((offset, start, group_size))
        start = start + group_size
    return bounds


def split_dot(onehot, values):
    return jnp.dot(onehot.astype(jnp.float32), values, precision=lax.Precision.HIGH)


LANES = 128
ROWS = 48


def stage_tables(deriv_r, deriv_s, lift, degree):
    basis_count = deriv_r.shape[0]
    nodes = degree + 1
    lift_t = jnp.zeros((ROWS, basis_count), jnp.float32).at[: 3 * nodes].set(lift.T)
    deriv_t = jnp.zeros((144, basis_count), jnp.float32)
    deriv_t = deriv_t.at[:basis_count].set(deriv_r.T).at[72 : 72 + basis_count].set(deriv_s.T)
    ones_table = face_table(degree)
    faces = ones_table.shape[0]
    own = np.zeros((basis_count, ROWS), np.float32)
    own[:, : faces * nodes] = ones_table.reshape(faces * nodes, basis_count).T
    parts = [own, own]
    for g in range(faces):
        other = np.zeros((basis_count, ROWS), np.float32)
        for f in range(faces):
            other[:, f * nodes : (f + 1) * nodes] = -ones_table[g, ::-1, :].T
        parts.extend([other, other])
    surf = jnp.asarray(np.concatenate(parts, axis=1), jnp.bfloat16)
    return lift_t, deriv_t, surf


def stage_kernel(
    hbm_ref, left_ref, right_ref, met_ref, geo_ref, li_ref, nf_ref, lt_ref, dt_ref, sm_ref,
    out_ref, x_ref, s2_ref, s1_ref, z_ref, oh_ref, sem,
):
    elem_count = hbm_ref.shape[2]
    copy = pltpu.make_async_copy(hbm_ref, x_ref.at[:, :, HALO : HALO + elem_count], sem)
    copy.start()
    copy.wait()
    x_ref[:, :, 0:HALO] = left_ref[...]
    x_ref[:, :, HALO + elem_count : 2 * HALO + elem_count] = right_ref[...]
    fields, basis_count, width = x_ref.shape
    blocks = width // LANES
    split_rows = 2 * fields * ROWS
    z_ref[:, 0:LANES] = jnp.zeros((split_rows, LANES), jnp.bfloat16)
    z_ref[:, width + LANES : width + 2 * LANES] = jnp.zeros((split_rows, LANES), jnp.bfloat16)
    rowface = lax.broadcasted_iota(jnp.int32, (ROWS, LANES), 0) // (ORDER + 1)
    window = lax.broadcasted_iota(jnp.int32, (3 * LANES, LANES), 0)

    def build(b, carry):
        off = pl.multiple_of(b * LANES, LANES)
        for g in range(3):
            spot = li_ref[g : g + 1, pl.ds(off, LANES)] - (off - LANES)
            oh_ref[g * blocks + b] = (window == spot).astype(jnp.bfloat16)
        return carry

    lax.fori_loop(0, blocks, build, 0)

    def dot(a, b):
        return jnp.dot(a, b, precision=highest, preferred_element_type=jnp.float32)

    def dot16(a, b):
        return jnp.dot(a, b, preferred_element_type=jnp.float32)

    def run(src_ref, kind):
        def traces(b, carry):
            off = pl.multiple_of(b * LANES, LANES)
            lifted = [dot(lt_ref[...], src_ref[c, :, pl.ds(off, LANES)]) for c in range(fields)]
            half_scale = geo_ref[0, :, pl.ds(off, LANES)]
            normal_x = geo_ref[1, :, pl.ds(off, LANES)]
            normal_y = geo_ref[2, :, pl.ds(off, LANES)]
            height, along_x, along_y = lifted
            face_height = half_scale * (
                gravity * (normal_x * along_x + normal_y * along_y) - wave_speed * height
            )
            face_along_x = half_scale * (depth * normal_x * height - wave_speed * along_x)
            face_along_y = half_scale * (depth * normal_y * height - wave_speed * along_y)
            dst = pl.multiple_of(off + LANES, LANES)
            for c, value in enumerate((face_height, face_along_x, face_along_y)):
                high = value.astype(jnp.bfloat16)
                low = (value - high.astype(jnp.float32)).astype(jnp.bfloat16)
                z_ref[c * ROWS : (c + 1) * ROWS, pl.ds(dst, LANES)] = high
                z_ref[(fields + c) * ROWS : (fields + c + 1) * ROWS, pl.ds(dst, LANES)] = low
            return carry

        lax.fori_loop(0, blocks, traces, 0)

        def update(b, carry):
            off = pl.multiple_of(b * LANES, LANES)
            near = z_ref[:, pl.ds(off, 3 * LANES)]
            gathered = []
            for g in range(3):
                onehot = oh_ref[g * blocks + b]
                across = nf_ref[g : g + 1, pl.ds(off, LANES)]
                picked = dot16(near, onehot)
                gathered.append((picked, rowface == across))
            m = met_ref[:, pl.ds(off, LANES)]
            m0, m1, m2, m3 = (m[k : k + 1] for k in range(4))
            cur = [src_ref[c, :, pl.ds(off, LANES)] for c in range(fields)]
            rs = [dot(dt_ref[...], cur[c]) for c in range(fields)]
            along_r = [v[0:basis_count] for v in rs]
            along_s = [v[72 : 72 + basis_count] for v in rs]
            volume = [
                -gravity * (m0 * along_r[1] + m1 * along_s[1] + m2 * along_r[2] + m3 * along_s[2]),
                -depth * (m0 * along_r[0] + m1 * along_s[0]),
                -depth * (m2 * along_r[0] + m3 * along_s[0]),
            ]
            here = pl.ds(pl.multiple_of(off + LANES, LANES), LANES)
            for c in range(fields):
                hi_rows = slice(c * ROWS, (c + 1) * ROWS)
                lo_rows = slice((fields + c) * ROWS, (fields + c + 1) * ROWS)
                pieces = [z_ref[hi_rows, here], z_ref[lo_rows, here]]
                for picked, mask in gathered:
                    for rows in (hi_rows, lo_rows):
                        pieces.append(jnp.where(mask, picked[rows], 0.0).astype(jnp.bfloat16))
                surface = dot16(sm_ref[...], jnp.concatenate(pieces, axis=0))
                new = cur[c] + time_step * (volume[c] + surface)
                if kind == 0:
                    s2_ref[c, :, pl.ds(off, LANES)] = 2.0 / 3.0 * new
                elif kind == 1:
                    s1_ref[c, :, pl.ds(off, LANES)] = 0.25 * new
                else:
                    dst = pl.multiple_of(off - LANES, LANES)
                    out_ref[c, :, pl.ds(dst, LANES)] = (
                        x_ref[c, :, pl.ds(off, LANES)] / 3.0 + 0.75 * s2_ref[c, :, pl.ds(off, LANES)] + new
                    )
            return carry

        if kind == 2:
            lax.fori_loop(1, blocks - 1, update, 0)
        else:
            lax.fori_loop(0, blocks, update, 0)

    run(x_ref, 0)
    run(s2_ref, 1)
    run(s1_ref, 2)


def body(
    adjoint,
    deriv_r,
    deriv_s,
    lift,
    metric,
    face_scale,
    face_angle,
    neighbours,
    neighbour_face,
    remap_table,
    intersection_elem,
    intersection_old,
    intersection_weight,
    block_type,
):
    fields, basis_count, elem_count = adjoint.shape
    nodes = ORDER + 1
    devices = lax.axis_size(AXES)
    elem_total = elem_count * devices
    first_elem = lax.axis_index(AXES) * elem_count
    width = elem_count + 2 * HALO

    count = lax.axis_size(AXES)
    left = lax.ppermute(adjoint[:, :, elem_count - HALO :], AXES, [(i, (i + 1) % count) for i in range(count)])
    right = lax.ppermute(adjoint[:, :, :HALO], AXES, [((i + 1) % count, i) for i in range(count)])
    params = extended(jnp.concatenate([metric, face_scale, face_angle], axis=0), HALO, axis=1)
    links = extended(jnp.concatenate([neighbours, neighbour_face], axis=0), HALO, axis=1)
    met = params[0:4]
    half_scale = 0.5 * params[4:7]
    angle = params[7:10]

    def spread(v):
        rows = jnp.repeat(v, nodes, axis=0)
        return jnp.concatenate([rows, jnp.zeros((ROWS - 3 * nodes, width), jnp.float32)], axis=0)

    geo = jnp.stack([spread(half_scale), spread(jnp.cos(angle)), spread(jnp.sin(angle))])
    local_index = (links[0:3] - first_elem + HALO + elem_total) % elem_total
    local_index = jnp.clip(local_index, 0, width - 1)
    across_face = links[3:6]
    lift_t, deriv_t, surf = stage_tables(deriv_r, deriv_s, lift, ORDER)
    vmem = pl.BlockSpec(memory_space=pltpu.VMEM)
    adj_new = pl.pallas_call(
        stage_kernel,
        out_shape=jax.ShapeDtypeStruct((fields, basis_count, elem_count), jnp.float32),
        in_specs=[pl.BlockSpec(memory_space=pl.ANY)] + [vmem] * 9,
        out_specs=vmem,
        scratch_shapes=[
            pltpu.VMEM((fields, basis_count, width), jnp.float32),
            pltpu.VMEM((fields, basis_count, width), jnp.float32),
            pltpu.VMEM((fields, basis_count, width), jnp.float32),
            pltpu.VMEM((2 * fields * ROWS, width + 2 * LANES), jnp.bfloat16),
            pltpu.VMEM((3 * (width // LANES), 3 * LANES, LANES), jnp.bfloat16),
            pltpu.SemaphoreType.DMA(()),
        ],
        compiler_params=pltpu.CompilerParams(vmem_limit_bytes=56 * 1024 * 1024),
    )(adjoint, left, right, met, geo, local_index, across_face, lift_t, deriv_t, surf)
    adj_rows = adj_new.reshape(fields * basis_count, elem_count).T

    rows_here = intersection_elem.shape[0]
    block_here = rows_here // BLOCK
    field_rows = fields * basis_count
    picked = jnp.take(adj_rows, intersection_elem, axis=0, mode="clip")
    picked = picked.reshape(block_here, BLOCK, fields, basis_count)
    chosen = jnp.take(remap_table, block_type, axis=0)
    mapped = jnp.einsum("brci,bij->brcj", picked, chosen, precision=highest)
    mapped = mapped * intersection_weight.reshape(block_here, BLOCK, 1, 1)
    mapped = mapped.reshape(rows_here, field_rows)
    labelled = jnp.concatenate(
        [mapped, intersection_old.astype(jnp.float32)[:, None]], axis=1
    )
    bounds = group_bounds(rows_here, REACH)
    old_count = E_OLD_DEV
    old_iota = jnp.arange(old_count, dtype=jnp.int32)[:, None]

    def scatter(rows):
        labels = rows[:, field_rows].astype(jnp.int32)
        return split_dot(old_iota == labels[None, :], rows[:, :field_rows])

    moved = []
    for offset, start_row, group_size in bounds:
        piece = labelled[start_row : start_row + group_size]
        if offset == 0:
            home = piece
        else:
            moved.append(shifted(piece, offset))
    old_sums = scatter(home) + scatter(jnp.concatenate(moved, axis=0))
    return (adj_new, old_sums.T.reshape(fields, basis_count, old_count))


def solution(mesh):
    in_specs = (
        P(None, None, AXES),
        P(),
        P(),
        P(),
        P(None, AXES),
        P(None, AXES),
        P(None, AXES),
        P(None, AXES),
        P(None, AXES),
        P(),
        P(AXES),
        P(AXES),
        P(AXES),
        P(AXES),
    )
    out_specs = (P(None, None, AXES), P(None, None, AXES))
    return jax.shard_map(body, mesh=mesh, in_specs=in_specs, out_specs=out_specs, check_vma=False)
```

```python
import jax
import jax.numpy as jnp
import numpy as np
from jax import lax
from jax.experimental import pallas as pl
from jax.experimental.pallas import tpu as pltpu
from jax.sharding import PartitionSpec as P

ORDER = 10
REACH = 4
BLOCK = 128
RIM = 32
HALO = 128
E_OLD_DEV = 2048

gravity = 2.0
depth = 0.5
wave_speed = 1.0
time_step = 0.04
highest = lax.Precision.HIGHEST
AXES = ("gx", "gy")


def extended(cells, width, axis=0):
    count = lax.axis_size(AXES)
    size = cells.shape[axis]
    head = lax.slice_in_dim(cells, 0, width, axis=axis)
    tail = lax.slice_in_dim(cells, size - width, size, axis=axis)
    return jnp.concatenate(
        [
            lax.ppermute(tail, AXES, [(i, (i + 1) % count) for i in range(count)]),
            cells,
            lax.ppermute(head, AXES, [((i + 1) % count, i) for i in range(count)]),
        ],
        axis=axis,
    )


def shifted(shard, by):
    length = lax.axis_size(AXES)
    return lax.ppermute(shard, AXES, [(i, (i + by) % length) for i in range(length)])


def face_table(degree):
    basis_count = (degree + 1) * (degree + 2) // 2

    def node_place(column, level):
        return level * (degree + 1) - level * (level - 1) // 2 + column

    ones_table = np.zeros((3, degree + 1, basis_count), np.float32)
    for level in range(degree + 1):
        ones_table[0, level, node_place(level, 0)] = 1.0
        ones_table[1, level, node_place(degree - level, level)] = 1.0
        ones_table[2, level, node_place(0, degree - level)] = 1.0
    return ones_table


def surface_matrix(degree):
    ones_table = face_table(degree)
    faces, nodes, basis_count = ones_table.shape
    own = ones_table.reshape(faces * nodes, basis_count)
    other = -ones_table[:, ::-1, :].reshape(faces * nodes, basis_count)
    return jnp.asarray(np.concatenate([own, other], axis=0))


def group_bounds(q_rows, reach):
    cap_far = q_rows // 32
    cap_near = q_rows // 8
    cap_home = q_rows - 2 * cap_near - 2 * (reach - 1) * cap_far
    bounds = []
    start = 0
    for offset in range(-reach, reach + 1):
        if offset == 0:
            group_size = cap_home
        elif abs(offset) == 1:
            group_size = cap_near
        else:
            group_size = cap_far
        bounds.append((offset, start, group_size))
        start = start + group_size
    return bounds


def split_dot(onehot, values):
    return jnp.dot(onehot.astype(jnp.float32), values, precision=lax.Precision.HIGH)


LANES = 128
ROWS = 48


def stage_tables(deriv_r, deriv_s, lift, degree):
    basis_count = deriv_r.shape[0]
    nodes = degree + 1
    lift_t = jnp.zeros((ROWS, basis_count), jnp.float32).at[: 3 * nodes].set(lift.T)
    deriv_t = jnp.zeros((144, basis_count), jnp.float32)
    deriv_t = deriv_t.at[:basis_count].set(deriv_r.T).at[72 : 72 + basis_count].set(deriv_s.T)
    ones_table = face_table(degree)
    faces = ones_table.shape[0]
    own = np.zeros((basis_count, ROWS), np.float32)
    own[:, : faces * nodes] = ones_table.reshape(faces * nodes, basis_count).T
    parts = [np.concatenate([own, own], axis=1)]
    for g in range(faces):
        other = np.zeros((basis_count, ROWS), np.float32)
        for f in range(faces):
            other[:, f * nodes : (f + 1) * nodes] = -ones_table[g, ::-1, :].T
        parts.append(np.concatenate([other, other], axis=1))
    surf = jnp.asarray(np.stack(parts), jnp.bfloat16)
    return lift_t, deriv_t, surf


def stage_kernel(
    hbm_ref, left_ref, right_ref, met_ref, geo_ref, li_ref, nf_ref, lt_ref, dt_ref, sm_ref,
    out_ref, x_ref, s2_ref, s1_ref, z_ref, oh_ref, acc_ref, sem,
):
    elem_count = hbm_ref.shape[2]
    copy = pltpu.make_async_copy(hbm_ref, x_ref.at[:, :, HALO : HALO + elem_count], sem)
    copy.start()
    copy.wait()
    x_ref[:, :, 0:HALO] = left_ref[...]
    x_ref[:, :, HALO + elem_count : 2 * HALO + elem_count] = right_ref[...]
    fields, basis_count, width = x_ref.shape
    blocks = width // LANES
    split_rows = 2 * fields * ROWS
    z_ref[:, 0:LANES] = jnp.zeros((split_rows, LANES), jnp.bfloat16)
    z_ref[:, width + LANES : width + 2 * LANES] = jnp.zeros((split_rows, LANES), jnp.bfloat16)
    rowface = lax.broadcasted_iota(jnp.int32, (2 * ROWS, LANES), 0) % ROWS // (ORDER + 1)
    window = lax.broadcasted_iota(jnp.int32, (3 * LANES, LANES), 0)

    def build(b, carry):
        off = pl.multiple_of(b * LANES, LANES)
        for g in range(3):
            spot = li_ref[g : g + 1, pl.ds(off, LANES)] - (off - LANES)
            oh_ref[g * blocks + b] = (window == spot).astype(jnp.bfloat16)
        return carry

    lax.fori_loop(0, blocks, build, 0)

    def dot(a, b):
        return jnp.dot(a, b, precision=highest, preferred_element_type=jnp.float32)

    def dot16(a, b):
        return jnp.dot(a, b, preferred_element_type=jnp.float32)

    def run(src_ref, kind):
        def traces(b, carry):
            off = pl.multiple_of(b * LANES, LANES)
            lifted = [dot(lt_ref[...], src_ref[c, :, pl.ds(off, LANES)]) for c in range(fields)]
            half_scale = geo_ref[0, :, pl.ds(off, LANES)]
            normal_x = geo_ref[1, :, pl.ds(off, LANES)]
            normal_y = geo_ref[2, :, pl.ds(off, LANES)]
            height, along_x, along_y = lifted
            face_height = half_scale * (
                gravity * (normal_x * along_x + normal_y * along_y) - wave_speed * height
            )
            face_along_x = half_scale * (depth * normal_x * height - wave_speed * along_x)
            face_along_y = half_scale * (depth * normal_y * height - wave_speed * along_y)
            dst = pl.multiple_of(off + LANES, LANES)
            for c, value in enumerate((face_height, face_along_x, face_along_y)):
                high = value.astype(jnp.bfloat16)
                low = (value - high.astype(jnp.float32)).astype(jnp.bfloat16)
                z_ref[2 * c * ROWS : (2 * c + 1) * ROWS, pl.ds(dst, LANES)] = high
                z_ref[(2 * c + 1) * ROWS : (2 * c + 2) * ROWS, pl.ds(dst, LANES)] = low
            return carry

        lax.fori_loop(0, blocks, traces, 0)

        def update(b, carry):
            off = pl.multiple_of(b * LANES, LANES)
            lanes = pl.ds(off, LANES)
            here = pl.ds(pl.multiple_of(off + LANES, LANES), LANES)
            m = met_ref[:, lanes]
            m0, m1, m2, m3 = (m[k : k + 1] for k in range(4))
            rs = dot(dt_ref[...], src_ref[0, :, lanes])
            along_r, along_s = rs[0:basis_count], rs[72 : 72 + basis_count]
            acc_ref[1] = -depth * (m0 * along_r + m1 * along_s)
            acc_ref[2] = -depth * (m2 * along_r + m3 * along_s)
            rs1 = dot(dt_ref[...], src_ref[1, :, lanes])
            rs2 = dot(dt_ref[...], src_ref[2, :, lanes])
            acc_ref[0] = -gravity * (
                m0 * rs1[0:basis_count] + m1 * rs1[72 : 72 + basis_count]
                + m2 * rs2[0:basis_count] + m3 * rs2[72 : 72 + basis_count]
            )
            own_table = sm_ref[0]
            for c in range(fields):
                rows = slice(2 * c * ROWS, (2 * c + 2) * ROWS)
                acc_ref[c] += dot16(own_table, z_ref[rows, here])
            for g in range(3):
                picked = dot16(z_ref[:, pl.ds(off, 3 * LANES)], oh_ref[g * blocks + b])
                mask = rowface == nf_ref[g : g + 1, lanes]
                table = sm_ref[g + 1]
                for c in range(fields):
                    rows = slice(2 * c * ROWS, (2 * c + 2) * ROWS)
                    outside = jnp.where(mask, picked[rows], 0.0).astype(jnp.bfloat16)
                    acc_ref[c] += dot16(table, outside)
            for c in range(fields):
                new = src_ref[c, :, lanes] + time_step * acc_ref[c]
                if kind == 0:
                    s2_ref[c, :, lanes] = 2.0 / 3.0 * new
                elif kind == 1:
                    s1_ref[c, :, lanes] = 0.25 * new
                else:
                    dst = pl.multiple_of(off - LANES, LANES)
                    out_ref[c, :, pl.ds(dst, LANES)] = (
                        x_ref[c, :, lanes] / 3.0 + 0.75 * s2_ref[c, :, lanes] + new
                    )
            return carry

        if kind == 2:
            lax.fori_loop(1, blocks - 1, update, 0)
        else:
            lax.fori_loop(0, blocks, update, 0)

    run(x_ref, 0)
    run(s2_ref, 1)
    run(s1_ref, 2)


def body(
    adjoint,
    deriv_r,
    deriv_s,
    lift,
    metric,
    face_scale,
    face_angle,
    neighbours,
    neighbour_face,
    remap_table,
    intersection_elem,
    intersection_old,
    intersection_weight,
    block_type,
):
    fields, basis_count, elem_count = adjoint.shape
    nodes = ORDER + 1
    devices = lax.axis_size(AXES)
    elem_total = elem_count * devices
    first_elem = lax.axis_index(AXES) * elem_count
    width = elem_count + 2 * HALO

    count = lax.axis_size(AXES)
    left = lax.ppermute(adjoint[:, :, elem_count - HALO :], AXES, [(i, (i + 1) % count) for i in range(count)])
    right = lax.ppermute(adjoint[:, :, :HALO], AXES, [((i + 1) % count, i) for i in range(count)])
    params = extended(jnp.concatenate([metric, face_scale, face_angle], axis=0), HALO, axis=1)
    links = extended(jnp.concatenate([neighbours, neighbour_face], axis=0), HALO, axis=1)
    met = params[0:4]
    half_scale = 0.5 * params[4:7]
    angle = params[7:10]

    def spread(v):
        rows = jnp.repeat(v, nodes, axis=0)
        return jnp.concatenate([rows, jnp.zeros((ROWS - 3 * nodes, width), jnp.float32)], axis=0)

    geo = jnp.stack([spread(half_scale), spread(jnp.cos(angle)), spread(jnp.sin(angle))])
    local_index = (links[0:3] - first_elem + HALO + elem_total) % elem_total
    local_index = jnp.clip(local_index, 0, width - 1)
    across_face = links[3:6]
    lift_t, deriv_t, surf = stage_tables(deriv_r, deriv_s, lift, ORDER)
    vmem = pl.BlockSpec(memory_space=pltpu.VMEM)
    adj_new = pl.pallas_call(
        stage_kernel,
        out_shape=jax.ShapeDtypeStruct((fields, basis_count, elem_count), jnp.float32),
        in_specs=[pl.BlockSpec(memory_space=pl.ANY)] + [vmem] * 9,
        out_specs=vmem,
        scratch_shapes=[
            pltpu.VMEM((fields, basis_count, width), jnp.float32),
            pltpu.VMEM((fields, basis_count, width), jnp.float32),
            pltpu.VMEM((fields, basis_count, width), jnp.float32),
            pltpu.VMEM((2 * fields * ROWS, width + 2 * LANES), jnp.bfloat16),
            pltpu.VMEM((3 * (width // LANES), 3 * LANES, LANES), jnp.bfloat16),
            pltpu.VMEM((fields, basis_count, LANES), jnp.float32),
            pltpu.SemaphoreType.DMA(()),
        ],
        compiler_params=pltpu.CompilerParams(vmem_limit_bytes=56 * 1024 * 1024),
    )(adjoint, left, right, met, geo, local_index, across_face, lift_t, deriv_t, surf)
    adj_rows = adj_new.reshape(fields * basis_count, elem_count).T

    rows_here = intersection_elem.shape[0]
    block_here = rows_here // BLOCK
    field_rows = fields * basis_count
    picked = jnp.take(adj_rows, intersection_elem, axis=0, mode="clip")
    picked = picked.reshape(block_here, BLOCK, fields, basis_count)
    chosen = jnp.take(remap_table, block_type, axis=0)
    mapped = jnp.einsum("brci,bij->brcj", picked, chosen, precision=highest)
    mapped = mapped * intersection_weight.reshape(block_here, BLOCK, 1, 1)
    mapped = mapped.reshape(rows_here, field_rows)
    labelled = jnp.concatenate(
        [mapped, intersection_old.astype(jnp.float32)[:, None]], axis=1
    )
    bounds = group_bounds(rows_here, REACH)
    old_count = E_OLD_DEV
    old_iota = jnp.arange(old_count, dtype=jnp.int32)[:, None]

    def scatter(rows):
        labels = rows[:, field_rows].astype(jnp.int32)
        return split_dot(old_iota == labels[None, :], rows[:, :field_rows])

    moved = []
    for offset, start_row, group_size in bounds:
        piece = labelled[start_row : start_row + group_size]
        if offset == 0:
            home = piece
        else:
            moved.append(shifted(piece, offset))
    old_sums = scatter(home) + scatter(jnp.concatenate(moved, axis=0))
    return (adj_new, old_sums.T.reshape(fields, basis_count, old_count))


def solution(mesh):
    in_specs = (
        P(None, None, AXES),
        P(),
        P(),
        P(),
        P(None, AXES),
        P(None, AXES),
        P(None, AXES),
        P(None, AXES),
        P(None, AXES),
        P(),
        P(AXES),
        P(AXES),
        P(AXES),
        P(AXES),
    )
    out_specs = (P(None, None, AXES), P(None, None, AXES))
    return jax.shard_map(body, mesh=mesh, in_specs=in_specs, out_specs=out_specs, check_vma=False)
```

```python
import jax
import jax.numpy as jnp
import numpy as np
from jax import lax
from jax.experimental import pallas as pl
from jax.experimental.pallas import tpu as pltpu
from jax.sharding import PartitionSpec as P

ORDER = 10
REACH = 4
BLOCK = 128
RIM = 32
HALO = 128
E_OLD_DEV = 2048

gravity = 2.0
depth = 0.5
wave_speed = 1.0
time_step = 0.04
highest = lax.Precision.HIGHEST
AXES = ("gx", "gy")


def extended(cells, width, axis=0):
    count = lax.axis_size(AXES)
    size = cells.shape[axis]
    head = lax.slice_in_dim(cells, 0, width, axis=axis)
    tail = lax.slice_in_dim(cells, size - width, size, axis=axis)
    return jnp.concatenate(
        [
            lax.ppermute(tail, AXES, [(i, (i + 1) % count) for i in range(count)]),
            cells,
            lax.ppermute(head, AXES, [((i + 1) % count, i) for i in range(count)]),
        ],
        axis=axis,
    )


def shifted(shard, by):
    length = lax.axis_size(AXES)
    return lax.ppermute(shard, AXES, [(i, (i + by) % length) for i in range(length)])


def face_table(degree):
    basis_count = (degree + 1) * (degree + 2) // 2

    def node_place(column, level):
        return level * (degree + 1) - level * (level - 1) // 2 + column

    ones_table = np.zeros((3, degree + 1, basis_count), np.float32)
    for level in range(degree + 1):
        ones_table[0, level, node_place(level, 0)] = 1.0
        ones_table[1, level, node_place(degree - level, level)] = 1.0
        ones_table[2, level, node_place(0, degree - level)] = 1.0
    return ones_table


def surface_matrix(degree):
    ones_table = face_table(degree)
    faces, nodes, basis_count = ones_table.shape
    own = ones_table.reshape(faces * nodes, basis_count)
    other = -ones_table[:, ::-1, :].reshape(faces * nodes, basis_count)
    return jnp.asarray(np.concatenate([own, other], axis=0))


def group_bounds(q_rows, reach):
    cap_far = q_rows // 32
    cap_near = q_rows // 8
    cap_home = q_rows - 2 * cap_near - 2 * (reach - 1) * cap_far
    bounds = []
    start = 0
    for offset in range(-reach, reach + 1):
        if offset == 0:
            group_size = cap_home
        elif abs(offset) == 1:
            group_size = cap_near
        else:
            group_size = cap_far
        bounds.append((offset, start, group_size))
        start = start + group_size
    return bounds


def split_dot(onehot, values):
    return jnp.dot(onehot.astype(jnp.float32), values, precision=lax.Precision.HIGH)


LANES = 128
ROWS = 48


def stage_tables(deriv_r, deriv_s, lift, degree):
    basis_count = deriv_r.shape[0]
    nodes = degree + 1
    lift_t = jnp.zeros((ROWS, basis_count), jnp.float32).at[: 3 * nodes].set(lift.T)
    deriv_t = jnp.zeros((144, basis_count), jnp.float32)
    deriv_t = deriv_t.at[:basis_count].set(deriv_r.T).at[72 : 72 + basis_count].set(deriv_s.T)
    ones_table = face_table(degree)
    faces = ones_table.shape[0]
    own = np.zeros((basis_count, ROWS), np.float32)
    own[:, : faces * nodes] = ones_table.reshape(faces * nodes, basis_count).T
    parts = [own, own]
    for g in range(faces):
        other = np.zeros((basis_count, ROWS), np.float32)
        for f in range(faces):
            other[:, f * nodes : (f + 1) * nodes] = -ones_table[g, ::-1, :].T
        parts.extend([other, other])
    surf = jnp.asarray(np.concatenate(parts, axis=1), jnp.bfloat16)
    return lift_t, deriv_t, surf


def stage_kernel(
    hbm_ref, left_ref, right_ref, met_ref, geo_ref, li_ref, nf_ref, lt_ref, dt_ref, sm_ref,
    out_ref, x_ref, s2_ref, s1_ref, z_ref, sem,
):
    elem_count = hbm_ref.shape[2]
    copy = pltpu.make_async_copy(hbm_ref, x_ref.at[:, :, HALO : HALO + elem_count], sem)
    copy.start()
    copy.wait()
    x_ref[:, :, 0:HALO] = left_ref[...]
    x_ref[:, :, HALO + elem_count : 2 * HALO + elem_count] = right_ref[...]
    fields, basis_count, width = x_ref.shape
    blocks = width // LANES
    split_rows = 2 * fields * ROWS
    z_ref[:, 0:LANES] = jnp.zeros((split_rows, LANES), jnp.bfloat16)
    z_ref[:, width + LANES : width + 2 * LANES] = jnp.zeros((split_rows, LANES), jnp.bfloat16)
    rowface = lax.broadcasted_iota(jnp.int32, (ROWS, LANES), 0) // (ORDER + 1)
    window = lax.broadcasted_iota(jnp.int32, (3 * LANES, LANES), 0)

    def dot(a, b):
        return jnp.dot(a, b, precision=highest, preferred_element_type=jnp.float32)

    def dot16(a, b):
        return jnp.dot(a, b, preferred_element_type=jnp.float32)

    def run(src_ref, kind):
        def traces(b, carry):
            off = pl.multiple_of(b * LANES, LANES)
            lifted = [dot(lt_ref[...], src_ref[c, :, pl.ds(off, LANES)]) for c in range(fields)]
            half_scale = geo_ref[0, :, pl.ds(off, LANES)]
            normal_x = geo_ref[1, :, pl.ds(off, LANES)]
            normal_y = geo_ref[2, :, pl.ds(off, LANES)]
            height, along_x, along_y = lifted
            face_height = half_scale * (
                gravity * (normal_x * along_x + normal_y * along_y) - wave_speed * height
            )
            face_along_x = half_scale * (depth * normal_x * height - wave_speed * along_x)
            face_along_y = half_scale * (depth * normal_y * height - wave_speed * along_y)
            dst = pl.multiple_of(off + LANES, LANES)
            for c, value in enumerate((face_height, face_along_x, face_along_y)):
                high = value.astype(jnp.bfloat16)
                low = (value - high.astype(jnp.float32)).astype(jnp.bfloat16)
                z_ref[c * ROWS : (c + 1) * ROWS, pl.ds(dst, LANES)] = high
                z_ref[(fields + c) * ROWS : (fields + c + 1) * ROWS, pl.ds(dst, LANES)] = low
            return carry

        lax.fori_loop(0, blocks, traces, 0)

        def update(b, carry):
            off = pl.multiple_of(b * LANES, LANES)
            near = z_ref[:, pl.ds(off, 3 * LANES)]
            gathered = []
            for g in range(3):
                spot = li_ref[g : g + 1, pl.ds(off, LANES)] - (off - LANES)
                onehot = (window == spot).astype(jnp.bfloat16)
                across = nf_ref[g : g + 1, pl.ds(off, LANES)]
                picked = dot16(near, onehot)
                gathered.append((picked, rowface == across))
            m = met_ref[:, pl.ds(off, LANES)]
            m0, m1, m2, m3 = (m[k : k + 1] for k in range(4))
            cur = [src_ref[c, :, pl.ds(off, LANES)] for c in range(fields)]
            rs = [dot(dt_ref[...], cur[c]) for c in range(fields)]
            along_r = [v[0:basis_count] for v in rs]
            along_s = [v[72 : 72 + basis_count] for v in rs]
            volume = [
                -gravity * (m0 * along_r[1] + m1 * along_s[1] + m2 * along_r[2] + m3 * along_s[2]),
                -depth * (m0 * along_r[0] + m1 * along_s[0]),
                -depth * (m2 * along_r[0] + m3 * along_s[0]),
            ]
            here = pl.ds(pl.multiple_of(off + LANES, LANES), LANES)
            for c in range(fields):
                hi_rows = slice(c * ROWS, (c + 1) * ROWS)
                lo_rows = slice((fields + c) * ROWS, (fields + c + 1) * ROWS)
                pieces = [z_ref[hi_rows, here], z_ref[lo_rows, here]]
                for picked, mask in gathered:
                    for rows in (hi_rows, lo_rows):
                        pieces.append(jnp.where(mask, picked[rows], 0.0).astype(jnp.bfloat16))
                surface = dot16(sm_ref[...], jnp.concatenate(pieces, axis=0))
                new = cur[c] + time_step * (volume[c] + surface)
                if kind == 0:
                    s2_ref[c, :, pl.ds(off, LANES)] = 2.0 / 3.0 * new
                elif kind == 1:
                    s1_ref[c, :, pl.ds(off, LANES)] = 0.25 * new
                else:
                    dst = pl.multiple_of(off - LANES, LANES)
                    out_ref[c, :, pl.ds(dst, LANES)] = (
                        x_ref[c, :, pl.ds(off, LANES)] / 3.0 + 0.75 * s2_ref[c, :, pl.ds(off, LANES)] + new
                    )
            return carry

        if kind == 2:
            lax.fori_loop(1, blocks - 1, update, 0)
        else:
            lax.fori_loop(0, blocks, update, 0)

    run(x_ref, 0)
    run(s2_ref, 1)
    run(s1_ref, 2)


def body(
    adjoint,
    deriv_r,
    deriv_s,
    lift,
    metric,
    face_scale,
    face_angle,
    neighbours,
    neighbour_face,
    remap_table,
    intersection_elem,
    intersection_old,
    intersection_weight,
    block_type,
):
    fields, basis_count, elem_count = adjoint.shape
    nodes = ORDER + 1
    devices = lax.axis_size(AXES)
    elem_total = elem_count * devices
    first_elem = lax.axis_index(AXES) * elem_count
    width = elem_count + 2 * HALO

    count = lax.axis_size(AXES)
    left = lax.ppermute(adjoint[:, :, elem_count - HALO :], AXES, [(i, (i + 1) % count) for i in range(count)])
    right = lax.ppermute(adjoint[:, :, :HALO], AXES, [((i + 1) % count, i) for i in range(count)])
    params = extended(jnp.concatenate([metric, face_scale, face_angle], axis=0), HALO, axis=1)
    links = extended(jnp.concatenate([neighbours, neighbour_face], axis=0), HALO, axis=1)
    met = params[0:4]
    half_scale = 0.5 * params[4:7]
    angle = params[7:10]

    def spread(v):
        rows = jnp.broadcast_to(v[:, None, :], (v.shape[0], nodes, width)).reshape(-1, width)
        return jnp.concatenate([rows, jnp.zeros((ROWS - 3 * nodes, width), jnp.float32)], axis=0)

    geo = jnp.stack([spread(half_scale), spread(jnp.cos(angle)), spread(jnp.sin(angle))])
    local_index = (links[0:3] - first_elem + HALO + elem_total) % elem_total
    local_index = jnp.clip(local_index, 0, width - 1)
    across_face = links[3:6]
    lift_t, deriv_t, surf = stage_tables(deriv_r, deriv_s, lift, ORDER)
    vmem = pl.BlockSpec(memory_space=pltpu.VMEM)
    adj_new = pl.pallas_call(
        stage_kernel,
        out_shape=jax.ShapeDtypeStruct((fields, basis_count, elem_count), jnp.float32),
        in_specs=[pl.BlockSpec(memory_space=pl.ANY)] + [vmem] * 9,
        out_specs=vmem,
        scratch_shapes=[
            pltpu.VMEM((fields, basis_count, width), jnp.float32),
            pltpu.VMEM((fields, basis_count, width), jnp.float32),
            pltpu.VMEM((fields, basis_count, width), jnp.float32),
            pltpu.VMEM((2 * fields * ROWS, width + 2 * LANES), jnp.bfloat16),
            pltpu.SemaphoreType.DMA(()),
        ],
        compiler_params=pltpu.CompilerParams(vmem_limit_bytes=56 * 1024 * 1024),
    )(adjoint, left, right, met, geo, local_index, across_face, lift_t, deriv_t, surf)
    adj_rows = adj_new.reshape(fields * basis_count, elem_count).T

    rows_here = intersection_elem.shape[0]
    block_here = rows_here // BLOCK
    field_rows = fields * basis_count
    picked = jnp.take(adj_rows, intersection_elem, axis=0, mode="clip")
    chosen = jnp.take(remap_table, block_type, axis=0)

    def remap_kernel(p_ref, t_ref, w_ref, lab_ref, o_ref):
        table = t_ref[0]
        weight = w_ref[...]
        for c in range(fields):
            part = jnp.dot(
                p_ref[:, c * basis_count : (c + 1) * basis_count], table,
                precision=highest, preferred_element_type=jnp.float32,
            )
            o_ref[:, c * basis_count : (c + 1) * basis_count] = part * weight
        o_ref[:, field_rows : field_rows + 1] = lab_ref[...].astype(jnp.float32)

    labelled = pl.pallas_call(
        remap_kernel,
        grid=(block_here,),
        in_specs=[
            pl.BlockSpec((BLOCK, field_rows), lambda b: (b, 0)),
            pl.BlockSpec((1, basis_count, basis_count), lambda b: (b, 0, 0)),
            pl.BlockSpec((BLOCK, 1), lambda b: (b, 0)),
            pl.BlockSpec((BLOCK, 1), lambda b: (b, 0)),
        ],
        out_specs=pl.BlockSpec((BLOCK, field_rows + 1), lambda b: (b, 0)),
        out_shape=jax.ShapeDtypeStruct((rows_here, field_rows + 1), jnp.float32),
    )(picked, chosen, intersection_weight[:, None], intersection_old[:, None])
    bounds = group_bounds(rows_here, REACH)
    old_count = E_OLD_DEV
    old_iota = jnp.arange(old_count, dtype=jnp.int32)[:, None]

    def scatter(rows):
        labels = rows[:, field_rows].astype(jnp.int32)
        return split_dot(old_iota == labels[None, :], rows[:, :field_rows])

    moved = []
    for offset, start_row, group_size in bounds:
        piece = labelled[start_row : start_row + group_size]
        if offset == 0:
            home = piece
        else:
            moved.append(shifted(piece, offset))
    old_sums = scatter(home) + scatter(jnp.concatenate(moved, axis=0))
    return (adj_new, old_sums.T.reshape(fields, basis_count, old_count))


def solution(mesh):
    in_specs = (
        P(None, None, AXES),
        P(),
        P(),
        P(),
        P(None, AXES),
        P(None, AXES),
        P(None, AXES),
        P(None, AXES),
        P(None, AXES),
        P(),
        P(AXES),
        P(AXES),
        P(AXES),
        P(AXES),
    )
    out_specs = (P(None, None, AXES), P(None, None, AXES))
    return jax.shard_map(body, mesh=mesh, in_specs=in_specs, out_specs=out_specs, check_vma=False)
```

```python
import jax
import jax.numpy as jnp
import numpy as np
from jax import lax
from jax.experimental import pallas as pl
from jax.experimental.pallas import tpu as pltpu
from jax.sharding import PartitionSpec as P

ORDER = 10
REACH = 4
BLOCK = 128
RIM = 32
HALO = 128
E_OLD_DEV = 2048

gravity = 2.0
depth = 0.5
wave_speed = 1.0
time_step = 0.04
highest = lax.Precision.HIGHEST
AXES = ("gx", "gy")


def extended(cells, width, axis=0):
    count = lax.axis_size(AXES)
    size = cells.shape[axis]
    head = lax.slice_in_dim(cells, 0, width, axis=axis)
    tail = lax.slice_in_dim(cells, size - width, size, axis=axis)
    return jnp.concatenate(
        [
            lax.ppermute(tail, AXES, [(i, (i + 1) % count) for i in range(count)]),
            cells,
            lax.ppermute(head, AXES, [((i + 1) % count, i) for i in range(count)]),
        ],
        axis=axis,
    )


def shifted(shard, by):
    length = lax.axis_size(AXES)
    return lax.ppermute(shard, AXES, [(i, (i + by) % length) for i in range(length)])


def face_table(degree):
    basis_count = (degree + 1) * (degree + 2) // 2

    def node_place(column, level):
        return level * (degree + 1) - level * (level - 1) // 2 + column

    ones_table = np.zeros((3, degree + 1, basis_count), np.float32)
    for level in range(degree + 1):
        ones_table[0, level, node_place(level, 0)] = 1.0
        ones_table[1, level, node_place(degree - level, level)] = 1.0
        ones_table[2, level, node_place(0, degree - level)] = 1.0
    return ones_table


def surface_matrix(degree):
    ones_table = face_table(degree)
    faces, nodes, basis_count = ones_table.shape
    own = ones_table.reshape(faces * nodes, basis_count)
    other = -ones_table[:, ::-1, :].reshape(faces * nodes, basis_count)
    return jnp.asarray(np.concatenate([own, other], axis=0))


def group_bounds(q_rows, reach):
    cap_far = q_rows // 32
    cap_near = q_rows // 8
    cap_home = q_rows - 2 * cap_near - 2 * (reach - 1) * cap_far
    bounds = []
    start = 0
    for offset in range(-reach, reach + 1):
        if offset == 0:
            group_size = cap_home
        elif abs(offset) == 1:
            group_size = cap_near
        else:
            group_size = cap_far
        bounds.append((offset, start, group_size))
        start = start + group_size
    return bounds


def split_dot(onehot, values):
    return jnp.dot(onehot.astype(jnp.float32), values, precision=lax.Precision.HIGH)


LANES = 128
ROWS = 48


def stage_tables(deriv_r, deriv_s, lift, degree):
    basis_count = deriv_r.shape[0]
    nodes = degree + 1
    lift_t = jnp.zeros((ROWS, basis_count), jnp.float32).at[: 3 * nodes].set(lift.T)
    deriv_t = jnp.zeros((144, basis_count), jnp.float32)
    deriv_t = deriv_t.at[:basis_count].set(deriv_r.T).at[72 : 72 + basis_count].set(deriv_s.T)
    ones_table = face_table(degree)
    faces = ones_table.shape[0]
    own = np.zeros((basis_count, ROWS), np.float32)
    own[:, : faces * nodes] = ones_table.reshape(faces * nodes, basis_count).T
    parts = [own, own]
    for g in range(faces):
        other = np.zeros((basis_count, ROWS), np.float32)
        for f in range(faces):
            other[:, f * nodes : (f + 1) * nodes] = -ones_table[g, ::-1, :].T
        parts.extend([other, other])
    surf = jnp.asarray(np.concatenate(parts, axis=1), jnp.bfloat16)
    return lift_t, deriv_t, surf


def stage_kernel(
    hbm_ref, left_ref, right_ref, met_ref, geo_ref, li_ref, nf_ref, lt_ref, dt_ref, sm_ref,
    out_ref, x_ref, s2_ref, s1_ref, z_ref, sem,
):
    elem_count = hbm_ref.shape[2]
    copy = pltpu.make_async_copy(hbm_ref, x_ref.at[:, :, HALO : HALO + elem_count], sem)
    copy.start()
    copy.wait()
    x_ref[:, :, 0:HALO] = left_ref[...]
    x_ref[:, :, HALO + elem_count : 2 * HALO + elem_count] = right_ref[...]
    fields, basis_count, width = x_ref.shape
    blocks = width // LANES
    split_rows = 2 * fields * ROWS
    z_ref[:, 0:LANES] = jnp.zeros((split_rows, LANES), jnp.bfloat16)
    z_ref[:, width + LANES : width + 2 * LANES] = jnp.zeros((split_rows, LANES), jnp.bfloat16)
    rowface = lax.broadcasted_iota(jnp.int32, (ROWS, LANES), 0) // (ORDER + 1)
    window = lax.broadcasted_iota(jnp.int32, (3 * LANES, LANES), 0)

    def dot(a, b):
        return jnp.dot(a, b, precision=highest, preferred_element_type=jnp.float32)

    def dot16(a, b):
        return jnp.dot(a, b, preferred_element_type=jnp.float32)

    def run(src_ref, kind):
        def traces(b, carry):
            off = pl.multiple_of(b * LANES, LANES)
            lifted = [dot(lt_ref[...], src_ref[c, :, pl.ds(off, LANES)]) for c in range(fields)]
            half_scale = geo_ref[0, :, pl.ds(off, LANES)]
            normal_x = geo_ref[1, :, pl.ds(off, LANES)]
            normal_y = geo_ref[2, :, pl.ds(off, LANES)]
            height, along_x, along_y = lifted
            face_height = half_scale * (
                gravity * (normal_x * along_x + normal_y * along_y) - wave_speed * height
            )
            face_along_x = half_scale * (depth * normal_x * height - wave_speed * along_x)
            face_along_y = half_scale * (depth * normal_y * height - wave_speed * along_y)
            dst = pl.multiple_of(off + LANES, LANES)
            for c, value in enumerate((face_height, face_along_x, face_along_y)):
                high = value.astype(jnp.bfloat16)
                low = (value - high.astype(jnp.float32)).astype(jnp.bfloat16)
                z_ref[c * ROWS : (c + 1) * ROWS, pl.ds(dst, LANES)] = high
                z_ref[(fields + c) * ROWS : (fields + c + 1) * ROWS, pl.ds(dst, LANES)] = low
            return carry

        lax.fori_loop(0, blocks, traces, 0)

        def update(b, carry):
            off = pl.multiple_of(b * LANES, LANES)
            near = z_ref[:, pl.ds(off, 3 * LANES)]
            gathered = []
            for g in range(3):
                spot = li_ref[g : g + 1, pl.ds(off, LANES)] - (off - LANES)
                onehot = (window == spot).astype(jnp.bfloat16)
                across = nf_ref[g : g + 1, pl.ds(off, LANES)]
                picked = dot16(near, onehot)
                gathered.append((picked, rowface == across))
            m = met_ref[:, pl.ds(off, LANES)]
            m0, m1, m2, m3 = (m[k : k + 1] for k in range(4))
            cur = [src_ref[c, :, pl.ds(off, LANES)] for c in range(fields)]
            rs = [dot(dt_ref[...], cur[c]) for c in range(fields)]
            along_r = [v[0:basis_count] for v in rs]
            along_s = [v[72 : 72 + basis_count] for v in rs]
            volume = [
                -gravity * (m0 * along_r[1] + m1 * along_s[1] + m2 * along_r[2] + m3 * along_s[2]),
                -depth * (m0 * along_r[0] + m1 * along_s[0]),
                -depth * (m2 * along_r[0] + m3 * along_s[0]),
            ]
            here = pl.ds(pl.multiple_of(off + LANES, LANES), LANES)
            for c in range(fields):
                hi_rows = slice(c * ROWS, (c + 1) * ROWS)
                lo_rows = slice((fields + c) * ROWS, (fields + c + 1) * ROWS)
                pieces = [z_ref[hi_rows, here], z_ref[lo_rows, here]]
                for picked, mask in gathered:
                    for rows in (hi_rows, lo_rows):
                        pieces.append(jnp.where(mask, picked[rows], 0.0).astype(jnp.bfloat16))
                surface = dot16(sm_ref[...], jnp.concatenate(pieces, axis=0))
                new = cur[c] + time_step * (volume[c] + surface)
                if kind == 0:
                    s2_ref[c, :, pl.ds(off, LANES)] = 2.0 / 3.0 * new
                elif kind == 1:
                    s1_ref[c, :, pl.ds(off, LANES)] = 0.25 * new
                else:
                    dst = pl.multiple_of(off - LANES, LANES)
                    out_ref[c, :, pl.ds(dst, LANES)] = (
                        x_ref[c, :, pl.ds(off, LANES)] / 3.0 + 0.75 * s2_ref[c, :, pl.ds(off, LANES)] + new
                    )
            return carry

        if kind == 2:
            lax.fori_loop(1, blocks - 1, update, 0)
        else:
            lax.fori_loop(0, blocks, update, 0)

    run(x_ref, 0)
    run(s2_ref, 1)
    run(s1_ref, 2)


def body(
    adjoint,
    deriv_r,
    deriv_s,
    lift,
    metric,
    face_scale,
    face_angle,
    neighbours,
    neighbour_face,
    remap_table,
    intersection_elem,
    intersection_old,
    intersection_weight,
    block_type,
):
    fields, basis_count, elem_count = adjoint.shape
    nodes = ORDER + 1
    devices = lax.axis_size(AXES)
    elem_total = elem_count * devices
    first_elem = lax.axis_index(AXES) * elem_count
    width = elem_count + 2 * HALO

    count = lax.axis_size(AXES)
    field_rows = fields * basis_count
    side = jnp.concatenate(
        [metric, face_scale, face_angle, neighbours.astype(jnp.float32), neighbour_face.astype(jnp.float32)],
        axis=0,
    )
    flat = adjoint.reshape(field_rows, elem_count)
    tail = jnp.concatenate([flat[:, elem_count - HALO :], side[:, elem_count - HALO :]], axis=0)
    head = jnp.concatenate([flat[:, :HALO], side[:, :HALO]], axis=0)
    from_left = lax.ppermute(tail, AXES, [(i, (i + 1) % count) for i in range(count)])
    from_right = lax.ppermute(head, AXES, [((i + 1) % count, i) for i in range(count)])
    left = from_left[:field_rows].reshape(fields, basis_count, HALO)
    right = from_right[:field_rows].reshape(fields, basis_count, HALO)
    side = jnp.concatenate([from_left[field_rows:], side, from_right[field_rows:]], axis=1)
    params = side[0:10]
    links = side[10:16].astype(jnp.int32)
    met = params[0:4]
    half_scale = 0.5 * params[4:7]
    angle = params[7:10]

    def spread(v):
        rows = jnp.broadcast_to(v[:, None, :], (v.shape[0], nodes, width)).reshape(-1, width)
        return jnp.concatenate([rows, jnp.zeros((ROWS - 3 * nodes, width), jnp.float32)], axis=0)

    geo = jnp.stack([spread(half_scale), spread(jnp.cos(angle)), spread(jnp.sin(angle))])
    local_index = (links[0:3] - first_elem + HALO + elem_total) % elem_total
    local_index = jnp.clip(local_index, 0, width - 1)
    across_face = links[3:6]
    lift_t, deriv_t, surf = stage_tables(deriv_r, deriv_s, lift, ORDER)
    vmem = pl.BlockSpec(memory_space=pltpu.VMEM)
    adj_new = pl.pallas_call(
        stage_kernel,
        out_shape=jax.ShapeDtypeStruct((fields, basis_count, elem_count), jnp.float32),
        in_specs=[pl.BlockSpec(memory_space=pl.ANY)] + [vmem] * 9,
        out_specs=vmem,
        scratch_shapes=[
            pltpu.VMEM((fields, basis_count, width), jnp.float32),
            pltpu.VMEM((fields, basis_count, width), jnp.float32),
            pltpu.VMEM((fields, basis_count, width), jnp.float32),
            pltpu.VMEM((2 * fields * ROWS, width + 2 * LANES), jnp.bfloat16),
            pltpu.SemaphoreType.DMA(()),
        ],
        compiler_params=pltpu.CompilerParams(vmem_limit_bytes=56 * 1024 * 1024),
    )(adjoint, left, right, met, geo, local_index, across_face, lift_t, deriv_t, surf)
    adj_rows = adj_new.reshape(fields * basis_count, elem_count).T

    rows_here = intersection_elem.shape[0]
    block_here = rows_here // BLOCK
    field_rows = fields * basis_count
    picked = jnp.take(adj_rows, intersection_elem, axis=0, mode="clip")
    picked = picked.reshape(block_here, BLOCK, fields, basis_count)
    chosen = jnp.take(remap_table, block_type, axis=0)
    mapped = jnp.einsum("brci,bij->brcj", picked, chosen, precision=highest)
    mapped = mapped * intersection_weight.reshape(block_here, BLOCK, 1, 1)
    mapped = mapped.reshape(rows_here, field_rows)
    labelled = jnp.concatenate(
        [mapped, intersection_old.astype(jnp.float32)[:, None]], axis=1
    )
    bounds = group_bounds(rows_here, REACH)
    old_count = E_OLD_DEV
    old_iota = jnp.arange(old_count, dtype=jnp.int32)[:, None]

    def scatter(rows):
        labels = rows[:, field_rows].astype(jnp.int32)
        return split_dot(old_iota == labels[None, :], rows[:, :field_rows])

    moved = []
    for offset, start_row, group_size in bounds:
        piece = labelled[start_row : start_row + group_size]
        if offset == 0:
            home = piece
        else:
            moved.append(shifted(piece, offset))
    old_sums = scatter(home) + scatter(jnp.concatenate(moved, axis=0))
    return (adj_new, old_sums.T.reshape(fields, basis_count, old_count))


def solution(mesh):
    in_specs = (
        P(None, None, AXES),
        P(),
        P(),
        P(),
        P(None, AXES),
        P(None, AXES),
        P(None, AXES),
        P(None, AXES),
        P(None, AXES),
        P(),
        P(AXES),
        P(AXES),
        P(AXES),
        P(AXES),
    )
    out_specs = (P(None, None, AXES), P(None, None, AXES))
    return jax.shard_map(body, mesh=mesh, in_specs=in_specs, out_specs=out_specs, check_vma=False)
```

```python
import jax
import jax.numpy as jnp
import numpy as np
from jax import lax
from jax.experimental import pallas as pl
from jax.experimental.pallas import tpu as pltpu
from jax.sharding import PartitionSpec as P

ORDER = 10
REACH = 4
BLOCK = 128
RIM = 32
HALO = 128
E_OLD_DEV = 2048

gravity = 2.0
depth = 0.5
wave_speed = 1.0
time_step = 0.04
highest = lax.Precision.HIGHEST
AXES = ("gx", "gy")


def extended(cells, width, axis=0):
    count = lax.axis_size(AXES)
    size = cells.shape[axis]
    head = lax.slice_in_dim(cells, 0, width, axis=axis)
    tail = lax.slice_in_dim(cells, size - width, size, axis=axis)
    return jnp.concatenate(
        [
            lax.ppermute(tail, AXES, [(i, (i + 1) % count) for i in range(count)]),
            cells,
            lax.ppermute(head, AXES, [((i + 1) % count, i) for i in range(count)]),
        ],
        axis=axis,
    )


def shifted(shard, by):
    length = lax.axis_size(AXES)
    return lax.ppermute(shard, AXES, [(i, (i + by) % length) for i in range(length)])


def face_table(degree):
    basis_count = (degree + 1) * (degree + 2) // 2

    def node_place(column, level):
        return level * (degree + 1) - level * (level - 1) // 2 + column

    ones_table = np.zeros((3, degree + 1, basis_count), np.float32)
    for level in range(degree + 1):
        ones_table[0, level, node_place(level, 0)] = 1.0
        ones_table[1, level, node_place(degree - level, level)] = 1.0
        ones_table[2, level, node_place(0, degree - level)] = 1.0
    return ones_table


def surface_matrix(degree):
    ones_table = face_table(degree)
    faces, nodes, basis_count = ones_table.shape
    own = ones_table.reshape(faces * nodes, basis_count)
    other = -ones_table[:, ::-1, :].reshape(faces * nodes, basis_count)
    return jnp.asarray(np.concatenate([own, other], axis=0))


def group_bounds(q_rows, reach):
    cap_far = q_rows // 32
    cap_near = q_rows // 8
    cap_home = q_rows - 2 * cap_near - 2 * (reach - 1) * cap_far
    bounds = []
    start = 0
    for offset in range(-reach, reach + 1):
        if offset == 0:
            group_size = cap_home
        elif abs(offset) == 1:
            group_size = cap_near
        else:
            group_size = cap_far
        bounds.append((offset, start, group_size))
        start = start + group_size
    return bounds


def split_dot(onehot, values):
    return jnp.dot(onehot.astype(jnp.float32), values, precision=lax.Precision.HIGH)


LANES = 128
ROWS = 48


def stage_tables(deriv_r, deriv_s, lift, degree):
    basis_count = deriv_r.shape[0]
    nodes = degree + 1
    lift_t = jnp.zeros((ROWS, basis_count), jnp.float32).at[: 3 * nodes].set(lift.T)
    deriv_t = jnp.zeros((144, basis_count), jnp.float32)
    deriv_t = deriv_t.at[:basis_count].set(deriv_r.T).at[72 : 72 + basis_count].set(deriv_s.T)
    ones_table = face_table(degree)
    faces = ones_table.shape[0]
    own = np.zeros((basis_count, ROWS), np.float32)
    own[:, : faces * nodes] = ones_table.reshape(faces * nodes, basis_count).T
    parts = [own, own]
    for g in range(faces):
        other = np.zeros((basis_count, ROWS), np.float32)
        for f in range(faces):
            other[:, f * nodes : (f + 1) * nodes] = -ones_table[g, ::-1, :].T
        parts.extend([other, other])
    surf = jnp.asarray(np.concatenate(parts, axis=1), jnp.bfloat16)
    return lift_t, deriv_t, surf


def stage_kernel(
    hbm_ref, left_ref, right_ref, met_ref, geo_ref, li_ref, nf_ref, lt_ref, dt_ref, sm_ref,
    out_ref, x_ref, s2_ref, s1_ref, z_ref, sem,
):
    elem_count = hbm_ref.shape[2]
    copy = pltpu.make_async_copy(hbm_ref, x_ref.at[:, :, HALO : HALO + elem_count], sem)
    copy.start()
    copy.wait()
    x_ref[:, :, 0:HALO] = left_ref[...]
    x_ref[:, :, HALO + elem_count : 2 * HALO + elem_count] = right_ref[...]
    fields, basis_count, width = x_ref.shape
    blocks = width // LANES
    split_rows = 2 * fields * ROWS
    z_ref[:, 0:LANES] = jnp.zeros((split_rows, LANES), jnp.bfloat16)
    z_ref[:, width + LANES : width + 2 * LANES] = jnp.zeros((split_rows, LANES), jnp.bfloat16)
    rowface = lax.broadcasted_iota(jnp.int32, (ROWS, LANES), 0) // (ORDER + 1)
    window = lax.broadcasted_iota(jnp.int32, (3 * LANES, LANES), 0)

    def dot(a, b):
        return jnp.dot(a, b, precision=highest, preferred_element_type=jnp.float32)

    def dot16(a, b):
        return jnp.dot(a, b, preferred_element_type=jnp.float32)

    def run(src_ref, kind):
        def traces(b, carry):
            off = pl.multiple_of(b * LANES, LANES)
            lifted = [dot(lt_ref[...], src_ref[c, :, pl.ds(off, LANES)]) for c in range(fields)]
            half_scale = geo_ref[0, :, pl.ds(off, LANES)]
            normal_x = geo_ref[1, :, pl.ds(off, LANES)]
            normal_y = geo_ref[2, :, pl.ds(off, LANES)]
            height, along_x, along_y = lifted
            face_height = half_scale * (
                gravity * (normal_x * along_x + normal_y * along_y) - wave_speed * height
            )
            face_along_x = half_scale * (depth * normal_x * height - wave_speed * along_x)
            face_along_y = half_scale * (depth * normal_y * height - wave_speed * along_y)
            dst = pl.multiple_of(off + LANES, LANES)
            for c, value in enumerate((face_height, face_along_x, face_along_y)):
                high = value.astype(jnp.bfloat16)
                low = (value - high.astype(jnp.float32)).astype(jnp.bfloat16)
                z_ref[c * ROWS : (c + 1) * ROWS, pl.ds(dst, LANES)] = high
                z_ref[(fields + c) * ROWS : (fields + c + 1) * ROWS, pl.ds(dst, LANES)] = low
            return carry

        lax.fori_loop(0, blocks, traces, 0)

        def update(b, carry):
            off = pl.multiple_of(b * LANES, LANES)
            near = z_ref[:, pl.ds(off, 3 * LANES)]
            gathered = []
            for g in range(3):
                spot = li_ref[g : g + 1, pl.ds(off, LANES)] - (off - LANES)
                onehot = (window == spot).astype(jnp.bfloat16)
                across = nf_ref[g : g + 1, pl.ds(off, LANES)]
                picked = dot16(near, onehot)
                gathered.append((picked, rowface == across))
            m = met_ref[:, pl.ds(off, LANES)]
            m0, m1, m2, m3 = (m[k : k + 1] for k in range(4))
            cur = [src_ref[c, :, pl.ds(off, LANES)] for c in range(fields)]
            rs = [dot(dt_ref[...], cur[c]) for c in range(fields)]
            along_r = [v[0:basis_count] for v in rs]
            along_s = [v[72 : 72 + basis_count] for v in rs]
            volume = [
                -gravity * (m0 * along_r[1] + m1 * along_s[1] + m2 * along_r[2] + m3 * along_s[2]),
                -depth * (m0 * along_r[0] + m1 * along_s[0]),
                -depth * (m2 * along_r[0] + m3 * along_s[0]),
            ]
            here = pl.ds(pl.multiple_of(off + LANES, LANES), LANES)
            for c in range(fields):
                hi_rows = slice(c * ROWS, (c + 1) * ROWS)
                lo_rows = slice((fields + c) * ROWS, (fields + c + 1) * ROWS)
                pieces = [z_ref[hi_rows, here], z_ref[lo_rows, here]]
                for picked, mask in gathered:
                    for rows in (hi_rows, lo_rows):
                        pieces.append(jnp.where(mask, picked[rows], 0.0).astype(jnp.bfloat16))
                surface = dot16(sm_ref[...], jnp.concatenate(pieces, axis=0))
                new = cur[c] + time_step * (volume[c] + surface)
                if kind == 0:
                    s2_ref[c, :, pl.ds(off, LANES)] = 2.0 / 3.0 * new
                elif kind == 1:
                    s1_ref[c, :, pl.ds(off, LANES)] = 0.25 * new
                else:
                    dst = pl.multiple_of(off - LANES, LANES)
                    out_ref[c, :, pl.ds(dst, LANES)] = (
                        x_ref[c, :, pl.ds(off, LANES)] / 3.0 + 0.75 * s2_ref[c, :, pl.ds(off, LANES)] + new
                    )
            return carry

        if kind == 2:
            lax.fori_loop(1, blocks - 1, update, 0)
        else:
            lax.fori_loop(0, blocks, update, 0)

    run(x_ref, 0)
    run(s2_ref, 1)
    run(s1_ref, 2)


def body(
    adjoint,
    deriv_r,
    deriv_s,
    lift,
    metric,
    face_scale,
    face_angle,
    neighbours,
    neighbour_face,
    remap_table,
    intersection_elem,
    intersection_old,
    intersection_weight,
    block_type,
):
    fields, basis_count, elem_count = adjoint.shape
    nodes = ORDER + 1
    devices = lax.axis_size(AXES)
    elem_total = elem_count * devices
    first_elem = lax.axis_index(AXES) * elem_count
    width = elem_count + 2 * HALO

    count = lax.axis_size(AXES)
    field_rows = fields * basis_count
    side = jnp.concatenate(
        [metric, face_scale, face_angle, neighbours.astype(jnp.float32), neighbour_face.astype(jnp.float32)],
        axis=0,
    )
    tail = adjoint[:, :, elem_count - HALO :].reshape(field_rows, HALO)
    tail = jnp.concatenate([tail, side[:, elem_count - HALO :]], axis=0)
    head = adjoint[:, :, :HALO].reshape(field_rows, HALO)
    head = jnp.concatenate([head, side[:, :HALO]], axis=0)
    from_left = lax.ppermute(tail, AXES, [(i, (i + 1) % count) for i in range(count)])
    from_right = lax.ppermute(head, AXES, [((i + 1) % count, i) for i in range(count)])
    left = from_left[:field_rows].reshape(fields, basis_count, HALO)
    right = from_right[:field_rows].reshape(fields, basis_count, HALO)
    side = jnp.concatenate([from_left[field_rows:], side, from_right[field_rows:]], axis=1)
    params = side[0:10]
    links = side[10:16].astype(jnp.int32)
    met = params[0:4]
    half_scale = 0.5 * params[4:7]
    angle = params[7:10]

    def spread(v):
        rows = jnp.broadcast_to(v[:, None, :], (v.shape[0], nodes, width)).reshape(-1, width)
        return jnp.concatenate([rows, jnp.zeros((ROWS - 3 * nodes, width), jnp.float32)], axis=0)

    geo = jnp.stack([spread(half_scale), spread(jnp.cos(angle)), spread(jnp.sin(angle))])
    local_index = (links[0:3] - first_elem + HALO + elem_total) % elem_total
    local_index = jnp.clip(local_index, 0, width - 1)
    across_face = links[3:6]
    lift_t, deriv_t, surf = stage_tables(deriv_r, deriv_s, lift, ORDER)
    vmem = pl.BlockSpec(memory_space=pltpu.VMEM)
    adj_new = pl.pallas_call(
        stage_kernel,
        out_shape=jax.ShapeDtypeStruct((fields, basis_count, elem_count), jnp.float32),
        in_specs=[pl.BlockSpec(memory_space=pl.ANY)] + [vmem] * 9,
        out_specs=vmem,
        scratch_shapes=[
            pltpu.VMEM((fields, basis_count, width), jnp.float32),
            pltpu.VMEM((fields, basis_count, width), jnp.float32),
            pltpu.VMEM((fields, basis_count, width), jnp.float32),
            pltpu.VMEM((2 * fields * ROWS, width + 2 * LANES), jnp.bfloat16),
            pltpu.SemaphoreType.DMA(()),
        ],
        compiler_params=pltpu.CompilerParams(vmem_limit_bytes=56 * 1024 * 1024),
    )(adjoint, left, right, met, geo, local_index, across_face, lift_t, deriv_t, surf)
    adj_rows = jnp.transpose(adj_new, (2, 0, 1)).reshape(elem_count, fields * basis_count)

    rows_here = intersection_elem.shape[0]
    block_here = rows_here // BLOCK
    field_rows = fields * basis_count
    picked = jnp.take(adj_rows, intersection_elem, axis=0, mode="clip")
    picked = picked.reshape(block_here, BLOCK, fields, basis_count)
    chosen = jnp.take(remap_table, block_type, axis=0)
    mapped = jnp.einsum("brci,bij->brcj", picked, chosen, precision=highest)
    mapped = mapped * intersection_weight.reshape(block_here, BLOCK, 1, 1)
    mapped = mapped.reshape(rows_here, field_rows)
    labelled = jnp.concatenate(
        [mapped, intersection_old.astype(jnp.float32)[:, None]], axis=1
    )
    bounds = group_bounds(rows_here, REACH)
    old_count = E_OLD_DEV
    old_iota = jnp.arange(old_count, dtype=jnp.int32)[:, None]

    def scatter(rows):
        labels = rows[:, field_rows].astype(jnp.int32)
        return split_dot(old_iota == labels[None, :], rows[:, :field_rows])

    moved = []
    for offset, start_row, group_size in bounds:
        piece = labelled[start_row : start_row + group_size]
        if offset == 0:
            home = piece
        else:
            moved.append(shifted(piece, offset))
    old_sums = scatter(home) + scatter(jnp.concatenate(moved, axis=0))
    return (adj_new, old_sums.T.reshape(fields, basis_count, old_count))


def solution(mesh):
    in_specs = (
        P(None, None, AXES),
        P(),
        P(),
        P(),
        P(None, AXES),
        P(None, AXES),
        P(None, AXES),
        P(None, AXES),
        P(None, AXES),
        P(),
        P(AXES),
        P(AXES),
        P(AXES),
        P(AXES),
    )
    out_specs = (P(None, None, AXES), P(None, None, AXES))
    return jax.shard_map(body, mesh=mesh, in_specs=in_specs, out_specs=out_specs, check_vma=False)
```

```python
import jax
import jax.numpy as jnp
import numpy as np
from jax import lax
from jax.experimental import pallas as pl
from jax.experimental.pallas import tpu as pltpu
from jax.sharding import PartitionSpec as P

ORDER = 10
REACH = 4
BLOCK = 128
RIM = 32
HALO = 128
E_OLD_DEV = 2048

gravity = 2.0
depth = 0.5
wave_speed = 1.0
time_step = 0.04
highest = lax.Precision.HIGHEST
AXES = ("gx", "gy")


def extended(cells, width, axis=0):
    count = lax.axis_size(AXES)
    size = cells.shape[axis]
    head = lax.slice_in_dim(cells, 0, width, axis=axis)
    tail = lax.slice_in_dim(cells, size - width, size, axis=axis)
    return jnp.concatenate(
        [
            lax.ppermute(tail, AXES, [(i, (i + 1) % count) for i in range(count)]),
            cells,
            lax.ppermute(head, AXES, [((i + 1) % count, i) for i in range(count)]),
        ],
        axis=axis,
    )


def shifted(shard, by):
    length = lax.axis_size(AXES)
    return lax.ppermute(shard, AXES, [(i, (i + by) % length) for i in range(length)])


def face_table(degree):
    basis_count = (degree + 1) * (degree + 2) // 2

    def node_place(column, level):
        return level * (degree + 1) - level * (level - 1) // 2 + column

    ones_table = np.zeros((3, degree + 1, basis_count), np.float32)
    for level in range(degree + 1):
        ones_table[0, level, node_place(level, 0)] = 1.0
        ones_table[1, level, node_place(degree - level, level)] = 1.0
        ones_table[2, level, node_place(0, degree - level)] = 1.0
    return ones_table


def surface_matrix(degree):
    ones_table = face_table(degree)
    faces, nodes, basis_count = ones_table.shape
    own = ones_table.reshape(faces * nodes, basis_count)
    other = -ones_table[:, ::-1, :].reshape(faces * nodes, basis_count)
    return jnp.asarray(np.concatenate([own, other], axis=0))


def group_bounds(q_rows, reach):
    cap_far = q_rows // 32
    cap_near = q_rows // 8
    cap_home = q_rows - 2 * cap_near - 2 * (reach - 1) * cap_far
    bounds = []
    start = 0
    for offset in range(-reach, reach + 1):
        if offset == 0:
            group_size = cap_home
        elif abs(offset) == 1:
            group_size = cap_near
        else:
            group_size = cap_far
        bounds.append((offset, start, group_size))
        start = start + group_size
    return bounds


def split_dot(onehot, values):
    return jnp.dot(onehot.astype(jnp.float32), values, precision=lax.Precision.HIGH)


LANES = 128
ROWS = 48


def stage_tables(deriv_r, deriv_s, lift, degree):
    basis_count = deriv_r.shape[0]
    nodes = degree + 1
    lift_t = jnp.zeros((ROWS, basis_count), jnp.float32).at[: 3 * nodes].set(lift.T)
    deriv_t = jnp.zeros((144, basis_count), jnp.float32)
    deriv_t = deriv_t.at[:basis_count].set(deriv_r.T).at[72 : 72 + basis_count].set(deriv_s.T)
    ones_table = face_table(degree)
    faces = ones_table.shape[0]
    own = np.zeros((basis_count, ROWS), np.float32)
    own[:, : faces * nodes] = ones_table.reshape(faces * nodes, basis_count).T
    parts = [own, own]
    for g in range(faces):
        other = np.zeros((basis_count, ROWS), np.float32)
        for f in range(faces):
            other[:, f * nodes : (f + 1) * nodes] = -ones_table[g, ::-1, :].T
        parts.extend([other, other])
    surf = jnp.asarray(np.concatenate(parts, axis=1), jnp.bfloat16)
    return lift_t, deriv_t, surf


def stage_kernel(
    hbm_ref, left_ref, right_ref, met_ref, geo_ref, li_ref, nf_ref, lt_ref, dt_ref, sm_ref,
    out_ref, x_ref, s2_ref, s1_ref, z_ref, sem,
):
    elem_count = hbm_ref.shape[2]
    copy = pltpu.make_async_copy(hbm_ref, x_ref.at[:, :, HALO : HALO + elem_count], sem)
    copy.start()
    copy.wait()
    x_ref[:, :, 0:HALO] = left_ref[...]
    x_ref[:, :, HALO + elem_count : 2 * HALO + elem_count] = right_ref[...]
    fields, basis_count, width = x_ref.shape
    blocks = width // LANES
    split_rows = 2 * fields * ROWS
    z_ref[:, 0:LANES] = jnp.zeros((split_rows, LANES), jnp.bfloat16)
    z_ref[:, width + LANES : width + 2 * LANES] = jnp.zeros((split_rows, LANES), jnp.bfloat16)
    rowface = lax.broadcasted_iota(jnp.int32, (ROWS, LANES), 0) // (ORDER + 1)
    window = lax.broadcasted_iota(jnp.int32, (3 * LANES, LANES), 0)

    def dot(a, b):
        return jnp.dot(a, b, precision=highest, preferred_element_type=jnp.float32)

    def dot16(a, b):
        return jnp.dot(a, b, preferred_element_type=jnp.float32)

    def run(src_ref, kind):
        def traces(b, carry):
            off = pl.multiple_of(b * LANES, LANES)
            lifted = [dot(lt_ref[...], src_ref[c, :, pl.ds(off, LANES)]) for c in range(fields)]
            half_scale = geo_ref[0, :, pl.ds(off, LANES)]
            normal_x = geo_ref[1, :, pl.ds(off, LANES)]
            normal_y = geo_ref[2, :, pl.ds(off, LANES)]
            height, along_x, along_y = lifted
            face_height = half_scale * (
                gravity * (normal_x * along_x + normal_y * along_y) - wave_speed * height
            )
            face_along_x = half_scale * (depth * normal_x * height - wave_speed * along_x)
            face_along_y = half_scale * (depth * normal_y * height - wave_speed * along_y)
            dst = pl.multiple_of(off + LANES, LANES)
            for c, value in enumerate((face_height, face_along_x, face_along_y)):
                high = value.astype(jnp.bfloat16)
                low = (value - high.astype(jnp.float32)).astype(jnp.bfloat16)
                z_ref[c * ROWS : (c + 1) * ROWS, pl.ds(dst, LANES)] = high
                z_ref[(fields + c) * ROWS : (fields + c + 1) * ROWS, pl.ds(dst, LANES)] = low
            return carry

        lax.fori_loop(0, blocks, traces, 0)

        def update(b, carry):
            off = pl.multiple_of(b * LANES, LANES)
            near = z_ref[:, pl.ds(off, 3 * LANES)]
            gathered = []
            for g in range(3):
                spot = li_ref[g : g + 1, pl.ds(off, LANES)] - (off - LANES)
                onehot = (window == spot).astype(jnp.bfloat16)
                across = nf_ref[g : g + 1, pl.ds(off, LANES)]
                picked = dot16(near, onehot)
                gathered.append((picked, rowface == across))
            m = met_ref[:, pl.ds(off, LANES)]
            m0, m1, m2, m3 = (m[k : k + 1] for k in range(4))
            cur = [src_ref[c, :, pl.ds(off, LANES)] for c in range(fields)]
            rs = [dot(dt_ref[...], cur[c]) for c in range(fields)]
            along_r = [v[0:basis_count] for v in rs]
            along_s = [v[72 : 72 + basis_count] for v in rs]
            volume = [
                -gravity * (m0 * along_r[1] + m1 * along_s[1] + m2 * along_r[2] + m3 * along_s[2]),
                -depth * (m0 * along_r[0] + m1 * along_s[0]),
                -depth * (m2 * along_r[0] + m3 * along_s[0]),
            ]
            here = pl.ds(pl.multiple_of(off + LANES, LANES), LANES)
            for c in range(fields):
                hi_rows = slice(c * ROWS, (c + 1) * ROWS)
                lo_rows = slice((fields + c) * ROWS, (fields + c + 1) * ROWS)
                pieces = [z_ref[hi_rows, here], z_ref[lo_rows, here]]
                for picked, mask in gathered:
                    for rows in (hi_rows, lo_rows):
                        pieces.append(jnp.where(mask, picked[rows], 0.0).astype(jnp.bfloat16))
                surface = dot16(sm_ref[...], jnp.concatenate(pieces, axis=0))
                new = cur[c] + time_step * (volume[c] + surface)
                if kind == 0:
                    s2_ref[c, :, pl.ds(off, LANES)] = 2.0 / 3.0 * new
                elif kind == 1:
                    s1_ref[c, :, pl.ds(off, LANES)] = 0.25 * new
                else:
                    dst = pl.multiple_of(off - LANES, LANES)
                    out_ref[c, :, pl.ds(dst, LANES)] = (
                        x_ref[c, :, pl.ds(off, LANES)] / 3.0 + 0.75 * s2_ref[c, :, pl.ds(off, LANES)] + new
                    )
            return carry

        if kind == 2:
            lax.fori_loop(1, blocks - 1, update, 0)
        else:
            lax.fori_loop(0, blocks, update, 0)

    run(x_ref, 0)
    run(s2_ref, 1)
    run(s1_ref, 2)


def body(
    adjoint,
    deriv_r,
    deriv_s,
    lift,
    metric,
    face_scale,
    face_angle,
    neighbours,
    neighbour_face,
    remap_table,
    intersection_elem,
    intersection_old,
    intersection_weight,
    block_type,
):
    fields, basis_count, elem_count = adjoint.shape
    nodes = ORDER + 1
    devices = lax.axis_size(AXES)
    elem_total = elem_count * devices
    first_elem = lax.axis_index(AXES) * elem_count
    width = elem_count + 2 * HALO

    count = lax.axis_size(AXES)
    field_rows = fields * basis_count
    side = jnp.concatenate(
        [metric, face_scale, face_angle, neighbours.astype(jnp.float32), neighbour_face.astype(jnp.float32)],
        axis=0,
    )
    tail = adjoint[:, :, elem_count - HALO :].reshape(field_rows, HALO)
    tail = jnp.concatenate([tail, side[:, elem_count - HALO :]], axis=0)
    head = adjoint[:, :, :HALO].reshape(field_rows, HALO)
    head = jnp.concatenate([head, side[:, :HALO]], axis=0)
    from_left = lax.ppermute(tail, AXES, [(i, (i + 1) % count) for i in range(count)])
    from_right = lax.ppermute(head, AXES, [((i + 1) % count, i) for i in range(count)])
    left = from_left[:field_rows].reshape(fields, basis_count, HALO)
    right = from_right[:field_rows].reshape(fields, basis_count, HALO)
    side = jnp.concatenate([from_left[field_rows:], side, from_right[field_rows:]], axis=1)
    params = side[0:10]
    links = side[10:16].astype(jnp.int32)
    met = params[0:4]
    half_scale = 0.5 * params[4:7]
    angle = params[7:10]

    def spread(v):
        rows = jnp.broadcast_to(v[:, None, :], (v.shape[0], nodes, width)).reshape(-1, width)
        return jnp.concatenate([rows, jnp.zeros((ROWS - 3 * nodes, width), jnp.float32)], axis=0)

    geo = jnp.stack([spread(half_scale), spread(jnp.cos(angle)), spread(jnp.sin(angle))])
    local_index = (links[0:3] - first_elem + HALO + elem_total) % elem_total
    local_index = jnp.clip(local_index, 0, width - 1)
    across_face = links[3:6]
    lift_t, deriv_t, surf = stage_tables(deriv_r, deriv_s, lift, ORDER)
    vmem = pl.BlockSpec(memory_space=pltpu.VMEM)
    adj_new = pl.pallas_call(
        stage_kernel,
        out_shape=jax.ShapeDtypeStruct((fields, basis_count, elem_count), jnp.float32),
        in_specs=[pl.BlockSpec(memory_space=pl.ANY)] + [vmem] * 9,
        out_specs=vmem,
        scratch_shapes=[
            pltpu.VMEM((fields, basis_count, width), jnp.float32),
            pltpu.VMEM((fields, basis_count, width), jnp.float32),
            pltpu.VMEM((fields, basis_count, width), jnp.float32),
            pltpu.VMEM((2 * fields * ROWS, width + 2 * LANES), jnp.bfloat16),
            pltpu.SemaphoreType.DMA(()),
        ],
        compiler_params=pltpu.CompilerParams(vmem_limit_bytes=56 * 1024 * 1024),
    )(adjoint, left, right, met, geo, local_index, across_face, lift_t, deriv_t, surf)
    adj_rows = jnp.transpose(adj_new, (2, 0, 1)).reshape(elem_count, fields * basis_count)

    rows_here = intersection_elem.shape[0]
    block_here = rows_here // BLOCK
    field_rows = fields * basis_count
    bounds = group_bounds(rows_here, REACH)
    old_count = E_OLD_DEV
    old_iota = jnp.arange(old_count, dtype=jnp.int32)[:, None]

    def labelled_rows(first, count):
        blocks = count // BLOCK
        elems = lax.slice_in_dim(intersection_elem, first, first + count)
        picked = jnp.take(adj_rows, elems, axis=0, mode="clip")
        picked = picked.reshape(blocks, BLOCK, fields, basis_count)
        kinds = lax.slice_in_dim(block_type, first // BLOCK, first // BLOCK + blocks)
        chosen = jnp.take(remap_table, kinds, axis=0)
        mapped = jnp.einsum("brci,bij->brcj", picked, chosen, precision=highest)
        weight = lax.slice_in_dim(intersection_weight, first, first + count)
        mapped = mapped * weight.reshape(blocks, BLOCK, 1, 1)
        mapped = mapped.reshape(count, field_rows)
        labels = lax.slice_in_dim(intersection_old, first, first + count)
        return jnp.concatenate([mapped, labels.astype(jnp.float32)[:, None]], axis=1)

    def scatter(rows):
        labels = rows[:, field_rows].astype(jnp.int32)
        return split_dot(old_iota == labels[None, :], rows[:, :field_rows])

    home_start = [start_row for offset, start_row, _ in bounds if offset == 0][0]
    home_size = [size for offset, _, size in bounds if offset == 0][0]
    home_end = home_start + home_size
    before = labelled_rows(0, home_start)
    after = labelled_rows(home_end, rows_here - home_end)
    moved = []
    for offset, start_row, group_size in bounds:
        if offset < 0:
            moved.append(shifted(before[start_row : start_row + group_size], offset))
        elif offset > 0:
            moved.append(shifted(after[start_row - home_end : start_row - home_end + group_size], offset))
    home = labelled_rows(home_start, home_size)
    old_sums = scatter(home) + scatter(jnp.concatenate(moved, axis=0))
    return (adj_new, old_sums.T.reshape(fields, basis_count, old_count))


def solution(mesh):
    in_specs = (
        P(None, None, AXES),
        P(),
        P(),
        P(),
        P(None, AXES),
        P(None, AXES),
        P(None, AXES),
        P(None, AXES),
        P(None, AXES),
        P(),
        P(AXES),
        P(AXES),
        P(AXES),
        P(AXES),
    )
    out_specs = (P(None, None, AXES), P(None, None, AXES))
    return jax.shard_map(body, mesh=mesh, in_specs=in_specs, out_specs=out_specs, check_vma=False)
```

```python
import jax
import jax.numpy as jnp
import numpy as np
from jax import lax
from jax.experimental import pallas as pl
from jax.experimental.pallas import tpu as pltpu
from jax.sharding import PartitionSpec as P

ORDER = 10
REACH = 4
BLOCK = 128
RIM = 32
HALO = 128
E_OLD_DEV = 2048

gravity = 2.0
depth = 0.5
wave_speed = 1.0
time_step = 0.04
highest = lax.Precision.HIGHEST
AXES = ("gx", "gy")


def extended(cells, width, axis=0):
    count = lax.axis_size(AXES)
    size = cells.shape[axis]
    head = lax.slice_in_dim(cells, 0, width, axis=axis)
    tail = lax.slice_in_dim(cells, size - width, size, axis=axis)
    return jnp.concatenate(
        [
            lax.ppermute(tail, AXES, [(i, (i + 1) % count) for i in range(count)]),
            cells,
            lax.ppermute(head, AXES, [((i + 1) % count, i) for i in range(count)]),
        ],
        axis=axis,
    )


def shifted(shard, by):
    length = lax.axis_size(AXES)
    return lax.ppermute(shard, AXES, [(i, (i + by) % length) for i in range(length)])


def face_table(degree):
    basis_count = (degree + 1) * (degree + 2) // 2

    def node_place(column, level):
        return level * (degree + 1) - level * (level - 1) // 2 + column

    ones_table = np.zeros((3, degree + 1, basis_count), np.float32)
    for level in range(degree + 1):
        ones_table[0, level, node_place(level, 0)] = 1.0
        ones_table[1, level, node_place(degree - level, level)] = 1.0
        ones_table[2, level, node_place(0, degree - level)] = 1.0
    return ones_table


def surface_matrix(degree):
    ones_table = face_table(degree)
    faces, nodes, basis_count = ones_table.shape
    own = ones_table.reshape(faces * nodes, basis_count)
    other = -ones_table[:, ::-1, :].reshape(faces * nodes, basis_count)
    return jnp.asarray(np.concatenate([own, other], axis=0))


def group_bounds(q_rows, reach):
    cap_far = q_rows // 32
    cap_near = q_rows // 8
    cap_home = q_rows - 2 * cap_near - 2 * (reach - 1) * cap_far
    bounds = []
    start = 0
    for offset in range(-reach, reach + 1):
        if offset == 0:
            group_size = cap_home
        elif abs(offset) == 1:
            group_size = cap_near
        else:
            group_size = cap_far
        bounds.append((offset, start, group_size))
        start = start + group_size
    return bounds


def split_dot(onehot, values):
    return jnp.dot(onehot.astype(jnp.float32), values, precision=lax.Precision.HIGH)


LANES = 128
ROWS = 48


def stage_tables(deriv_r, deriv_s, lift, degree):
    basis_count = deriv_r.shape[0]
    nodes = degree + 1
    lift_t = jnp.zeros((ROWS, basis_count), jnp.float32).at[: 3 * nodes].set(lift.T)
    deriv_t = jnp.zeros((144, basis_count), jnp.float32)
    deriv_t = deriv_t.at[:basis_count].set(deriv_r.T).at[72 : 72 + basis_count].set(deriv_s.T)
    ones_table = face_table(degree)
    faces = ones_table.shape[0]
    own = np.zeros((basis_count, ROWS), np.float32)
    own[:, : faces * nodes] = ones_table.reshape(faces * nodes, basis_count).T
    parts = [own, own]
    for g in range(faces):
        other = np.zeros((basis_count, ROWS), np.float32)
        for f in range(faces):
            other[:, f * nodes : (f + 1) * nodes] = -ones_table[g, ::-1, :].T
        parts.extend([other, other])
    surf = jnp.asarray(np.concatenate(parts, axis=1), jnp.bfloat16)
    return lift_t, deriv_t, surf


def stage_kernel(
    hbm_ref, left_ref, right_ref, met_ref, geo_ref, li_ref, nf_ref, lt_ref, dt_ref, sm_ref,
    out_ref, x_ref, s2_ref, s1_ref, z_ref, sem,
):
    elem_count = hbm_ref.shape[2]
    copy = pltpu.make_async_copy(hbm_ref, x_ref.at[:, :, HALO : HALO + elem_count], sem)
    copy.start()
    copy.wait()
    x_ref[:, :, 0:HALO] = left_ref[...]
    x_ref[:, :, HALO + elem_count : 2 * HALO + elem_count] = right_ref[...]
    fields, basis_count, width = x_ref.shape
    blocks = width // LANES
    split_rows = 2 * fields * ROWS
    z_ref[:, 0:LANES] = jnp.zeros((split_rows, LANES), jnp.bfloat16)
    z_ref[:, width + LANES : width + 2 * LANES] = jnp.zeros((split_rows, LANES), jnp.bfloat16)
    rowface = lax.broadcasted_iota(jnp.int32, (ROWS, LANES), 0) // (ORDER + 1)
    window = lax.broadcasted_iota(jnp.int32, (3 * LANES, LANES), 0)

    def dot(a, b):
        return jnp.dot(a, b, precision=highest, preferred_element_type=jnp.float32)

    def dot16(a, b):
        return jnp.dot(a, b, preferred_element_type=jnp.float32)

    def run(src_ref, kind):
        def traces(b, carry):
            off = pl.multiple_of(b * LANES, LANES)
            lifted = [dot(lt_ref[...], src_ref[c, :, pl.ds(off, LANES)]) for c in range(fields)]
            half_scale = geo_ref[0, :, pl.ds(off, LANES)]
            normal_x = geo_ref[1, :, pl.ds(off, LANES)]
            normal_y = geo_ref[2, :, pl.ds(off, LANES)]
            height, along_x, along_y = lifted
            face_height = half_scale * (
                gravity * (normal_x * along_x + normal_y * along_y) - wave_speed * height
            )
            face_along_x = half_scale * (depth * normal_x * height - wave_speed * along_x)
            face_along_y = half_scale * (depth * normal_y * height - wave_speed * along_y)
            dst = pl.multiple_of(off + LANES, LANES)
            for c, value in enumerate((face_height, face_along_x, face_along_y)):
                high = value.astype(jnp.bfloat16)
                low = (value - high.astype(jnp.float32)).astype(jnp.bfloat16)
                z_ref[c * ROWS : (c + 1) * ROWS, pl.ds(dst, LANES)] = high
                z_ref[(fields + c) * ROWS : (fields + c + 1) * ROWS, pl.ds(dst, LANES)] = low
            return carry

        lax.fori_loop(0, blocks, traces, 0)

        def update(b, carry):
            off = pl.multiple_of(b * LANES, LANES)
            near = z_ref[:, pl.ds(off, 3 * LANES)]
            gathered = []
            for g in range(3):
                spot = li_ref[g : g + 1, pl.ds(off, LANES)] - (off - LANES)
                onehot = (window == spot).astype(jnp.bfloat16)
                across = nf_ref[g : g + 1, pl.ds(off, LANES)]
                picked = dot16(near, onehot)
                gathered.append((picked, rowface == across))
            m = met_ref[:, pl.ds(off, LANES)]
            m0, m1, m2, m3 = (m[k : k + 1] for k in range(4))
            cur = [src_ref[c, :, pl.ds(off, LANES)] for c in range(fields)]
            rs = [dot(dt_ref[...], cur[c]) for c in range(fields)]
            along_r = [v[0:basis_count] for v in rs]
            along_s = [v[72 : 72 + basis_count] for v in rs]
            volume = [
                -gravity * (m0 * along_r[1] + m1 * along_s[1] + m2 * along_r[2] + m3 * along_s[2]),
                -depth * (m0 * along_r[0] + m1 * along_s[0]),
                -depth * (m2 * along_r[0] + m3 * along_s[0]),
            ]
            here = pl.ds(pl.multiple_of(off + LANES, LANES), LANES)
            for c in range(fields):
                hi_rows = slice(c * ROWS, (c + 1) * ROWS)
                lo_rows = slice((fields + c) * ROWS, (fields + c + 1) * ROWS)
                pieces = [z_ref[hi_rows, here], z_ref[lo_rows, here]]
                for picked, mask in gathered:
                    for rows in (hi_rows, lo_rows):
                        pieces.append(jnp.where(mask, picked[rows], 0.0).astype(jnp.bfloat16))
                surface = dot16(sm_ref[...], jnp.concatenate(pieces, axis=0))
                new = cur[c] + time_step * (volume[c] + surface)
                if kind == 0:
                    s2_ref[c, :, pl.ds(off, LANES)] = 2.0 / 3.0 * new
                elif kind == 1:
                    s1_ref[c, :, pl.ds(off, LANES)] = 0.25 * new
                else:
                    dst = pl.multiple_of(off - LANES, LANES)
                    out_ref[c, :, pl.ds(dst, LANES)] = (
                        x_ref[c, :, pl.ds(off, LANES)] / 3.0 + 0.75 * s2_ref[c, :, pl.ds(off, LANES)] + new
                    )
            return carry

        if kind == 2:
            lax.fori_loop(1, blocks - 1, update, 0)
        else:
            lax.fori_loop(0, blocks, update, 0)

    run(x_ref, 0)
    run(s2_ref, 1)
    run(s1_ref, 2)


def body(
    adjoint,
    deriv_r,
    deriv_s,
    lift,
    metric,
    face_scale,
    face_angle,
    neighbours,
    neighbour_face,
    remap_table,
    intersection_elem,
    intersection_old,
    intersection_weight,
    block_type,
):
    fields, basis_count, elem_count = adjoint.shape
    nodes = ORDER + 1
    devices = lax.axis_size(AXES)
    elem_total = elem_count * devices
    first_elem = lax.axis_index(AXES) * elem_count
    width = elem_count + 2 * HALO

    count = lax.axis_size(AXES)
    field_rows = fields * basis_count
    side = jnp.concatenate(
        [metric, face_scale, face_angle, neighbours.astype(jnp.float32), neighbour_face.astype(jnp.float32)],
        axis=0,
    )
    tail = adjoint[:, :, elem_count - HALO :].reshape(field_rows, HALO)
    tail = jnp.concatenate([tail, side[:, elem_count - HALO :]], axis=0)
    head = adjoint[:, :, :HALO].reshape(field_rows, HALO)
    head = jnp.concatenate([head, side[:, :HALO]], axis=0)
    from_left = lax.ppermute(tail, AXES, [(i, (i + 1) % count) for i in range(count)])
    from_right = lax.ppermute(head, AXES, [((i + 1) % count, i) for i in range(count)])
    left = from_left[:field_rows].reshape(fields, basis_count, HALO)
    right = from_right[:field_rows].reshape(fields, basis_count, HALO)
    side = jnp.concatenate([from_left[field_rows:], side, from_right[field_rows:]], axis=1)
    params = side[0:10]
    links = side[10:16].astype(jnp.int32)
    met = params[0:4]
    half_scale = 0.5 * params[4:7]
    angle = params[7:10]

    def spread(v):
        rows = jnp.broadcast_to(v[:, None, :], (v.shape[0], nodes, width)).reshape(-1, width)
        return jnp.concatenate([rows, jnp.zeros((ROWS - 3 * nodes, width), jnp.float32)], axis=0)

    geo = jnp.stack([spread(half_scale), spread(jnp.cos(angle)), spread(jnp.sin(angle))])
    local_index = (links[0:3] - first_elem + HALO + elem_total) % elem_total
    local_index = jnp.clip(local_index, 0, width - 1)
    across_face = links[3:6]
    lift_t, deriv_t, surf = stage_tables(deriv_r, deriv_s, lift, ORDER)
    vmem = pl.BlockSpec(memory_space=pltpu.VMEM)
    adj_new = pl.pallas_call(
        stage_kernel,
        out_shape=jax.ShapeDtypeStruct((fields, basis_count, elem_count), jnp.float32),
        in_specs=[pl.BlockSpec(memory_space=pl.ANY)] + [vmem] * 9,
        out_specs=vmem,
        scratch_shapes=[
            pltpu.VMEM((fields, basis_count, width), jnp.float32),
            pltpu.VMEM((fields, basis_count, width), jnp.float32),
            pltpu.VMEM((fields, basis_count, width), jnp.float32),
            pltpu.VMEM((2 * fields * ROWS, width + 2 * LANES), jnp.bfloat16),
            pltpu.SemaphoreType.DMA(()),
        ],
        compiler_params=pltpu.CompilerParams(vmem_limit_bytes=56 * 1024 * 1024),
    )(adjoint, left, right, met, geo, local_index, across_face, lift_t, deriv_t, surf)
    adj_rows = jnp.transpose(adj_new, (2, 0, 1)).reshape(elem_count, fields * basis_count)

    rows_here = intersection_elem.shape[0]
    block_here = rows_here // BLOCK
    field_rows = fields * basis_count
    bounds = group_bounds(rows_here, REACH)
    old_count = E_OLD_DEV
    old_iota = jnp.arange(old_count, dtype=jnp.int32)[:, None]

    def labelled_rows(first, count):
        blocks = count // BLOCK
        elems = lax.slice_in_dim(intersection_elem, first, first + count)
        picked = jnp.take(adj_rows, elems, axis=0, mode="clip")
        picked = picked.reshape(blocks, BLOCK, fields, basis_count)
        kinds = lax.slice_in_dim(block_type, first // BLOCK, first // BLOCK + blocks)
        chosen = jnp.take(remap_table, kinds, axis=0)
        mapped = jnp.einsum("brci,bij->brcj", picked, chosen, precision=lax.Precision.HIGH)
        weight = lax.slice_in_dim(intersection_weight, first, first + count)
        mapped = mapped * weight.reshape(blocks, BLOCK, 1, 1)
        mapped = mapped.reshape(count, field_rows)
        labels = lax.slice_in_dim(intersection_old, first, first + count)
        return jnp.concatenate([mapped, labels.astype(jnp.float32)[:, None]], axis=1)

    def scatter(rows):
        labels = rows[:, field_rows].astype(jnp.int32)
        return split_dot(old_iota == labels[None, :], rows[:, :field_rows])

    home_start = [start_row for offset, start_row, _ in bounds if offset == 0][0]
    home_size = [size for offset, _, size in bounds if offset == 0][0]
    home_end = home_start + home_size
    before = labelled_rows(0, home_start)
    after = labelled_rows(home_end, rows_here - home_end)
    moved = []
    for offset, start_row, group_size in bounds:
        if offset < 0:
            moved.append(shifted(before[start_row : start_row + group_size], offset))
        elif offset > 0:
            moved.append(shifted(after[start_row - home_end : start_row - home_end + group_size], offset))
    home = labelled_rows(home_start, home_size)
    old_sums = scatter(home) + scatter(jnp.concatenate(moved, axis=0))
    return (adj_new, old_sums.T.reshape(fields, basis_count, old_count))


def solution(mesh):
    in_specs = (
        P(None, None, AXES),
        P(),
        P(),
        P(),
        P(None, AXES),
        P(None, AXES),
        P(None, AXES),
        P(None, AXES),
        P(None, AXES),
        P(),
        P(AXES),
        P(AXES),
        P(AXES),
        P(AXES),
    )
    out_specs = (P(None, None, AXES), P(None, None, AXES))
    return jax.shard_map(body, mesh=mesh, in_specs=in_specs, out_specs=out_specs, check_vma=False)
```

```python
import jax
import jax.numpy as jnp
import numpy as np
from jax import lax
from jax.experimental import pallas as pl
from jax.experimental.pallas import tpu as pltpu
from jax.sharding import PartitionSpec as P

ORDER = 10
REACH = 4
BLOCK = 128
RIM = 32
HALO = 128
E_OLD_DEV = 2048

gravity = 2.0
depth = 0.5
wave_speed = 1.0
time_step = 0.04
highest = lax.Precision.HIGHEST
AXES = ("gx", "gy")


def extended(cells, width, axis=0):
    count = lax.axis_size(AXES)
    size = cells.shape[axis]
    head = lax.slice_in_dim(cells, 0, width, axis=axis)
    tail = lax.slice_in_dim(cells, size - width, size, axis=axis)
    return jnp.concatenate(
        [
            lax.ppermute(tail, AXES, [(i, (i + 1) % count) for i in range(count)]),
            cells,
            lax.ppermute(head, AXES, [((i + 1) % count, i) for i in range(count)]),
        ],
        axis=axis,
    )


def shifted(shard, by):
    length = lax.axis_size(AXES)
    return lax.ppermute(shard, AXES, [(i, (i + by) % length) for i in range(length)])


def face_table(degree):
    basis_count = (degree + 1) * (degree + 2) // 2

    def node_place(column, level):
        return level * (degree + 1) - level * (level - 1) // 2 + column

    ones_table = np.zeros((3, degree + 1, basis_count), np.float32)
    for level in range(degree + 1):
        ones_table[0, level, node_place(level, 0)] = 1.0
        ones_table[1, level, node_place(degree - level, level)] = 1.0
        ones_table[2, level, node_place(0, degree - level)] = 1.0
    return ones_table


def surface_matrix(degree):
    ones_table = face_table(degree)
    faces, nodes, basis_count = ones_table.shape
    own = ones_table.reshape(faces * nodes, basis_count)
    other = -ones_table[:, ::-1, :].reshape(faces * nodes, basis_count)
    return jnp.asarray(np.concatenate([own, other], axis=0))


def group_bounds(q_rows, reach):
    cap_far = q_rows // 32
    cap_near = q_rows // 8
    cap_home = q_rows - 2 * cap_near - 2 * (reach - 1) * cap_far
    bounds = []
    start = 0
    for offset in range(-reach, reach + 1):
        if offset == 0:
            group_size = cap_home
        elif abs(offset) == 1:
            group_size = cap_near
        else:
            group_size = cap_far
        bounds.append((offset, start, group_size))
        start = start + group_size
    return bounds


def split_dot(onehot, values):
    high = lax.reduce_precision(values, exponent_bits=8, mantissa_bits=7)
    both = jnp.concatenate([high, values - high], axis=1).astype(jnp.bfloat16)
    out = jnp.dot(onehot.astype(jnp.bfloat16), both, preferred_element_type=jnp.float32)
    cols = values.shape[1]
    return out[:, :cols] + out[:, cols:]


LANES = 128
ROWS = 48


def stage_tables(deriv_r, deriv_s, lift, degree):
    basis_count = deriv_r.shape[0]
    nodes = degree + 1
    lift_t = jnp.zeros((ROWS, basis_count), jnp.float32).at[: 3 * nodes].set(lift.T)
    deriv_t = jnp.zeros((144, basis_count), jnp.float32)
    deriv_t = deriv_t.at[:basis_count].set(deriv_r.T).at[72 : 72 + basis_count].set(deriv_s.T)
    ones_table = face_table(degree)
    faces = ones_table.shape[0]
    own = np.zeros((basis_count, ROWS), np.float32)
    own[:, : faces * nodes] = ones_table.reshape(faces * nodes, basis_count).T
    parts = [own, own]
    for g in range(faces):
        other = np.zeros((basis_count, ROWS), np.float32)
        for f in range(faces):
            other[:, f * nodes : (f + 1) * nodes] = -ones_table[g, ::-1, :].T
        parts.extend([other, other])
    surf = jnp.asarray(np.concatenate(parts, axis=1), jnp.bfloat16)
    return lift_t, deriv_t, surf


def stage_kernel(
    hbm_ref, left_ref, right_ref, met_ref, geo_ref, li_ref, nf_ref, lt_ref, dt_ref, sm_ref,
    out_ref, x_ref, s2_ref, s1_ref, z_ref, sem,
):
    elem_count = hbm_ref.shape[2]
    copy = pltpu.make_async_copy(hbm_ref, x_ref.at[:, :, HALO : HALO + elem_count], sem)
    copy.start()
    copy.wait()
    x_ref[:, :, 0:HALO] = left_ref[...]
    x_ref[:, :, HALO + elem_count : 2 * HALO + elem_count] = right_ref[...]
    fields, basis_count, width = x_ref.shape
    blocks = width // LANES
    split_rows = 2 * fields * ROWS
    z_ref[:, 0:LANES] = jnp.zeros((split_rows, LANES), jnp.bfloat16)
    z_ref[:, width + LANES : width + 2 * LANES] = jnp.zeros((split_rows, LANES), jnp.bfloat16)
    rowface = lax.broadcasted_iota(jnp.int32, (ROWS, LANES), 0) // (ORDER + 1)
    window = lax.broadcasted_iota(jnp.int32, (3 * LANES, LANES), 0)

    def dot(a, b):
        return jnp.dot(a, b, precision=highest, preferred_element_type=jnp.float32)

    def dot16(a, b):
        return jnp.dot(a, b, preferred_element_type=jnp.float32)

    def run(src_ref, kind):
        def traces(b, carry):
            off = pl.multiple_of(b * LANES, LANES)
            lifted = [dot(lt_ref[...], src_ref[c, :, pl.ds(off, LANES)]) for c in range(fields)]
            half_scale = geo_ref[0, :, pl.ds(off, LANES)]
            normal_x = geo_ref[1, :, pl.ds(off, LANES)]
            normal_y = geo_ref[2, :, pl.ds(off, LANES)]
            height, along_x, along_y = lifted
            face_height = half_scale * (
                gravity * (normal_x * along_x + normal_y * along_y) - wave_speed * height
            )
            face_along_x = half_scale * (depth * normal_x * height - wave_speed * along_x)
            face_along_y = half_scale * (depth * normal_y * height - wave_speed * along_y)
            dst = pl.multiple_of(off + LANES, LANES)
            for c, value in enumerate((face_height, face_along_x, face_along_y)):
                high = value.astype(jnp.bfloat16)
                low = (value - high.astype(jnp.float32)).astype(jnp.bfloat16)
                z_ref[c * ROWS : (c + 1) * ROWS, pl.ds(dst, LANES)] = high
                z_ref[(fields + c) * ROWS : (fields + c + 1) * ROWS, pl.ds(dst, LANES)] = low
            return carry

        lax.fori_loop(0, blocks, traces, 0)

        def update(b, carry):
            off = pl.multiple_of(b * LANES, LANES)
            near = z_ref[:, pl.ds(off, 3 * LANES)]
            gathered = []
            for g in range(3):
                spot = li_ref[g : g + 1, pl.ds(off, LANES)] - (off - LANES)
                onehot = (window == spot).astype(jnp.bfloat16)
                across = nf_ref[g : g + 1, pl.ds(off, LANES)]
                picked = dot16(near, onehot)
                gathered.append((picked, rowface == across))
            m = met_ref[:, pl.ds(off, LANES)]
            m0, m1, m2, m3 = (m[k : k + 1] for k in range(4))
            cur = [src_ref[c, :, pl.ds(off, LANES)] for c in range(fields)]
            rs = [dot(dt_ref[...], cur[c]) for c in range(fields)]
            along_r = [v[0:basis_count] for v in rs]
            along_s = [v[72 : 72 + basis_count] for v in rs]
            volume = [
                -gravity * (m0 * along_r[1] + m1 * along_s[1] + m2 * along_r[2] + m3 * along_s[2]),
                -depth * (m0 * along_r[0] + m1 * along_s[0]),
                -depth * (m2 * along_r[0] + m3 * along_s[0]),
            ]
            here = pl.ds(pl.multiple_of(off + LANES, LANES), LANES)
            for c in range(fields):
                hi_rows = slice(c * ROWS, (c + 1) * ROWS)
                lo_rows = slice((fields + c) * ROWS, (fields + c + 1) * ROWS)
                pieces = [z_ref[hi_rows, here], z_ref[lo_rows, here]]
                for picked, mask in gathered:
                    for rows in (hi_rows, lo_rows):
                        pieces.append(jnp.where(mask, picked[rows], 0.0).astype(jnp.bfloat16))
                surface = dot16(sm_ref[...], jnp.concatenate(pieces, axis=0))
                new = cur[c] + time_step * (volume[c] + surface)
                if kind == 0:
                    s2_ref[c, :, pl.ds(off, LANES)] = 2.0 / 3.0 * new
                elif kind == 1:
                    s1_ref[c, :, pl.ds(off, LANES)] = 0.25 * new
                else:
                    dst = pl.multiple_of(off - LANES, LANES)
                    out_ref[c, :, pl.ds(dst, LANES)] = (
                        x_ref[c, :, pl.ds(off, LANES)] / 3.0 + 0.75 * s2_ref[c, :, pl.ds(off, LANES)] + new
                    )
            return carry

        if kind == 2:
            lax.fori_loop(1, blocks - 1, update, 0)
        else:
            lax.fori_loop(0, blocks, update, 0)

    run(x_ref, 0)
    run(s2_ref, 1)
    run(s1_ref, 2)


def body(
    adjoint,
    deriv_r,
    deriv_s,
    lift,
    metric,
    face_scale,
    face_angle,
    neighbours,
    neighbour_face,
    remap_table,
    intersection_elem,
    intersection_old,
    intersection_weight,
    block_type,
):
    fields, basis_count, elem_count = adjoint.shape
    nodes = ORDER + 1
    devices = lax.axis_size(AXES)
    elem_total = elem_count * devices
    first_elem = lax.axis_index(AXES) * elem_count
    width = elem_count + 2 * HALO

    count = lax.axis_size(AXES)
    field_rows = fields * basis_count
    side = jnp.concatenate(
        [metric, face_scale, face_angle, neighbours.astype(jnp.float32), neighbour_face.astype(jnp.float32)],
        axis=0,
    )
    tail = adjoint[:, :, elem_count - HALO :].reshape(field_rows, HALO)
    tail = jnp.concatenate([tail, side[:, elem_count - HALO :]], axis=0)
    head = adjoint[:, :, :HALO].reshape(field_rows, HALO)
    head = jnp.concatenate([head, side[:, :HALO]], axis=0)
    from_left = lax.ppermute(tail, AXES, [(i, (i + 1) % count) for i in range(count)])
    from_right = lax.ppermute(head, AXES, [((i + 1) % count, i) for i in range(count)])
    left = from_left[:field_rows].reshape(fields, basis_count, HALO)
    right = from_right[:field_rows].reshape(fields, basis_count, HALO)
    side = jnp.concatenate([from_left[field_rows:], side, from_right[field_rows:]], axis=1)
    params = side[0:10]
    links = side[10:16].astype(jnp.int32)
    met = params[0:4]
    half_scale = 0.5 * params[4:7]
    angle = params[7:10]

    def spread(v):
        rows = jnp.broadcast_to(v[:, None, :], (v.shape[0], nodes, width)).reshape(-1, width)
        return jnp.concatenate([rows, jnp.zeros((ROWS - 3 * nodes, width), jnp.float32)], axis=0)

    geo = jnp.stack([spread(half_scale), spread(jnp.cos(angle)), spread(jnp.sin(angle))])
    local_index = (links[0:3] - first_elem + HALO + elem_total) % elem_total
    local_index = jnp.clip(local_index, 0, width - 1)
    across_face = links[3:6]
    lift_t, deriv_t, surf = stage_tables(deriv_r, deriv_s, lift, ORDER)
    vmem = pl.BlockSpec(memory_space=pltpu.VMEM)
    adj_new = pl.pallas_call(
        stage_kernel,
        out_shape=jax.ShapeDtypeStruct((fields, basis_count, elem_count), jnp.float32),
        in_specs=[pl.BlockSpec(memory_space=pl.ANY)] + [vmem] * 9,
        out_specs=vmem,
        scratch_shapes=[
            pltpu.VMEM((fields, basis_count, width), jnp.float32),
            pltpu.VMEM((fields, basis_count, width), jnp.float32),
            pltpu.VMEM((fields, basis_count, width), jnp.float32),
            pltpu.VMEM((2 * fields * ROWS, width + 2 * LANES), jnp.bfloat16),
            pltpu.SemaphoreType.DMA(()),
        ],
        compiler_params=pltpu.CompilerParams(vmem_limit_bytes=56 * 1024 * 1024),
    )(adjoint, left, right, met, geo, local_index, across_face, lift_t, deriv_t, surf)
    adj_rows = jnp.transpose(adj_new, (2, 0, 1)).reshape(elem_count, fields * basis_count)

    rows_here = intersection_elem.shape[0]
    block_here = rows_here // BLOCK
    field_rows = fields * basis_count
    bounds = group_bounds(rows_here, REACH)
    old_count = E_OLD_DEV
    old_iota = jnp.arange(old_count, dtype=jnp.int32)[:, None]

    def labelled_rows(first, count):
        blocks = count // BLOCK
        elems = lax.slice_in_dim(intersection_elem, first, first + count)
        picked = jnp.take(adj_rows, elems, axis=0, mode="clip")
        picked = picked.reshape(blocks, BLOCK, fields, basis_count)
        kinds = lax.slice_in_dim(block_type, first // BLOCK, first // BLOCK + blocks)
        chosen = jnp.take(remap_table, kinds, axis=0)
        mapped = jnp.einsum("brci,bij->brcj", picked, chosen, precision=lax.Precision.HIGH)
        weight = lax.slice_in_dim(intersection_weight, first, first + count)
        mapped = mapped * weight.reshape(blocks, BLOCK, 1, 1)
        mapped = mapped.reshape(count, field_rows)
        labels = lax.slice_in_dim(intersection_old, first, first + count)
        return jnp.concatenate([mapped, labels.astype(jnp.float32)[:, None]], axis=1)

    def scatter(rows):
        labels = rows[:, field_rows].astype(jnp.int32)
        return split_dot(old_iota == labels[None, :], rows[:, :field_rows])

    home_start = [start_row for offset, start_row, _ in bounds if offset == 0][0]
    home_size = [size for offset, _, size in bounds if offset == 0][0]
    home_end = home_start + home_size
    before = labelled_rows(0, home_start)
    after = labelled_rows(home_end, rows_here - home_end)
    moved = []
    for offset, start_row, group_size in bounds:
        if offset < 0:
            moved.append(shifted(before[start_row : start_row + group_size], offset))
        elif offset > 0:
            moved.append(shifted(after[start_row - home_end : start_row - home_end + group_size], offset))
    home = labelled_rows(home_start, home_size)
    old_sums = scatter(home) + scatter(jnp.concatenate(moved, axis=0))
    return (adj_new, old_sums.T.reshape(fields, basis_count, old_count))


def solution(mesh):
    in_specs = (
        P(None, None, AXES),
        P(),
        P(),
        P(),
        P(None, AXES),
        P(None, AXES),
        P(None, AXES),
        P(None, AXES),
        P(None, AXES),
        P(),
        P(AXES),
        P(AXES),
        P(AXES),
        P(AXES),
    )
    out_specs = (P(None, None, AXES), P(None, None, AXES))
    return jax.shard_map(body, mesh=mesh, in_specs=in_specs, out_specs=out_specs, check_vma=False)
```

```python
import jax
import jax.numpy as jnp
import numpy as np
from jax import lax
from jax.experimental import pallas as pl
from jax.experimental.pallas import tpu as pltpu
from jax.sharding import PartitionSpec as P

ORDER = 10
REACH = 4
BLOCK = 128
RIM = 32
HALO = 128
E_OLD_DEV = 2048

gravity = 2.0
depth = 0.5
wave_speed = 1.0
time_step = 0.04
highest = lax.Precision.HIGHEST
AXES = ("gx", "gy")


def extended(cells, width, axis=0):
    count = lax.axis_size(AXES)
    size = cells.shape[axis]
    head = lax.slice_in_dim(cells, 0, width, axis=axis)
    tail = lax.slice_in_dim(cells, size - width, size, axis=axis)
    return jnp.concatenate(
        [
            lax.ppermute(tail, AXES, [(i, (i + 1) % count) for i in range(count)]),
            cells,
            lax.ppermute(head, AXES, [((i + 1) % count, i) for i in range(count)]),
        ],
        axis=axis,
    )


def shifted(shard, by):
    length = lax.axis_size(AXES)
    return lax.ppermute(shard, AXES, [(i, (i + by) % length) for i in range(length)])


def face_table(degree):
    basis_count = (degree + 1) * (degree + 2) // 2

    def node_place(column, level):
        return level * (degree + 1) - level * (level - 1) // 2 + column

    ones_table = np.zeros((3, degree + 1, basis_count), np.float32)
    for level in range(degree + 1):
        ones_table[0, level, node_place(level, 0)] = 1.0
        ones_table[1, level, node_place(degree - level, level)] = 1.0
        ones_table[2, level, node_place(0, degree - level)] = 1.0
    return ones_table


def surface_matrix(degree):
    ones_table = face_table(degree)
    faces, nodes, basis_count = ones_table.shape
    own = ones_table.reshape(faces * nodes, basis_count)
    other = -ones_table[:, ::-1, :].reshape(faces * nodes, basis_count)
    return jnp.asarray(np.concatenate([own, other], axis=0))


def group_bounds(q_rows, reach):
    cap_far = q_rows // 32
    cap_near = q_rows // 8
    cap_home = q_rows - 2 * cap_near - 2 * (reach - 1) * cap_far
    bounds = []
    start = 0
    for offset in range(-reach, reach + 1):
        if offset == 0:
            group_size = cap_home
        elif abs(offset) == 1:
            group_size = cap_near
        else:
            group_size = cap_far
        bounds.append((offset, start, group_size))
        start = start + group_size
    return bounds


def split_dot(onehot, values):
    return jnp.dot(onehot.astype(jnp.float32), values, precision=lax.Precision.HIGH)


def split_dot_halves(onehot, values):
    high = lax.reduce_precision(values, exponent_bits=8, mantissa_bits=7)
    both = jnp.concatenate([high, values - high], axis=1).astype(jnp.bfloat16)
    out = jnp.dot(onehot.astype(jnp.bfloat16), both, preferred_element_type=jnp.float32)
    cols = values.shape[1]
    return out[:, :cols] + out[:, cols:]


LANES = 128
ROWS = 48


def stage_tables(deriv_r, deriv_s, lift, degree):
    basis_count = deriv_r.shape[0]
    nodes = degree + 1
    lift_t = jnp.zeros((ROWS, basis_count), jnp.float32).at[: 3 * nodes].set(lift.T)
    deriv_t = jnp.zeros((144, basis_count), jnp.float32)
    deriv_t = deriv_t.at[:basis_count].set(deriv_r.T).at[72 : 72 + basis_count].set(deriv_s.T)
    ones_table = face_table(degree)
    faces = ones_table.shape[0]
    own = np.zeros((basis_count, ROWS), np.float32)
    own[:, : faces * nodes] = ones_table.reshape(faces * nodes, basis_count).T
    parts = [own, own]
    for g in range(faces):
        other = np.zeros((basis_count, ROWS), np.float32)
        for f in range(faces):
            other[:, f * nodes : (f + 1) * nodes] = -ones_table[g, ::-1, :].T
        parts.extend([other, other])
    surf = jnp.asarray(np.concatenate(parts, axis=1), jnp.bfloat16)
    return lift_t, deriv_t, surf


def stage_kernel(
    hbm_ref, left_ref, right_ref, met_ref, geo_ref, li_ref, nf_ref, lt_ref, dt_ref, sm_ref,
    out_ref, x_ref, s2_ref, s1_ref, z_ref, sem,
):
    elem_count = hbm_ref.shape[2]
    copy = pltpu.make_async_copy(hbm_ref, x_ref.at[:, :, HALO : HALO + elem_count], sem)
    copy.start()
    copy.wait()
    x_ref[:, :, 0:HALO] = left_ref[...]
    x_ref[:, :, HALO + elem_count : 2 * HALO + elem_count] = right_ref[...]
    fields, basis_count, width = x_ref.shape
    blocks = width // LANES
    split_rows = 2 * fields * ROWS
    z_ref[:, 0:LANES] = jnp.zeros((split_rows, LANES), jnp.bfloat16)
    z_ref[:, width + LANES : width + 2 * LANES] = jnp.zeros((split_rows, LANES), jnp.bfloat16)
    rowface = lax.broadcasted_iota(jnp.int32, (ROWS, LANES), 0) // (ORDER + 1)
    window = lax.broadcasted_iota(jnp.int32, (3 * LANES, LANES), 0)

    def dot(a, b):
        return jnp.dot(a, b, precision=highest, preferred_element_type=jnp.float32)

    def dot16(a, b):
        return jnp.dot(a, b, preferred_element_type=jnp.float32)

    def run(src_ref, kind):
        def traces(b, carry):
            off = pl.multiple_of(b * LANES, LANES)
            lifted = [dot(lt_ref[...], src_ref[c, :, pl.ds(off, LANES)]) for c in range(fields)]
            half_scale = geo_ref[0, :, pl.ds(off, LANES)]
            normal_x = geo_ref[1, :, pl.ds(off, LANES)]
            normal_y = geo_ref[2, :, pl.ds(off, LANES)]
            height, along_x, along_y = lifted
            face_height = half_scale * (
                gravity * (normal_x * along_x + normal_y * along_y) - wave_speed * height
            )
            face_along_x = half_scale * (depth * normal_x * height - wave_speed * along_x)
            face_along_y = half_scale * (depth * normal_y * height - wave_speed * along_y)
            dst = pl.multiple_of(off + LANES, LANES)
            for c, value in enumerate((face_height, face_along_x, face_along_y)):
                high = value.astype(jnp.bfloat16)
                low = (value - high.astype(jnp.float32)).astype(jnp.bfloat16)
                z_ref[c * ROWS : (c + 1) * ROWS, pl.ds(dst, LANES)] = high
                z_ref[(fields + c) * ROWS : (fields + c + 1) * ROWS, pl.ds(dst, LANES)] = low
            return carry

        lax.fori_loop(0, blocks, traces, 0)

        def update(b, carry):
            off = pl.multiple_of(b * LANES, LANES)
            near = z_ref[:, pl.ds(off, 3 * LANES)]
            gathered = []
            for g in range(3):
                spot = li_ref[g : g + 1, pl.ds(off, LANES)] - (off - LANES)
                onehot = (window == spot).astype(jnp.bfloat16)
                across = nf_ref[g : g + 1, pl.ds(off, LANES)]
                picked = dot16(near, onehot)
                gathered.append((picked, rowface == across))
            m = met_ref[:, pl.ds(off, LANES)]
            m0, m1, m2, m3 = (m[k : k + 1] for k in range(4))
            cur = [src_ref[c, :, pl.ds(off, LANES)] for c in range(fields)]
            rs = [dot(dt_ref[...], cur[c]) for c in range(fields)]
            along_r = [v[0:basis_count] for v in rs]
            along_s = [v[72 : 72 + basis_count] for v in rs]
            volume = [
                -gravity * (m0 * along_r[1] + m1 * along_s[1] + m2 * along_r[2] + m3 * along_s[2]),
                -depth * (m0 * along_r[0] + m1 * along_s[0]),
                -depth * (m2 * along_r[0] + m3 * along_s[0]),
            ]
            here = pl.ds(pl.multiple_of(off + LANES, LANES), LANES)
            for c in range(fields):
                hi_rows = slice(c * ROWS, (c + 1) * ROWS)
                lo_rows = slice((fields + c) * ROWS, (fields + c + 1) * ROWS)
                pieces = [z_ref[hi_rows, here], z_ref[lo_rows, here]]
                for picked, mask in gathered:
                    for rows in (hi_rows, lo_rows):
                        pieces.append(jnp.where(mask, picked[rows], 0.0).astype(jnp.bfloat16))
                surface = dot16(sm_ref[...], jnp.concatenate(pieces, axis=0))
                new = cur[c] + time_step * (volume[c] + surface)
                if kind == 0:
                    s2_ref[c, :, pl.ds(off, LANES)] = 2.0 / 3.0 * new
                elif kind == 1:
                    s1_ref[c, :, pl.ds(off, LANES)] = 0.25 * new
                else:
                    dst = pl.multiple_of(off - LANES, LANES)
                    out_ref[c, :, pl.ds(dst, LANES)] = (
                        x_ref[c, :, pl.ds(off, LANES)] / 3.0 + 0.75 * s2_ref[c, :, pl.ds(off, LANES)] + new
                    )
            return carry

        if kind == 2:
            lax.fori_loop(1, blocks - 1, update, 0)
        else:
            lax.fori_loop(0, blocks, update, 0)

    run(x_ref, 0)
    run(s2_ref, 1)
    run(s1_ref, 2)


def body(
    adjoint,
    deriv_r,
    deriv_s,
    lift,
    metric,
    face_scale,
    face_angle,
    neighbours,
    neighbour_face,
    remap_table,
    intersection_elem,
    intersection_old,
    intersection_weight,
    block_type,
):
    fields, basis_count, elem_count = adjoint.shape
    nodes = ORDER + 1
    devices = lax.axis_size(AXES)
    elem_total = elem_count * devices
    first_elem = lax.axis_index(AXES) * elem_count
    width = elem_count + 2 * HALO

    count = lax.axis_size(AXES)
    field_rows = fields * basis_count
    side = jnp.concatenate(
        [metric, face_scale, face_angle, neighbours.astype(jnp.float32), neighbour_face.astype(jnp.float32)],
        axis=0,
    )
    tail = adjoint[:, :, elem_count - HALO :].reshape(field_rows, HALO)
    tail = jnp.concatenate([tail, side[:, elem_count - HALO :]], axis=0)
    head = adjoint[:, :, :HALO].reshape(field_rows, HALO)
    head = jnp.concatenate([head, side[:, :HALO]], axis=0)
    from_left = lax.ppermute(tail, AXES, [(i, (i + 1) % count) for i in range(count)])
    from_right = lax.ppermute(head, AXES, [((i + 1) % count, i) for i in range(count)])
    left = from_left[:field_rows].reshape(fields, basis_count, HALO)
    right = from_right[:field_rows].reshape(fields, basis_count, HALO)
    side = jnp.concatenate([from_left[field_rows:], side, from_right[field_rows:]], axis=1)
    params = side[0:10]
    links = side[10:16].astype(jnp.int32)
    met = params[0:4]
    half_scale = 0.5 * params[4:7]
    angle = params[7:10]

    def spread(v):
        rows = jnp.broadcast_to(v[:, None, :], (v.shape[0], nodes, width)).reshape(-1, width)
        return jnp.concatenate([rows, jnp.zeros((ROWS - 3 * nodes, width), jnp.float32)], axis=0)

    geo = jnp.stack([spread(half_scale), spread(jnp.cos(angle)), spread(jnp.sin(angle))])
    local_index = (links[0:3] - first_elem + HALO + elem_total) % elem_total
    local_index = jnp.clip(local_index, 0, width - 1)
    across_face = links[3:6]
    lift_t, deriv_t, surf = stage_tables(deriv_r, deriv_s, lift, ORDER)
    vmem = pl.BlockSpec(memory_space=pltpu.VMEM)
    adj_new = pl.pallas_call(
        stage_kernel,
        out_shape=jax.ShapeDtypeStruct((fields, basis_count, elem_count), jnp.float32),
        in_specs=[pl.BlockSpec(memory_space=pl.ANY)] + [vmem] * 9,
        out_specs=vmem,
        scratch_shapes=[
            pltpu.VMEM((fields, basis_count, width), jnp.float32),
            pltpu.VMEM((fields, basis_count, width), jnp.float32),
            pltpu.VMEM((fields, basis_count, width), jnp.float32),
            pltpu.VMEM((2 * fields * ROWS, width + 2 * LANES), jnp.bfloat16),
            pltpu.SemaphoreType.DMA(()),
        ],
        compiler_params=pltpu.CompilerParams(vmem_limit_bytes=56 * 1024 * 1024),
    )(adjoint, left, right, met, geo, local_index, across_face, lift_t, deriv_t, surf)
    adj_rows = jnp.transpose(adj_new, (2, 0, 1)).reshape(elem_count, fields * basis_count)

    rows_here = intersection_elem.shape[0]
    block_here = rows_here // BLOCK
    field_rows = fields * basis_count
    bounds = group_bounds(rows_here, REACH)
    old_count = E_OLD_DEV
    old_iota = jnp.arange(old_count, dtype=jnp.int32)[:, None]

    def labelled_rows(first, count):
        blocks = count // BLOCK
        elems = lax.slice_in_dim(intersection_elem, first, first + count)
        picked = jnp.take(adj_rows, elems, axis=0, mode="clip")
        picked = picked.reshape(blocks, BLOCK, fields, basis_count)
        kinds = lax.slice_in_dim(block_type, first // BLOCK, first // BLOCK + blocks)
        chosen = jnp.take(remap_table, kinds, axis=0)
        mapped = jnp.einsum("brci,bij->brcj", picked, chosen, precision=lax.Precision.HIGH)
        weight = lax.slice_in_dim(intersection_weight, first, first + count)
        mapped = mapped * weight.reshape(blocks, BLOCK, 1, 1)
        mapped = mapped.reshape(count, field_rows)
        labels = lax.slice_in_dim(intersection_old, first, first + count)
        return jnp.concatenate([mapped, labels.astype(jnp.float32)[:, None]], axis=1)

    def scatter(rows, how):
        labels = rows[:, field_rows].astype(jnp.int32)
        return how(old_iota == labels[None, :], rows[:, :field_rows])

    home_start = [start_row for offset, start_row, _ in bounds if offset == 0][0]
    home_size = [size for offset, _, size in bounds if offset == 0][0]
    home_end = home_start + home_size
    before = labelled_rows(0, home_start)
    after = labelled_rows(home_end, rows_here - home_end)
    moved = []
    for offset, start_row, group_size in bounds:
        if offset < 0:
            moved.append(shifted(before[start_row : start_row + group_size], offset))
        elif offset > 0:
            moved.append(shifted(after[start_row - home_end : start_row - home_end + group_size], offset))
    home = labelled_rows(home_start, home_size)
    old_sums = scatter(home, split_dot) + scatter(jnp.concatenate(moved, axis=0), split_dot_halves)
    return (adj_new, old_sums.T.reshape(fields, basis_count, old_count))


def solution(mesh):
    in_specs = (
        P(None, None, AXES),
        P(),
        P(),
        P(),
        P(None, AXES),
        P(None, AXES),
        P(None, AXES),
        P(None, AXES),
        P(None, AXES),
        P(),
        P(AXES),
        P(AXES),
        P(AXES),
        P(AXES),
    )
    out_specs = (P(None, None, AXES), P(None, None, AXES))
    return jax.shard_map(body, mesh=mesh, in_specs=in_specs, out_specs=out_specs, check_vma=False)
```

```python
import jax
import jax.numpy as jnp
import numpy as np
from jax import lax
from jax.experimental import pallas as pl
from jax.experimental.pallas import tpu as pltpu
from jax.sharding import PartitionSpec as P

ORDER = 10
REACH = 4
BLOCK = 128
RIM = 32
HALO = 128
E_OLD_DEV = 2048

gravity = 2.0
depth = 0.5
wave_speed = 1.0
time_step = 0.04
highest = lax.Precision.HIGHEST
AXES = ("gx", "gy")


def extended(cells, width, axis=0):
    count = lax.axis_size(AXES)
    size = cells.shape[axis]
    head = lax.slice_in_dim(cells, 0, width, axis=axis)
    tail = lax.slice_in_dim(cells, size - width, size, axis=axis)
    return jnp.concatenate(
        [
            lax.ppermute(tail, AXES, [(i, (i + 1) % count) for i in range(count)]),
            cells,
            lax.ppermute(head, AXES, [((i + 1) % count, i) for i in range(count)]),
        ],
        axis=axis,
    )


def shifted(shard, by):
    length = lax.axis_size(AXES)
    return lax.ppermute(shard, AXES, [(i, (i + by) % length) for i in range(length)])


def face_table(degree):
    basis_count = (degree + 1) * (degree + 2) // 2

    def node_place(column, level):
        return level * (degree + 1) - level * (level - 1) // 2 + column

    ones_table = np.zeros((3, degree + 1, basis_count), np.float32)
    for level in range(degree + 1):
        ones_table[0, level, node_place(level, 0)] = 1.0
        ones_table[1, level, node_place(degree - level, level)] = 1.0
        ones_table[2, level, node_place(0, degree - level)] = 1.0
    return ones_table


def surface_matrix(degree):
    ones_table = face_table(degree)
    faces, nodes, basis_count = ones_table.shape
    own = ones_table.reshape(faces * nodes, basis_count)
    other = -ones_table[:, ::-1, :].reshape(faces * nodes, basis_count)
    return jnp.asarray(np.concatenate([own, other], axis=0))


def group_bounds(q_rows, reach):
    cap_far = q_rows // 32
    cap_near = q_rows // 8
    cap_home = q_rows - 2 * cap_near - 2 * (reach - 1) * cap_far
    bounds = []
    start = 0
    for offset in range(-reach, reach + 1):
        if offset == 0:
            group_size = cap_home
        elif abs(offset) == 1:
            group_size = cap_near
        else:
            group_size = cap_far
        bounds.append((offset, start, group_size))
        start = start + group_size
    return bounds


def split_dot(onehot, values):
    return jnp.dot(onehot.astype(jnp.float32), values, precision=lax.Precision.HIGH)


def split_dot_halves(onehot, values):
    high = lax.reduce_precision(values, exponent_bits=8, mantissa_bits=7)
    both = jnp.concatenate([high, values - high], axis=1).astype(jnp.bfloat16)
    out = jnp.dot(onehot.astype(jnp.bfloat16), both, preferred_element_type=jnp.float32)
    cols = values.shape[1]
    return out[:, :cols] + out[:, cols:]


LANES = 128
ROWS = 48


def stage_tables(deriv_r, deriv_s, lift, degree):
    basis_count = deriv_r.shape[0]
    nodes = degree + 1
    lift_t = jnp.zeros((ROWS, basis_count), jnp.float32).at[: 3 * nodes].set(lift.T)
    deriv_t = jnp.zeros((144, basis_count), jnp.float32)
    deriv_t = deriv_t.at[:basis_count].set(deriv_r.T).at[72 : 72 + basis_count].set(deriv_s.T)
    ones_table = face_table(degree)
    faces = ones_table.shape[0]
    own = np.zeros((basis_count, ROWS), np.float32)
    own[:, : faces * nodes] = ones_table.reshape(faces * nodes, basis_count).T
    parts = [own, own]
    for g in range(faces):
        other = np.zeros((basis_count, ROWS), np.float32)
        for f in range(faces):
            other[:, f * nodes : (f + 1) * nodes] = -ones_table[g, ::-1, :].T
        parts.extend([other, other])
    surf = jnp.asarray(np.concatenate(parts, axis=1), jnp.bfloat16)
    return lift_t, deriv_t, surf


def stage_kernel(
    hbm_ref, left_ref, right_ref, met_ref, geo_ref, li_ref, nf_ref, lt_ref, dt_ref, sm_ref,
    out_ref, x_ref, s2_ref, s1_ref, z_ref, sem,
):
    elem_count = hbm_ref.shape[2]
    copy = pltpu.make_async_copy(hbm_ref, x_ref.at[:, :, HALO : HALO + elem_count], sem)
    copy.start()
    copy.wait()
    x_ref[:, :, 0:HALO] = left_ref[...]
    x_ref[:, :, HALO + elem_count : 2 * HALO + elem_count] = right_ref[...]
    fields, basis_count, width = x_ref.shape
    blocks = width // LANES
    split_rows = 2 * fields * ROWS
    z_ref[:, 0:LANES] = jnp.zeros((split_rows, LANES), jnp.bfloat16)
    z_ref[:, width + LANES : width + 2 * LANES] = jnp.zeros((split_rows, LANES), jnp.bfloat16)
    rowface = lax.broadcasted_iota(jnp.int32, (ROWS, LANES), 0) // (ORDER + 1)
    window = lax.broadcasted_iota(jnp.int32, (3 * LANES, LANES), 0)

    def dot(a, b):
        return jnp.dot(a, b, precision=highest, preferred_element_type=jnp.float32)

    def dot16(a, b):
        return jnp.dot(a, b, preferred_element_type=jnp.float32)

    def run(src_ref, kind):
        def traces(b, carry):
            off = pl.multiple_of(b * LANES, LANES)
            lifted = [dot(lt_ref[...], src_ref[c, :, pl.ds(off, LANES)]) for c in range(fields)]
            half_scale = geo_ref[0, :, pl.ds(off, LANES)]
            normal_x = geo_ref[1, :, pl.ds(off, LANES)]
            normal_y = geo_ref[2, :, pl.ds(off, LANES)]
            height, along_x, along_y = lifted
            face_height = half_scale * (
                gravity * (normal_x * along_x + normal_y * along_y) - wave_speed * height
            )
            face_along_x = half_scale * (depth * normal_x * height - wave_speed * along_x)
            face_along_y = half_scale * (depth * normal_y * height - wave_speed * along_y)
            dst = pl.multiple_of(off + LANES, LANES)
            for c, value in enumerate((face_height, face_along_x, face_along_y)):
                high = value.astype(jnp.bfloat16)
                low = (value - high.astype(jnp.float32)).astype(jnp.bfloat16)
                z_ref[c * ROWS : (c + 1) * ROWS, pl.ds(dst, LANES)] = high
                z_ref[(fields + c) * ROWS : (fields + c + 1) * ROWS, pl.ds(dst, LANES)] = low
            return carry

        lax.fori_loop(0, blocks, traces, 0)

        def update(b, carry):
            off = pl.multiple_of(b * LANES, LANES)
            near = z_ref[:, pl.ds(off, 3 * LANES)]
            gathered = []
            for g in range(3):
                spot = li_ref[g : g + 1, pl.ds(off, LANES)] - (off - LANES)
                onehot = (window == spot).astype(jnp.bfloat16)
                across = nf_ref[g : g + 1, pl.ds(off, LANES)]
                picked = dot16(near, onehot)
                gathered.append((picked, rowface == across))
            m = met_ref[:, pl.ds(off, LANES)]
            m0, m1, m2, m3 = (m[k : k + 1] for k in range(4))
            cur = [src_ref[c, :, pl.ds(off, LANES)] for c in range(fields)]
            rs = [dot(dt_ref[...], cur[c]) for c in range(fields)]
            along_r = [v[0:basis_count] for v in rs]
            along_s = [v[72 : 72 + basis_count] for v in rs]
            volume = [
                -gravity * (m0 * along_r[1] + m1 * along_s[1] + m2 * along_r[2] + m3 * along_s[2]),
                -depth * (m0 * along_r[0] + m1 * along_s[0]),
                -depth * (m2 * along_r[0] + m3 * along_s[0]),
            ]
            here = pl.ds(pl.multiple_of(off + LANES, LANES), LANES)
            for c in range(fields):
                hi_rows = slice(c * ROWS, (c + 1) * ROWS)
                lo_rows = slice((fields + c) * ROWS, (fields + c + 1) * ROWS)
                pieces = [z_ref[hi_rows, here], z_ref[lo_rows, here]]
                for picked, mask in gathered:
                    for rows in (hi_rows, lo_rows):
                        pieces.append(jnp.where(mask, picked[rows], 0.0).astype(jnp.bfloat16))
                surface = dot16(sm_ref[...], jnp.concatenate(pieces, axis=0))
                new = cur[c] + time_step * (volume[c] + surface)
                if kind == 0:
                    s2_ref[c, :, pl.ds(off, LANES)] = 2.0 / 3.0 * new
                elif kind == 1:
                    s1_ref[c, :, pl.ds(off, LANES)] = 0.25 * new
                else:
                    dst = pl.multiple_of(off - LANES, LANES)
                    out_ref[c, :, pl.ds(dst, LANES)] = (
                        x_ref[c, :, pl.ds(off, LANES)] / 3.0 + 0.75 * s2_ref[c, :, pl.ds(off, LANES)] + new
                    )
            return carry

        if kind == 2:
            lax.fori_loop(1, blocks - 1, update, 0)
        else:
            lax.fori_loop(0, blocks, update, 0)

    run(x_ref, 0)
    run(s2_ref, 1)
    run(s1_ref, 2)


def body(
    adjoint,
    deriv_r,
    deriv_s,
    lift,
    metric,
    face_scale,
    face_angle,
    neighbours,
    neighbour_face,
    remap_table,
    intersection_elem,
    intersection_old,
    intersection_weight,
    block_type,
):
    fields, basis_count, elem_count = adjoint.shape
    nodes = ORDER + 1
    devices = lax.axis_size(AXES)
    elem_total = elem_count * devices
    first_elem = lax.axis_index(AXES) * elem_count
    width = elem_count + 2 * HALO

    count = lax.axis_size(AXES)
    field_rows = fields * basis_count
    side = jnp.concatenate(
        [metric, face_scale, face_angle, neighbours.astype(jnp.float32), neighbour_face.astype(jnp.float32)],
        axis=0,
    )
    tail = adjoint[:, :, elem_count - HALO :].reshape(field_rows, HALO)
    tail = jnp.concatenate([tail, side[:, elem_count - HALO :]], axis=0)
    head = adjoint[:, :, :HALO].reshape(field_rows, HALO)
    head = jnp.concatenate([head, side[:, :HALO]], axis=0)
    from_left = lax.ppermute(tail, AXES, [(i, (i + 1) % count) for i in range(count)])
    from_right = lax.ppermute(head, AXES, [((i + 1) % count, i) for i in range(count)])
    left = from_left[:field_rows].reshape(fields, basis_count, HALO)
    right = from_right[:field_rows].reshape(fields, basis_count, HALO)
    side = jnp.concatenate([from_left[field_rows:], side, from_right[field_rows:]], axis=1)
    params = side[0:10]
    links = side[10:16].astype(jnp.int32)
    met = params[0:4]
    half_scale = 0.5 * params[4:7]
    angle = params[7:10]

    def spread(v):
        rows = jnp.broadcast_to(v[:, None, :], (v.shape[0], nodes, width)).reshape(-1, width)
        return jnp.concatenate([rows, jnp.zeros((ROWS - 3 * nodes, width), jnp.float32)], axis=0)

    geo = jnp.stack([spread(half_scale), spread(jnp.cos(angle)), spread(jnp.sin(angle))])
    local_index = (links[0:3] - first_elem + HALO + elem_total) % elem_total
    local_index = jnp.clip(local_index, 0, width - 1)
    across_face = links[3:6]
    lift_t, deriv_t, surf = stage_tables(deriv_r, deriv_s, lift, ORDER)
    vmem = pl.BlockSpec(memory_space=pltpu.VMEM)
    adj_new = pl.pallas_call(
        stage_kernel,
        out_shape=jax.ShapeDtypeStruct((fields, basis_count, elem_count), jnp.float32),
        in_specs=[pl.BlockSpec(memory_space=pl.ANY)] + [vmem] * 9,
        out_specs=vmem,
        scratch_shapes=[
            pltpu.VMEM((fields, basis_count, width), jnp.float32),
            pltpu.VMEM((fields, basis_count, width), jnp.float32),
            pltpu.VMEM((fields, basis_count, width), jnp.float32),
            pltpu.VMEM((2 * fields * ROWS, width + 2 * LANES), jnp.bfloat16),
            pltpu.SemaphoreType.DMA(()),
        ],
        compiler_params=pltpu.CompilerParams(vmem_limit_bytes=56 * 1024 * 1024),
    )(adjoint, left, right, met, geo, local_index, across_face, lift_t, deriv_t, surf)
    adj_rows = jnp.transpose(adj_new, (2, 0, 1)).reshape(elem_count, fields * basis_count)

    rows_here = intersection_elem.shape[0]
    block_here = rows_here // BLOCK
    field_rows = fields * basis_count
    bounds = group_bounds(rows_here, REACH)
    old_count = E_OLD_DEV
    old_iota = jnp.arange(old_count, dtype=jnp.int32)[:, None]

    all_chosen = remap_table.at[block_type].get(mode="promise_in_bounds")

    def labelled_rows(first, count):
        blocks = count // BLOCK
        elems = lax.slice_in_dim(intersection_elem, first, first + count)
        picked = adj_rows.at[elems].get(mode="promise_in_bounds")
        picked = picked.reshape(blocks, BLOCK, fields, basis_count)
        chosen = lax.slice_in_dim(all_chosen, first // BLOCK, first // BLOCK + blocks)
        mapped = jnp.einsum("brci,bij->brcj", picked, chosen, precision=lax.Precision.HIGH)
        weight = lax.slice_in_dim(intersection_weight, first, first + count)
        mapped = mapped * weight.reshape(blocks, BLOCK, 1, 1)
        mapped = mapped.reshape(count, field_rows)
        labels = lax.slice_in_dim(intersection_old, first, first + count)
        return jnp.concatenate([mapped, labels.astype(jnp.float32)[:, None]], axis=1)

    def scatter(rows, how):
        labels = rows[:, field_rows].astype(jnp.int32)
        return how(old_iota == labels[None, :], rows[:, :field_rows])

    home_start = [start_row for offset, start_row, _ in bounds if offset == 0][0]
    home_size = [size for offset, _, size in bounds if offset == 0][0]
    home_end = home_start + home_size
    before = labelled_rows(0, home_start)
    after = labelled_rows(home_end, rows_here - home_end)
    moved = []
    for offset, start_row, group_size in bounds:
        if offset < 0:
            moved.append(shifted(before[start_row : start_row + group_size], offset))
        elif offset > 0:
            moved.append(shifted(after[start_row - home_end : start_row - home_end + group_size], offset))
    home = labelled_rows(home_start, home_size)
    old_sums = scatter(home, split_dot) + scatter(jnp.concatenate(moved, axis=0), split_dot_halves)
    return (adj_new, old_sums.T.reshape(fields, basis_count, old_count))


def solution(mesh):
    in_specs = (
        P(None, None, AXES),
        P(),
        P(),
        P(),
        P(None, AXES),
        P(None, AXES),
        P(None, AXES),
        P(None, AXES),
        P(None, AXES),
        P(),
        P(AXES),
        P(AXES),
        P(AXES),
        P(AXES),
    )
    out_specs = (P(None, None, AXES), P(None, None, AXES))
    return jax.shard_map(body, mesh=mesh, in_specs=in_specs, out_specs=out_specs, check_vma=False)
```

```python
import jax
import jax.numpy as jnp
import numpy as np
from jax import lax
from jax.experimental import pallas as pl
from jax.experimental.pallas import tpu as pltpu
from jax.sharding import PartitionSpec as P

ORDER = 10
REACH = 4
BLOCK = 128
RIM = 32
HALO = 128
E_OLD_DEV = 2048

gravity = 2.0
depth = 0.5
wave_speed = 1.0
time_step = 0.04
highest = lax.Precision.HIGHEST
AXES = ("gx", "gy")


def extended(cells, width, axis=0):
    count = lax.axis_size(AXES)
    size = cells.shape[axis]
    head = lax.slice_in_dim(cells, 0, width, axis=axis)
    tail = lax.slice_in_dim(cells, size - width, size, axis=axis)
    return jnp.concatenate(
        [
            lax.ppermute(tail, AXES, [(i, (i + 1) % count) for i in range(count)]),
            cells,
            lax.ppermute(head, AXES, [((i + 1) % count, i) for i in range(count)]),
        ],
        axis=axis,
    )


def shifted(shard, by):
    length = lax.axis_size(AXES)
    return lax.ppermute(shard, AXES, [(i, (i + by) % length) for i in range(length)])


def face_table(degree):
    basis_count = (degree + 1) * (degree + 2) // 2

    def node_place(column, level):
        return level * (degree + 1) - level * (level - 1) // 2 + column

    ones_table = np.zeros((3, degree + 1, basis_count), np.float32)
    for level in range(degree + 1):
        ones_table[0, level, node_place(level, 0)] = 1.0
        ones_table[1, level, node_place(degree - level, level)] = 1.0
        ones_table[2, level, node_place(0, degree - level)] = 1.0
    return ones_table


def surface_matrix(degree):
    ones_table = face_table(degree)
    faces, nodes, basis_count = ones_table.shape
    own = ones_table.reshape(faces * nodes, basis_count)
    other = -ones_table[:, ::-1, :].reshape(faces * nodes, basis_count)
    return jnp.asarray(np.concatenate([own, other], axis=0))


def group_bounds(q_rows, reach):
    cap_far = q_rows // 32
    cap_near = q_rows // 8
    cap_home = q_rows - 2 * cap_near - 2 * (reach - 1) * cap_far
    bounds = []
    start = 0
    for offset in range(-reach, reach + 1):
        if offset == 0:
            group_size = cap_home
        elif abs(offset) == 1:
            group_size = cap_near
        else:
            group_size = cap_far
        bounds.append((offset, start, group_size))
        start = start + group_size
    return bounds


def split_dot(onehot, values):
    return jnp.dot(onehot.astype(jnp.float32), values, precision=lax.Precision.HIGH)


def split_dot_halves(onehot, values):
    high = lax.reduce_precision(values, exponent_bits=8, mantissa_bits=7)
    both = jnp.concatenate([high, values - high], axis=1).astype(jnp.bfloat16)
    out = jnp.dot(onehot.astype(jnp.bfloat16), both, preferred_element_type=jnp.float32)
    cols = values.shape[1]
    return out[:, :cols] + out[:, cols:]


LANES = 128
ROWS = 48


def stage_tables(deriv_r, deriv_s, lift, degree):
    basis_count = deriv_r.shape[0]
    nodes = degree + 1
    lift_t = jnp.zeros((ROWS, basis_count), jnp.float32).at[: 3 * nodes].set(lift.T)
    deriv_t = jnp.zeros((144, basis_count), jnp.float32)
    deriv_t = deriv_t.at[:basis_count].set(deriv_r.T).at[72 : 72 + basis_count].set(deriv_s.T)
    ones_table = face_table(degree)
    faces = ones_table.shape[0]
    own = np.zeros((basis_count, ROWS), np.float32)
    own[:, : faces * nodes] = ones_table.reshape(faces * nodes, basis_count).T
    parts = [own, own]
    for g in range(faces):
        other = np.zeros((basis_count, ROWS), np.float32)
        for f in range(faces):
            other[:, f * nodes : (f + 1) * nodes] = -ones_table[g, ::-1, :].T
        parts.extend([other, other])
    surf = jnp.asarray(np.concatenate(parts, axis=1), jnp.bfloat16)
    return lift_t, deriv_t, surf


def stage_kernel(
    hbm_ref, left_ref, right_ref, met_ref, geo_ref, li_ref, nf_ref, lt_ref, dt_ref, sm_ref,
    out_ref, x_ref, s2_ref, s1_ref, z_ref, sem,
):
    elem_count = hbm_ref.shape[2]
    copy = pltpu.make_async_copy(hbm_ref, x_ref.at[:, :, HALO : HALO + elem_count], sem)
    copy.start()
    copy.wait()
    x_ref[:, :, 0:HALO] = left_ref[...]
    x_ref[:, :, HALO + elem_count : 2 * HALO + elem_count] = right_ref[...]
    fields, basis_count, width = x_ref.shape
    blocks = width // LANES
    split_rows = 2 * fields * ROWS
    z_ref[:, 0:LANES] = jnp.zeros((split_rows, LANES), jnp.bfloat16)
    z_ref[:, width + LANES : width + 2 * LANES] = jnp.zeros((split_rows, LANES), jnp.bfloat16)
    rowface = lax.broadcasted_iota(jnp.int32, (ROWS, LANES), 0) // (ORDER + 1)
    window = lax.broadcasted_iota(jnp.int32, (3 * LANES, LANES), 0)

    def dot(a, b):
        return jnp.dot(a, b, precision=lax.Precision.HIGH, preferred_element_type=jnp.float32)

    def dot16(a, b):
        return jnp.dot(a, b, preferred_element_type=jnp.float32)

    def run(src_ref, kind):
        def traces(b, carry):
            off = pl.multiple_of(b * LANES, LANES)
            lifted = [dot(lt_ref[...], src_ref[c, :, pl.ds(off, LANES)]) for c in range(fields)]
            half_scale = geo_ref[0, :, pl.ds(off, LANES)]
            normal_x = geo_ref[1, :, pl.ds(off, LANES)]
            normal_y = geo_ref[2, :, pl.ds(off, LANES)]
            height, along_x, along_y = lifted
            face_height = half_scale * (
                gravity * (normal_x * along_x + normal_y * along_y) - wave_speed * height
            )
            face_along_x = half_scale * (depth * normal_x * height - wave_speed * along_x)
            face_along_y = half_scale * (depth * normal_y * height - wave_speed * along_y)
            dst = pl.multiple_of(off + LANES, LANES)
            for c, value in enumerate((face_height, face_along_x, face_along_y)):
                high = value.astype(jnp.bfloat16)
                low = (value - high.astype(jnp.float32)).astype(jnp.bfloat16)
                z_ref[c * ROWS : (c + 1) * ROWS, pl.ds(dst, LANES)] = high
                z_ref[(fields + c) * ROWS : (fields + c + 1) * ROWS, pl.ds(dst, LANES)] = low
            return carry

        lax.fori_loop(0, blocks, traces, 0)

        def update(b, carry):
            off = pl.multiple_of(b * LANES, LANES)
            near = z_ref[:, pl.ds(off, 3 * LANES)]
            gathered = []
            for g in range(3):
                spot = li_ref[g : g + 1, pl.ds(off, LANES)] - (off - LANES)
                onehot = (window == spot).astype(jnp.bfloat16)
                across = nf_ref[g : g + 1, pl.ds(off, LANES)]
                picked = dot16(near, onehot)
                gathered.append((picked, rowface == across))
            m = met_ref[:, pl.ds(off, LANES)]
            m0, m1, m2, m3 = (m[k : k + 1] for k in range(4))
            cur = [src_ref[c, :, pl.ds(off, LANES)] for c in range(fields)]
            rs = [dot(dt_ref[...], cur[c]) for c in range(fields)]
            along_r = [v[0:basis_count] for v in rs]
            along_s = [v[72 : 72 + basis_count] for v in rs]
            volume = [
                -gravity * (m0 * along_r[1] + m1 * along_s[1] + m2 * along_r[2] + m3 * along_s[2]),
                -depth * (m0 * along_r[0] + m1 * along_s[0]),
                -depth * (m2 * along_r[0] + m3 * along_s[0]),
            ]
            here = pl.ds(pl.multiple_of(off + LANES, LANES), LANES)
            for c in range(fields):
                hi_rows = slice(c * ROWS, (c + 1) * ROWS)
                lo_rows = slice((fields + c) * ROWS, (fields + c + 1) * ROWS)
                pieces = [z_ref[hi_rows, here], z_ref[lo_rows, here]]
                for picked, mask in gathered:
                    for rows in (hi_rows, lo_rows):
                        pieces.append(jnp.where(mask, picked[rows], 0.0).astype(jnp.bfloat16))
                surface = dot16(sm_ref[...], jnp.concatenate(pieces, axis=0))
                new = cur[c] + time_step * (volume[c] + surface)
                if kind == 0:
                    s2_ref[c, :, pl.ds(off, LANES)] = 2.0 / 3.0 * new
                elif kind == 1:
                    s1_ref[c, :, pl.ds(off, LANES)] = 0.25 * new
                else:
                    dst = pl.multiple_of(off - LANES, LANES)
                    out_ref[c, :, pl.ds(dst, LANES)] = (
                        x_ref[c, :, pl.ds(off, LANES)] / 3.0 + 0.75 * s2_ref[c, :, pl.ds(off, LANES)] + new
                    )
            return carry

        if kind == 2:
            lax.fori_loop(1, blocks - 1, update, 0)
        else:
            lax.fori_loop(0, blocks, update, 0)

    run(x_ref, 0)
    run(s2_ref, 1)
    run(s1_ref, 2)


def body(
    adjoint,
    deriv_r,
    deriv_s,
    lift,
    metric,
    face_scale,
    face_angle,
    neighbours,
    neighbour_face,
    remap_table,
    intersection_elem,
    intersection_old,
    intersection_weight,
    block_type,
):
    fields, basis_count, elem_count = adjoint.shape
    nodes = ORDER + 1
    devices = lax.axis_size(AXES)
    elem_total = elem_count * devices
    first_elem = lax.axis_index(AXES) * elem_count
    width = elem_count + 2 * HALO

    count = lax.axis_size(AXES)
    field_rows = fields * basis_count
    side = jnp.concatenate(
        [metric, face_scale, face_angle, neighbours.astype(jnp.float32), neighbour_face.astype(jnp.float32)],
        axis=0,
    )
    tail = adjoint[:, :, elem_count - HALO :].reshape(field_rows, HALO)
    tail = jnp.concatenate([tail, side[:, elem_count - HALO :]], axis=0)
    head = adjoint[:, :, :HALO].reshape(field_rows, HALO)
    head = jnp.concatenate([head, side[:, :HALO]], axis=0)
    from_left = lax.ppermute(tail, AXES, [(i, (i + 1) % count) for i in range(count)])
    from_right = lax.ppermute(head, AXES, [((i + 1) % count, i) for i in range(count)])
    left = from_left[:field_rows].reshape(fields, basis_count, HALO)
    right = from_right[:field_rows].reshape(fields, basis_count, HALO)
    side = jnp.concatenate([from_left[field_rows:], side, from_right[field_rows:]], axis=1)
    params = side[0:10]
    links = side[10:16].astype(jnp.int32)
    met = params[0:4]
    half_scale = 0.5 * params[4:7]
    angle = params[7:10]

    def spread(v):
        rows = jnp.broadcast_to(v[:, None, :], (v.shape[0], nodes, width)).reshape(-1, width)
        return jnp.concatenate([rows, jnp.zeros((ROWS - 3 * nodes, width), jnp.float32)], axis=0)

    geo = jnp.stack([spread(half_scale), spread(jnp.cos(angle)), spread(jnp.sin(angle))])
    local_index = (links[0:3] - first_elem + HALO + elem_total) % elem_total
    local_index = jnp.clip(local_index, 0, width - 1)
    across_face = links[3:6]
    lift_t, deriv_t, surf = stage_tables(deriv_r, deriv_s, lift, ORDER)
    vmem = pl.BlockSpec(memory_space=pltpu.VMEM)
    adj_new = pl.pallas_call(
        stage_kernel,
        out_shape=jax.ShapeDtypeStruct((fields, basis_count, elem_count), jnp.float32),
        in_specs=[pl.BlockSpec(memory_space=pl.ANY)] + [vmem] * 9,
        out_specs=vmem,
        scratch_shapes=[
            pltpu.VMEM((fields, basis_count, width), jnp.float32),
            pltpu.VMEM((fields, basis_count, width), jnp.float32),
            pltpu.VMEM((fields, basis_count, width), jnp.float32),
            pltpu.VMEM((2 * fields * ROWS, width + 2 * LANES), jnp.bfloat16),
            pltpu.SemaphoreType.DMA(()),
        ],
        compiler_params=pltpu.CompilerParams(vmem_limit_bytes=56 * 1024 * 1024),
    )(adjoint, left, right, met, geo, local_index, across_face, lift_t, deriv_t, surf)
    adj_rows = jnp.transpose(adj_new, (2, 0, 1)).reshape(elem_count, fields * basis_count)

    rows_here = intersection_elem.shape[0]
    block_here = rows_here // BLOCK
    field_rows = fields * basis_count
    bounds = group_bounds(rows_here, REACH)
    old_count = E_OLD_DEV
    old_iota = jnp.arange(old_count, dtype=jnp.int32)[:, None]

    def labelled_rows(first, count):
        blocks = count // BLOCK
        elems = lax.slice_in_dim(intersection_elem, first, first + count)
        picked = jnp.take(adj_rows, elems, axis=0, mode="clip")
        picked = picked.reshape(blocks, BLOCK, fields, basis_count)
        kinds = lax.slice_in_dim(block_type, first // BLOCK, first // BLOCK + blocks)
        chosen = jnp.take(remap_table, kinds, axis=0)
        mapped = jnp.einsum("brci,bij->brcj", picked, chosen, precision=lax.Precision.HIGH)
        weight = lax.slice_in_dim(intersection_weight, first, first + count)
        mapped = mapped * weight.reshape(blocks, BLOCK, 1, 1)
        mapped = mapped.reshape(count, field_rows)
        labels = lax.slice_in_dim(intersection_old, first, first + count)
        return jnp.concatenate([mapped, labels.astype(jnp.float32)[:, None]], axis=1)

    def scatter(rows, how):
        labels = rows[:, field_rows].astype(jnp.int32)
        return how(old_iota == labels[None, :], rows[:, :field_rows])

    home_start = [start_row for offset, start_row, _ in bounds if offset == 0][0]
    home_size = [size for offset, _, size in bounds if offset == 0][0]
    home_end = home_start + home_size
    before = labelled_rows(0, home_start)
    after = labelled_rows(home_end, rows_here - home_end)
    moved = []
    for offset, start_row, group_size in bounds:
        if offset < 0:
            moved.append(shifted(before[start_row : start_row + group_size], offset))
        elif offset > 0:
            moved.append(shifted(after[start_row - home_end : start_row - home_end + group_size], offset))
    home = labelled_rows(home_start, home_size)
    old_sums = scatter(home, split_dot) + scatter(jnp.concatenate(moved, axis=0), split_dot_halves)
    return (adj_new, old_sums.T.reshape(fields, basis_count, old_count))


def solution(mesh):
    in_specs = (
        P(None, None, AXES),
        P(),
        P(),
        P(),
        P(None, AXES),
        P(None, AXES),
        P(None, AXES),
        P(None, AXES),
        P(None, AXES),
        P(),
        P(AXES),
        P(AXES),
        P(AXES),
        P(AXES),
    )
    out_specs = (P(None, None, AXES), P(None, None, AXES))
    return jax.shard_map(body, mesh=mesh, in_specs=in_specs, out_specs=out_specs, check_vma=False)
```

```python
import jax
import jax.numpy as jnp
import numpy as np
from jax import lax
from jax.experimental import pallas as pl
from jax.experimental.pallas import tpu as pltpu
from jax.sharding import PartitionSpec as P

ORDER = 10
REACH = 4
BLOCK = 128
RIM = 32
HALO = 128
E_OLD_DEV = 2048

gravity = 2.0
depth = 0.5
wave_speed = 1.0
time_step = 0.04
highest = lax.Precision.HIGHEST
AXES = ("gx", "gy")


def extended(cells, width, axis=0):
    count = lax.axis_size(AXES)
    size = cells.shape[axis]
    head = lax.slice_in_dim(cells, 0, width, axis=axis)
    tail = lax.slice_in_dim(cells, size - width, size, axis=axis)
    return jnp.concatenate(
        [
            lax.ppermute(tail, AXES, [(i, (i + 1) % count) for i in range(count)]),
            cells,
            lax.ppermute(head, AXES, [((i + 1) % count, i) for i in range(count)]),
        ],
        axis=axis,
    )


def shifted(shard, by):
    length = lax.axis_size(AXES)
    return lax.ppermute(shard, AXES, [(i, (i + by) % length) for i in range(length)])


def face_table(degree):
    basis_count = (degree + 1) * (degree + 2) // 2

    def node_place(column, level):
        return level * (degree + 1) - level * (level - 1) // 2 + column

    ones_table = np.zeros((3, degree + 1, basis_count), np.float32)
    for level in range(degree + 1):
        ones_table[0, level, node_place(level, 0)] = 1.0
        ones_table[1, level, node_place(degree - level, level)] = 1.0
        ones_table[2, level, node_place(0, degree - level)] = 1.0
    return ones_table


def surface_matrix(degree):
    ones_table = face_table(degree)
    faces, nodes, basis_count = ones_table.shape
    own = ones_table.reshape(faces * nodes, basis_count)
    other = -ones_table[:, ::-1, :].reshape(faces * nodes, basis_count)
    return jnp.asarray(np.concatenate([own, other], axis=0))


def group_bounds(q_rows, reach):
    cap_far = q_rows // 32
    cap_near = q_rows // 8
    cap_home = q_rows - 2 * cap_near - 2 * (reach - 1) * cap_far
    bounds = []
    start = 0
    for offset in range(-reach, reach + 1):
        if offset == 0:
            group_size = cap_home
        elif abs(offset) == 1:
            group_size = cap_near
        else:
            group_size = cap_far
        bounds.append((offset, start, group_size))
        start = start + group_size
    return bounds


def split_dot(onehot, values):
    return jnp.dot(onehot.astype(jnp.float32), values, precision=lax.Precision.HIGH)


def split_dot_halves(onehot, values):
    high = lax.reduce_precision(values, exponent_bits=8, mantissa_bits=7)
    both = jnp.concatenate([high, values - high], axis=1).astype(jnp.bfloat16)
    out = jnp.dot(onehot.astype(jnp.bfloat16), both, preferred_element_type=jnp.float32)
    cols = values.shape[1]
    return out[:, :cols] + out[:, cols:]


LANES = 128
ROWS = 48


def stage_tables(deriv_r, deriv_s, lift, degree):
    basis_count = deriv_r.shape[0]
    nodes = degree + 1
    lift_t = jnp.zeros((ROWS, basis_count), jnp.float32).at[: 3 * nodes].set(lift.T)
    deriv_t = jnp.zeros((144, basis_count), jnp.float32)
    deriv_t = deriv_t.at[:basis_count].set(deriv_r.T).at[72 : 72 + basis_count].set(deriv_s.T)
    ones_table = face_table(degree)
    faces = ones_table.shape[0]
    own = np.zeros((basis_count, ROWS), np.float32)
    own[:, : faces * nodes] = ones_table.reshape(faces * nodes, basis_count).T
    parts = [own, own]
    for g in range(faces):
        other = np.zeros((basis_count, ROWS), np.float32)
        for f in range(faces):
            other[:, f * nodes : (f + 1) * nodes] = -ones_table[g, ::-1, :].T
        parts.extend([other, other])
    surf = jnp.asarray(np.concatenate(parts, axis=1), jnp.bfloat16)
    return lift_t, deriv_t, surf


def stage_kernel(
    hbm_ref, left_ref, right_ref, met_ref, geo_ref, li_ref, nf_ref, lt_ref, dt_ref, sm_ref,
    out_ref, x_ref, s2_ref, s1_ref, z_ref, oh_ref, sem,
):
    elem_count = hbm_ref.shape[2]
    copy = pltpu.make_async_copy(hbm_ref, x_ref.at[:, :, HALO : HALO + elem_count], sem)
    copy.start()
    copy.wait()
    x_ref[:, :, 0:HALO] = left_ref[...]
    x_ref[:, :, HALO + elem_count : 2 * HALO + elem_count] = right_ref[...]
    fields, basis_count, width = x_ref.shape
    blocks = width // LANES
    split_rows = 2 * fields * ROWS
    z_ref[:, 0:LANES] = jnp.zeros((split_rows, LANES), jnp.bfloat16)
    z_ref[:, width + LANES : width + 2 * LANES] = jnp.zeros((split_rows, LANES), jnp.bfloat16)
    rowface = lax.broadcasted_iota(jnp.int32, (ROWS, LANES), 0) // (ORDER + 1)
    window = lax.broadcasted_iota(jnp.int32, (3 * LANES, LANES), 0)

    def build(b, carry):
        off = pl.multiple_of(b * LANES, LANES)
        for g in range(3):
            spot = li_ref[g : g + 1, pl.ds(off, LANES)] - (off - LANES)
            oh_ref[g * blocks + b] = (window == spot).astype(jnp.bfloat16)
        return carry

    lax.fori_loop(0, blocks, build, 0)

    def dot(a, b):
        return jnp.dot(a, b, precision=lax.Precision.HIGH, preferred_element_type=jnp.float32)

    def dot16(a, b):
        return jnp.dot(a, b, preferred_element_type=jnp.float32)

    def run(src_ref, kind):
        def traces(b, carry):
            off = pl.multiple_of(b * LANES, LANES)
            lifted = [dot(lt_ref[...], src_ref[c, :, pl.ds(off, LANES)]) for c in range(fields)]
            half_scale = geo_ref[0, :, pl.ds(off, LANES)]
            normal_x = geo_ref[1, :, pl.ds(off, LANES)]
            normal_y = geo_ref[2, :, pl.ds(off, LANES)]
            height, along_x, along_y = lifted
            face_height = half_scale * (
                gravity * (normal_x * along_x + normal_y * along_y) - wave_speed * height
            )
            face_along_x = half_scale * (depth * normal_x * height - wave_speed * along_x)
            face_along_y = half_scale * (depth * normal_y * height - wave_speed * along_y)
            dst = pl.multiple_of(off + LANES, LANES)
            for c, value in enumerate((face_height, face_along_x, face_along_y)):
                high = value.astype(jnp.bfloat16)
                low = (value - high.astype(jnp.float32)).astype(jnp.bfloat16)
                z_ref[c * ROWS : (c + 1) * ROWS, pl.ds(dst, LANES)] = high
                z_ref[(fields + c) * ROWS : (fields + c + 1) * ROWS, pl.ds(dst, LANES)] = low
            return carry

        lax.fori_loop(0, blocks, traces, 0)

        def update(b, carry):
            off = pl.multiple_of(b * LANES, LANES)
            near = z_ref[:, pl.ds(off, 3 * LANES)]
            gathered = []
            for g in range(3):
                onehot = oh_ref[g * blocks + b]
                across = nf_ref[g : g + 1, pl.ds(off, LANES)]
                picked = dot16(near, onehot)
                gathered.append((picked, rowface == across))
            m = met_ref[:, pl.ds(off, LANES)]
            m0, m1, m2, m3 = (m[k : k + 1] for k in range(4))
            cur = [src_ref[c, :, pl.ds(off, LANES)] for c in range(fields)]
            rs = [dot(dt_ref[...], cur[c]) for c in range(fields)]
            along_r = [v[0:basis_count] for v in rs]
            along_s = [v[72 : 72 + basis_count] for v in rs]
            volume = [
                -gravity * (m0 * along_r[1] + m1 * along_s[1] + m2 * along_r[2] + m3 * along_s[2]),
                -depth * (m0 * along_r[0] + m1 * along_s[0]),
                -depth * (m2 * along_r[0] + m3 * along_s[0]),
            ]
            here = pl.ds(pl.multiple_of(off + LANES, LANES), LANES)
            for c in range(fields):
                hi_rows = slice(c * ROWS, (c + 1) * ROWS)
                lo_rows = slice((fields + c) * ROWS, (fields + c + 1) * ROWS)
                pieces = [z_ref[hi_rows, here], z_ref[lo_rows, here]]
                for picked, mask in gathered:
                    for rows in (hi_rows, lo_rows):
                        pieces.append(jnp.where(mask, picked[rows], 0.0).astype(jnp.bfloat16))
                surface = dot16(sm_ref[...], jnp.concatenate(pieces, axis=0))
                new = cur[c] + time_step * (volume[c] + surface)
                if kind == 0:
                    s2_ref[c, :, pl.ds(off, LANES)] = 2.0 / 3.0 * new
                elif kind == 1:
                    s1_ref[c, :, pl.ds(off, LANES)] = 0.25 * new
                else:
                    dst = pl.multiple_of(off - LANES, LANES)
                    out_ref[c, :, pl.ds(dst, LANES)] = (
                        x_ref[c, :, pl.ds(off, LANES)] / 3.0 + 0.75 * s2_ref[c, :, pl.ds(off, LANES)] + new
                    )
            return carry

        if kind == 2:
            lax.fori_loop(1, blocks - 1, update, 0)
        else:
            lax.fori_loop(0, blocks, update, 0)

    run(x_ref, 0)
    run(s2_ref, 1)
    run(s1_ref, 2)


def body(
    adjoint,
    deriv_r,
    deriv_s,
    lift,
    metric,
    face_scale,
    face_angle,
    neighbours,
    neighbour_face,
    remap_table,
    intersection_elem,
    intersection_old,
    intersection_weight,
    block_type,
):
    fields, basis_count, elem_count = adjoint.shape
    nodes = ORDER + 1
    devices = lax.axis_size(AXES)
    elem_total = elem_count * devices
    first_elem = lax.axis_index(AXES) * elem_count
    width = elem_count + 2 * HALO

    count = lax.axis_size(AXES)
    field_rows = fields * basis_count
    side = jnp.concatenate(
        [metric, face_scale, face_angle, neighbours.astype(jnp.float32), neighbour_face.astype(jnp.float32)],
        axis=0,
    )
    tail = adjoint[:, :, elem_count - HALO :].reshape(field_rows, HALO)
    tail = jnp.concatenate([tail, side[:, elem_count - HALO :]], axis=0)
    head = adjoint[:, :, :HALO].reshape(field_rows, HALO)
    head = jnp.concatenate([head, side[:, :HALO]], axis=0)
    from_left = lax.ppermute(tail, AXES, [(i, (i + 1) % count) for i in range(count)])
    from_right = lax.ppermute(head, AXES, [((i + 1) % count, i) for i in range(count)])
    left = from_left[:field_rows].reshape(fields, basis_count, HALO)
    right = from_right[:field_rows].reshape(fields, basis_count, HALO)
    side = jnp.concatenate([from_left[field_rows:], side, from_right[field_rows:]], axis=1)
    params = side[0:10]
    links = side[10:16].astype(jnp.int32)
    met = params[0:4]
    half_scale = 0.5 * params[4:7]
    angle = params[7:10]

    def spread(v):
        rows = jnp.broadcast_to(v[:, None, :], (v.shape[0], nodes, width)).reshape(-1, width)
        return jnp.concatenate([rows, jnp.zeros((ROWS - 3 * nodes, width), jnp.float32)], axis=0)

    geo = jnp.stack([spread(half_scale), spread(jnp.cos(angle)), spread(jnp.sin(angle))])
    local_index = (links[0:3] - first_elem + HALO + elem_total) % elem_total
    local_index = jnp.clip(local_index, 0, width - 1)
    across_face = links[3:6]
    lift_t, deriv_t, surf = stage_tables(deriv_r, deriv_s, lift, ORDER)
    vmem = pl.BlockSpec(memory_space=pltpu.VMEM)
    adj_new = pl.pallas_call(
        stage_kernel,
        out_shape=jax.ShapeDtypeStruct((fields, basis_count, elem_count), jnp.float32),
        in_specs=[pl.BlockSpec(memory_space=pl.ANY)] + [vmem] * 9,
        out_specs=vmem,
        scratch_shapes=[
            pltpu.VMEM((fields, basis_count, width), jnp.float32),
            pltpu.VMEM((fields, basis_count, width), jnp.float32),
            pltpu.VMEM((fields, basis_count, width), jnp.float32),
            pltpu.VMEM((2 * fields * ROWS, width + 2 * LANES), jnp.bfloat16),
            pltpu.VMEM((3 * (width // LANES), 3 * LANES, LANES), jnp.bfloat16),
            pltpu.SemaphoreType.DMA(()),
        ],
        compiler_params=pltpu.CompilerParams(vmem_limit_bytes=56 * 1024 * 1024),
    )(adjoint, left, right, met, geo, local_index, across_face, lift_t, deriv_t, surf)
    adj_rows = jnp.transpose(adj_new, (2, 0, 1)).reshape(elem_count, fields * basis_count)

    rows_here = intersection_elem.shape[0]
    block_here = rows_here // BLOCK
    field_rows = fields * basis_count
    bounds = group_bounds(rows_here, REACH)
    old_count = E_OLD_DEV
    old_iota = jnp.arange(old_count, dtype=jnp.int32)[:, None]

    def labelled_rows(first, count):
        blocks = count // BLOCK
        elems = lax.slice_in_dim(intersection_elem, first, first + count)
        picked = jnp.take(adj_rows, elems, axis=0, mode="clip")
        picked = picked.reshape(blocks, BLOCK, fields, basis_count)
        kinds = lax.slice_in_dim(block_type, first // BLOCK, first // BLOCK + blocks)
        chosen = jnp.take(remap_table, kinds, axis=0)
        mapped = jnp.einsum("brci,bij->brcj", picked, chosen, precision=lax.Precision.HIGH)
        weight = lax.slice_in_dim(intersection_weight, first, first + count)
        mapped = mapped * weight.reshape(blocks, BLOCK, 1, 1)
        mapped = mapped.reshape(count, field_rows)
        labels = lax.slice_in_dim(intersection_old, first, first + count)
        return jnp.concatenate([mapped, labels.astype(jnp.float32)[:, None]], axis=1)

    def scatter(rows, how):
        labels = rows[:, field_rows].astype(jnp.int32)
        return how(old_iota == labels[None, :], rows[:, :field_rows])

    home_start = [start_row for offset, start_row, _ in bounds if offset == 0][0]
    home_size = [size for offset, _, size in bounds if offset == 0][0]
    home_end = home_start + home_size
    before = labelled_rows(0, home_start)
    after = labelled_rows(home_end, rows_here - home_end)
    moved = []
    for offset, start_row, group_size in bounds:
        if offset < 0:
            moved.append(shifted(before[start_row : start_row + group_size], offset))
        elif offset > 0:
            moved.append(shifted(after[start_row - home_end : start_row - home_end + group_size], offset))
    home = labelled_rows(home_start, home_size)
    old_sums = scatter(home, split_dot) + scatter(jnp.concatenate(moved, axis=0), split_dot_halves)
    return (adj_new, old_sums.T.reshape(fields, basis_count, old_count))


def solution(mesh):
    in_specs = (
        P(None, None, AXES),
        P(),
        P(),
        P(),
        P(None, AXES),
        P(None, AXES),
        P(None, AXES),
        P(None, AXES),
        P(None, AXES),
        P(),
        P(AXES),
        P(AXES),
        P(AXES),
        P(AXES),
    )
    out_specs = (P(None, None, AXES), P(None, None, AXES))
    return jax.shard_map(body, mesh=mesh, in_specs=in_specs, out_specs=out_specs, check_vma=False)
```
